32 devices in a mesh: group: 2 (over y), ctx: 8 (over z, x), dp: 2 (over core).
Axes of the slice: x: 2, y: 2, z: 4, core: 2. Of those that a mesh axis runs over, the one named last changes fastest.
Arguments:
- queries: bfloat16 [4, 1024, 512], P(('group', 'dp'), 'ctx'), parts along dimension 0, may hold values from -30 to 30
- key_rows: bfloat16 [4, 1024, 512], P(('group', 'dp'), 'ctx'), parts along dimension 0, may hold values from -30 to 30
- values: bfloat16 [4, 1024, 512], P(('group', 'dp'), 'ctx'), parts along dimension 0, may hold values from -6 to 6
- cotangent: bfloat16 [4, 1024, 1024], P(('group', 'dp'), 'ctx'), parts along dimension 0, may hold values from -6 to 6
- out_proj: bfloat16 [512, 1024], replicated, may hold values from -6 to 6
- conv_kernel: float32 [31, 1024], replicated, may hold values from -1.8 to 1.8
- lengths: int32 [4], P(('group', 'dp')), parts along dimension 0, may hold values from 640 to 1024, as said below
Outputs:
- grad_query: bfloat16 [4, 1024, 512], P(('group', 'dp'), 'ctx'), parts along dimension 0
- grad_key: bfloat16 [4, 1024, 512], P(('group', 'dp'), 'ctx'), parts along dimension 0
- grad_value: bfloat16 [4, 1024, 512], P(('group', 'dp'), 'ctx'), parts along dimension 0
- grad_out_proj: bfloat16 [1024, 1024], P('group'), parts along dimension 0
- grad_kernel: float32 [62, 1024], P('group'), parts along dimension 0
The draws below stay inside these ranges and needn't reach their ends.
There are 2 independent parts, one for each index of `group`. The reference program is written for one: setup_inputs(seed, part) draws one part's arguments, and reference() takes and returns one part's arrays. A program takes and returns all parts, laid end to end along the dimension named above; an argument that names none is the same for every part. Nothing has to cross between parts.
Inputs may be any that keep to these rules, and one draw needn't show every extreme that they name: `lengths`: in every draw at least one recording is valid over all its 1024 frames.
All inputs are finite; a program needn't handle non-finite values.
Results may differ from the reference program's by a relative error of at most 0.014.
The reference program's roundings to bfloat16 on the way count: a program that leaves them out, or rounds other values in their place, can miss the bound.
Values may be sent and summed in bfloat16 or wider, within the bound.
No kernel may reach another device: no remote copies, remote signals or barrier semaphores. Data moves between devices by JAX's collectives and lax.ppermute only.
A program may use at most 64 MiB of HBM per device.

```python
import math
import jax
import jax.numpy as jnp
from jax import lax

D = 1024
HEADS = 8
HDIM = 64
KW = 31
REACH = 3
TOK_DEV = 128
STREAMS = 2
TIME = 1024
HW = 512


def paired_rows(key):
    folded = jax.random.fold_in(key, 7)
    key_query, key_keys = jax.random.split(folded, 2)
    full_shape = (STREAMS, TIME, HW)
    query_base = jax.random.normal(key_query, full_shape, jnp.float32)
    key_base = jax.random.normal(key_keys, full_shape, jnp.float32)
    key_out = key_base
    query_out = query_base
    return (jnp.clip(query_out, -30.0, 30.0), jnp.clip(key_out, -30.0, 30.0))


def draw_queries(key, part):
    return paired_rows(key)[0].astype(jnp.bfloat16)


def draw_key_rows(key, part):
    return paired_rows(key)[1].astype(jnp.bfloat16)


def draw_lengths(key, part):
    folded = jax.random.fold_in(key, 11)
    key_values, key_pick = jax.random.split(folded, 2)
    drawn = jax.random.randint(key_values, (STREAMS,), TIME - REACH * TOK_DEV, TIME + 1)
    picked = jax.random.randint(key_pick, (), 0, STREAMS)
    drawn = jnp.where(jnp.arange(STREAMS) == picked, TIME, drawn)
    return drawn.astype(jnp.int32)


def block_levels(rng, extent, cuts, low, high):
    def one(position, parts):
        steps = jax.random.uniform(jax.random.fold_in(jax.random.fold_in(rng, 6), position), (parts,), jnp.float32, low / len(cuts), high / len(cuts))
        return jnp.repeat(jnp.exp(steps), extent[position] // parts).reshape((-1,) + (1,) * (len(extent) - position - 1))

    gain = one(*cuts[0])
    for cut in cuts[1:]:
        gain = gain * one(*cut)
    return gain


def centred(key, extent, scale, most, pieces=(), kind=jnp.bfloat16):
    loudness = block_levels(key, extent, pieces, -0.22, 0.18) if pieces else 1.0
    values = jax.random.normal(key, extent, jnp.float32) * scale * loudness
    return jnp.minimum(jnp.maximum(values, -most), most).astype(kind)


def setup_inputs(seed: int = 0, part: int = 0) -> dict:
    keys = jax.random.split(jax.random.key(seed), 8)
    part_splits = jax.random.split(jax.random.fold_in(keys[7], part), 8)
    return {
        "queries": draw_queries(jax.random.fold_in(jax.random.fold_in(keys[7], part), 71), part),
        "key_rows": draw_key_rows(jax.random.fold_in(jax.random.fold_in(keys[7], part), 71), part),
        "values": centred(part_splits[2], (STREAMS, TIME, HW), 1.0, 6.0, ((0, 2), (1, 8))),
        "cotangent": centred(part_splits[3], (STREAMS, TIME, D), 1.0, 6.0, ((0, 2), (1, 8))),
        "out_proj": centred(keys[4], (HW, D), 1.0, 6.0),
        "conv_kernel": centred(keys[5], (KW, D), 0.3, 1.8, (), jnp.float32),
        "lengths": draw_lengths(jax.random.fold_in(jax.random.fold_in(keys[7], part), 71), part),
    }


def reference(queries, key_rows, values, cotangent, out_proj, conv_kernel, lengths):
    halo_width = (KW - 1) // 2
    scale_factor = 1.0 / math.sqrt(HDIM)
    span_blocks = 2 * REACH + 1
    pad_rows = REACH * TOK_DEV
    block_count = TIME // TOK_DEV
    relative = jnp.arange(span_blocks * TOK_DEV, dtype=jnp.int32)
    block_ids = jnp.arange(block_count, dtype=jnp.int32)

    def one_stream(query_rec, key_rec, value_rec, cot_rec, length_here):
        key_pad = jnp.pad(key_rec.astype(jnp.float32), ((pad_rows, pad_rows), (0, 0)))
        value_pad = jnp.pad(value_rec.astype(jnp.float32), ((pad_rows, pad_rows), (0, 0)))

        def window(block):
            start_row = (block * TOK_DEV).astype(jnp.int32)
            query_b = lax.dynamic_slice_in_dim(query_rec, start_row, TOK_DEV, 0).astype(jnp.float32).reshape(TOK_DEV, HEADS, HDIM)
            key_b = lax.dynamic_slice_in_dim(key_pad, start_row, span_blocks * TOK_DEV, 0).reshape(span_blocks * TOK_DEV, HEADS, HDIM)
            value_b = lax.dynamic_slice_in_dim(value_pad, start_row, span_blocks * TOK_DEV, 0).reshape(span_blocks * TOK_DEV, HEADS, HDIM)
            key_frames = (block - REACH) * TOK_DEV + relative
            valid_keys = (key_frames >= 0) & (key_frames < length_here)
            scores = jnp.einsum('qhd,khd->hqk', query_b, key_b) * scale_factor
            scores = jnp.where(valid_keys[None, None, :], scores, -jnp.inf)
            row_max = lax.optimization_barrier(jnp.max(scores, axis=2, keepdims=True))
            row_total = lax.optimization_barrier(jnp.sum(jnp.exp(scores - row_max), axis=2, keepdims=True))
            log_total = row_max + jnp.log(row_total)
            weights = jnp.exp(scores - log_total).astype(jnp.bfloat16).astype(jnp.float32)
            return (query_b, key_b, value_b, weights)

        def forward_block(block):
            query_b, key_b, value_b, weights = window(block)
            return jnp.einsum('hqk,khd->qhd', weights, value_b).reshape(TOK_DEV, HW).astype(jnp.bfloat16)
        attended = lax.map(forward_block, block_ids).reshape(TIME, HW)
        frames = jnp.arange(TIME, dtype=jnp.int32)
        validity = (frames < length_here).astype(jnp.float32)
        hidden = jnp.dot(attended, out_proj, preferred_element_type=jnp.float32)
        masked = (hidden * validity[:, None]).astype(jnp.bfloat16)
        padded_m = jnp.pad(masked.astype(jnp.float32), ((halo_width, halo_width), (0, 0)))
        conv_out = jnp.zeros((TIME, D), jnp.float32)
        for tap_index in range(KW):
            conv_out = conv_out + conv_kernel[tap_index] * padded_m[tap_index:tap_index + TIME]
        sigmoid_c = jax.nn.sigmoid(conv_out)
        grad_conv = (cot_rec.astype(jnp.float32) * (sigmoid_c + conv_out * sigmoid_c * (1.0 - sigmoid_c))).astype(jnp.bfloat16)
        grad_wide = grad_conv.astype(jnp.float32)
        padded_g = jnp.pad(grad_wide, ((halo_width, halo_width), (0, 0)))
        grad_masked = jnp.zeros((TIME, D), jnp.float32)
        kernel_terms = []
        for tap_index in range(KW):
            start_row = 2 * halo_width - tap_index
            grad_masked = grad_masked + conv_kernel[tap_index] * padded_g[start_row:start_row + TIME]
            kernel_terms.append(lax.optimization_barrier(jnp.sum(padded_m[tap_index:tap_index + TIME] * grad_wide, axis=0)))
        kernel_term = jnp.stack(kernel_terms, axis=0)
        grad_hidden = (cot_rec.astype(jnp.float32) + validity[:, None] * grad_masked).astype(jnp.bfloat16)
        proj_term = jnp.dot(attended.T, grad_hidden, preferred_element_type=jnp.float32)
        grad_attended = jnp.dot(grad_hidden, out_proj.T, preferred_element_type=jnp.float32).astype(jnp.bfloat16)

        def backward_block(carry, block):
            start_row = (block * TOK_DEV).astype(jnp.int32)
            query_b, key_b, value_b, weights = window(block)
            grad_heads = lax.dynamic_slice_in_dim(grad_attended, start_row, TOK_DEV, 0).astype(jnp.float32).reshape(TOK_DEV, HEADS, HDIM)
            attended_heads = lax.dynamic_slice_in_dim(attended, start_row, TOK_DEV, 0).astype(jnp.float32).reshape(TOK_DEV, HEADS, HDIM)
            delta_rows = lax.optimization_barrier(jnp.sum(grad_heads * attended_heads, axis=2))
            grad_weights = jnp.einsum('qhd,khd->hqk', grad_heads, value_b)
            logits_wide = (weights * (grad_weights - delta_rows.T[:, :, None])).astype(jnp.bfloat16).astype(jnp.float32)
            grad_query = (jnp.einsum('hqk,khd->qhd', logits_wide, key_b) * scale_factor).reshape(TOK_DEV, HW).astype(jnp.bfloat16)
            key_term = (jnp.einsum('hqk,qhd->khd', logits_wide, query_b) * scale_factor).reshape(span_blocks * TOK_DEV, HW)
            value_term = jnp.einsum('hqk,qhd->khd', weights, grad_heads).reshape(span_blocks * TOK_DEV, HW)
            key_acc = lax.dynamic_update_slice_in_dim(carry[0], lax.dynamic_slice_in_dim(carry[0], start_row, span_blocks * TOK_DEV, 0) + key_term, start_row, 0)
            value_acc = lax.dynamic_update_slice_in_dim(carry[1], lax.dynamic_slice_in_dim(carry[1], start_row, span_blocks * TOK_DEV, 0) + value_term, start_row, 0)
            return ((key_acc, value_acc), grad_query)
        zero_acc = jnp.zeros((TIME + 2 * pad_rows, HW), jnp.float32)
        accs, grad_query = lax.scan(backward_block, (zero_acc, zero_acc), block_ids)
        grad_key = accs[0][pad_rows:pad_rows + TIME].astype(jnp.bfloat16)
        grad_value = accs[1][pad_rows:pad_rows + TIME].astype(jnp.bfloat16)
        return (grad_query.reshape(TIME, HW), grad_key, grad_value, proj_term, kernel_term)
    proj_total = jnp.zeros((HW, D), jnp.float32)
    kernel_total = jnp.zeros((KW, D), jnp.float32)
    query_list, key_list, value_list = ([], [], [])
    for stream in range(STREAMS):
        outs = one_stream(queries[stream], key_rows[stream], values[stream], cotangent[stream], lengths[stream])
        query_list.append(outs[0])
        key_list.append(outs[1])
        value_list.append(outs[2])
        proj_total = proj_total + outs[3]
        kernel_total = kernel_total + outs[4]
    return (jnp.stack(query_list, 0), jnp.stack(key_list, 0), jnp.stack(value_list, 0), proj_total.astype(jnp.bfloat16), kernel_total)
```

```python
import math

import jax
import jax.numpy as jnp
from jax import lax
from jax.sharding import PartitionSpec as P

HEADS = 8
HDIM = 64
KW = 31
REACH = 3


def passed_along(block, axis, distance):
    devices = range(lax.axis_size(axis))
    route = [(i - distance, i) for i in devices if i - distance in devices]
    return lax.ppermute(block, axis, route)


def padded(cells, sides, width):
    for axis, dim in sides:
        count = lax.axis_size(axis)
        ends = count - 1
        head = lax.slice_in_dim(cells, 0, width, axis=dim)
        tail = lax.slice_in_dim(cells, cells.shape[dim] - width, cells.shape[dim], axis=dim)
        cells = jnp.concatenate(
            [
                lax.ppermute(tail, axis, [(i, (i + 1) % count) for i in range(ends)]),
                cells,
                lax.ppermute(head, axis, [((i + 1) % count, i) for i in range(ends)]),
            ],
            axis=dim,
        )
    return cells


def collect(piece_own, shifter):
    from_below = [shifter(piece_own, distance) for distance in range(REACH, 0, -1)]
    from_above = [shifter(piece_own, -distance) for distance in range(1, REACH + 1)]
    return jnp.stack(from_below + [piece_own] + from_above, axis=0)


def give_back(partials, shifter):
    total = partials[REACH]
    for offset in range(2 * REACH + 1):
        if offset != REACH:
            total = total + shifter(partials[offset], offset - REACH)
    return total


def on_device(queries, key_rows, values, cotangent, out_proj, conv_kernel, lengths):
    tokens = queries.shape[1]
    width_heads = queries.shape[2]
    channels = out_proj.shape[1]
    span_blocks = 2 * REACH + 1
    scale_factor = 1.0 / math.sqrt(HDIM)
    halo_width = (KW - 1) // 2
    block_index = lax.axis_index("ctx")
    length_here = lengths[0]
    query_here = queries[0]
    key_here = key_rows[0]
    value_here = values[0]
    cot_here = cotangent[0]
    frames = block_index * tokens + jnp.arange(tokens, dtype=jnp.int32)
    valid_rows = frames < length_here
    key_frames = (block_index - REACH) * tokens + jnp.arange(span_blocks * tokens, dtype=jnp.int32)
    valid_keys = (key_frames >= 0) & (key_frames < length_here)

    def kv_shift(piece_rows, offset_by):
        return passed_along(piece_rows, "ctx", offset_by)

    gathered = collect(jnp.stack([key_here, value_here], axis=0), kv_shift)
    key_all = gathered[:, 0].reshape(span_blocks * tokens, HEADS, HDIM)
    value_all = gathered[:, 1].reshape(span_blocks * tokens, HEADS, HDIM)
    query_heads = query_here.reshape(tokens, HEADS, HDIM)
    scores = (
        jnp.einsum("qhd,khd->hqk", query_heads, key_all, preferred_element_type=jnp.float32)
        * scale_factor
    )
    scores = jnp.where(valid_keys[None, None, :], scores, -jnp.inf)
    row_max = jnp.max(scores, axis=2, keepdims=True)
    row_total = jnp.sum(jnp.exp(scores - row_max), axis=2, keepdims=True)
    log_total = row_max + jnp.log(row_total)
    weights = jnp.exp(scores - log_total).astype(jnp.bfloat16)
    attended = jnp.einsum("hqk,khd->qhd", weights, value_all, preferred_element_type=jnp.float32)
    attended = attended.reshape(tokens, width_heads).astype(jnp.bfloat16)
    hidden = jnp.dot(attended, out_proj, preferred_element_type=jnp.float32)
    masked = jnp.where(valid_rows[:, None], hidden, 0.0).astype(jnp.bfloat16)

    def pad_time(field_rows):
        return padded(field_rows, (("ctx", 0),), halo_width)

    padded_m = pad_time(masked)
    conv_out = jnp.zeros((tokens, channels), jnp.float32)
    for tap_index in range(KW):
        conv_out = conv_out + conv_kernel[tap_index] * padded_m[tap_index : tap_index + tokens]
    sigmoid_c = jax.nn.sigmoid(conv_out)
    grad_conv = (
        cot_here.astype(jnp.float32) * (sigmoid_c + conv_out * sigmoid_c * (1.0 - sigmoid_c))
    ).astype(jnp.bfloat16)
    padded_g = pad_time(grad_conv)
    grad_wide = grad_conv.astype(jnp.float32)
    grad_masked = jnp.zeros((tokens, channels), jnp.float32)
    kernel_terms = []
    for tap_index in range(KW):
        start_row = 2 * halo_width - tap_index
        grad_masked = (
            grad_masked + conv_kernel[tap_index] * padded_g[start_row : start_row + tokens]
        )
        kernel_terms.append(
            jnp.sum(
                padded_m[tap_index : tap_index + tokens].astype(jnp.float32) * grad_wide, axis=0
            )
        )
    kernel_local = jnp.stack(kernel_terms, axis=0)
    grad_hidden = (
        cot_here.astype(jnp.float32) + jnp.where(valid_rows[:, None], grad_masked, 0.0)
    ).astype(jnp.bfloat16)
    proj_local = lax.dot_general(
        attended, grad_hidden, (((0,), (0,)), ((), ())), preferred_element_type=jnp.float32
    )
    proj_part = lax.psum_scatter(proj_local, ("ctx", "dp"), scatter_dimension=0, tiled=True)
    proj_sum = lax.all_gather(proj_part.astype(jnp.bfloat16), ("ctx", "dp"), axis=0, tiled=True)
    kernel_sum = lax.psum(kernel_local, ("ctx", "dp"))
    grad_attended = lax.dot_general(
        grad_hidden, out_proj, (((1,), (1,)), ((), ())), preferred_element_type=jnp.float32
    ).astype(jnp.bfloat16)
    grad_heads = grad_attended.reshape(tokens, HEADS, HDIM)
    attended_heads = attended.reshape(tokens, HEADS, HDIM)
    delta_rows = jnp.sum(
        grad_heads.astype(jnp.float32) * attended_heads.astype(jnp.float32), axis=2
    )
    grad_weights = jnp.einsum(
        "qhd,khd->hqk", grad_heads, value_all, preferred_element_type=jnp.float32
    )
    grad_logits = (weights.astype(jnp.float32) * (grad_weights - delta_rows.T[:, :, None])).astype(
        jnp.bfloat16
    )
    grad_query = (
        jnp.einsum("hqk,khd->qhd", grad_logits, key_all, preferred_element_type=jnp.float32)
        * scale_factor
    )
    grad_query = grad_query.reshape(tokens, width_heads).astype(jnp.bfloat16)
    grad_key_all = (
        jnp.einsum("hqk,qhd->khd", grad_logits, query_heads, preferred_element_type=jnp.float32)
        * scale_factor
    )
    grad_value_all = jnp.einsum(
        "hqk,qhd->khd", weights, grad_heads, preferred_element_type=jnp.float32
    )
    placed = jnp.stack(
        [
            grad_key_all.reshape(span_blocks, tokens, width_heads),
            grad_value_all.reshape(span_blocks, tokens, width_heads),
        ],
        axis=1,
    )

    def grad_shift(piece_rows, offset_by):
        return passed_along(piece_rows, "ctx", offset_by)

    own_grads = give_back(placed, grad_shift)
    grad_key = own_grads[0].astype(jnp.bfloat16)
    grad_value = own_grads[1].astype(jnp.bfloat16)
    return (
        grad_query[None],
        grad_key[None],
        grad_value[None],
        proj_sum,
        kernel_sum,
    )


def solution(mesh):
    return jax.shard_map(
        on_device,
        mesh=mesh,
        in_specs=(
            P(("group", "dp"), "ctx", None),
            P(("group", "dp"), "ctx", None),
            P(("group", "dp"), "ctx", None),
            P(("group", "dp"), "ctx", None),
            P(),
            P(),
            P(("group", "dp")),
        ),
        out_specs=(
            P(("group", "dp"), "ctx", None),
            P(("group", "dp"), "ctx", None),
            P(("group", "dp"), "ctx", None),
            P("group", None),
            P("group", None),
        ),
        check_vma=False,
    )
```

```python
import math

import jax
import jax.numpy as jnp
from jax import lax
from jax.sharding import PartitionSpec as P

HEADS = 8
HDIM = 64
KW = 31
REACH = 3


def passed_along(block, axis, distance):
    devices = range(lax.axis_size(axis))
    route = [(i - distance, i) for i in devices if i - distance in devices]
    return lax.ppermute(block, axis, route)


def padded(cells, sides, width):
    for axis, dim in sides:
        count = lax.axis_size(axis)
        ends = count - 1
        head = lax.slice_in_dim(cells, 0, width, axis=dim)
        tail = lax.slice_in_dim(cells, cells.shape[dim] - width, cells.shape[dim], axis=dim)
        cells = jnp.concatenate(
            [
                lax.ppermute(tail, axis, [(i, (i + 1) % count) for i in range(ends)]),
                cells,
                lax.ppermute(head, axis, [((i + 1) % count, i) for i in range(ends)]),
            ],
            axis=dim,
        )
    return cells


def collect(piece_own, shifter):
    from_below = [shifter(piece_own, distance) for distance in range(REACH, 0, -1)]
    from_above = [shifter(piece_own, -distance) for distance in range(1, REACH + 1)]
    return jnp.stack(from_below + [piece_own] + from_above, axis=0)


def give_back(partials, shifter):
    total = partials[REACH]
    for offset in range(2 * REACH + 1):
        if offset != REACH:
            total = total + shifter(partials[offset], offset - REACH)
    return total


def on_device(queries, key_rows, values, cotangent, out_proj, conv_kernel, lengths):
    tokens = queries.shape[1]
    width_heads = queries.shape[2]
    channels = out_proj.shape[1]
    span_blocks = 2 * REACH + 1
    scale_factor = 1.0 / math.sqrt(HDIM)
    halo_width = (KW - 1) // 2
    block_index = lax.axis_index("ctx")
    length_here = lengths[0]
    query_here = queries[0]
    key_here = key_rows[0]
    value_here = values[0]
    cot_here = cotangent[0]
    frames = block_index * tokens + jnp.arange(tokens, dtype=jnp.int32)
    valid_rows = frames < length_here
    key_frames = (block_index - REACH) * tokens + jnp.arange(span_blocks * tokens, dtype=jnp.int32)
    valid_keys = (key_frames >= 0) & (key_frames < length_here)

    def kv_shift(piece_rows, offset_by):
        return passed_along(piece_rows, "ctx", offset_by)

    gathered = collect(jnp.stack([key_here, value_here], axis=0), kv_shift)
    key_all = gathered[:, 0].reshape(span_blocks * tokens, HEADS, HDIM)
    value_all = gathered[:, 1].reshape(span_blocks * tokens, HEADS, HDIM)
    query_heads = query_here.reshape(tokens, HEADS, HDIM)
    scores = (
        jnp.einsum("qhd,khd->hqk", query_heads, key_all, preferred_element_type=jnp.float32)
        * scale_factor
    )
    scores = jnp.where(valid_keys[None, None, :], scores, -jnp.inf)
    row_max = jnp.max(scores, axis=2, keepdims=True)
    row_total = jnp.sum(jnp.exp(scores - row_max), axis=2, keepdims=True)
    log_total = row_max + jnp.log(row_total)
    weights = jnp.exp(scores - log_total).astype(jnp.bfloat16)
    attended = jnp.einsum("hqk,khd->qhd", weights, value_all, preferred_element_type=jnp.float32)
    attended = attended.reshape(tokens, width_heads).astype(jnp.bfloat16)
    hidden = jnp.dot(attended, out_proj, preferred_element_type=jnp.float32)
    masked = jnp.where(valid_rows[:, None], hidden, 0.0).astype(jnp.bfloat16)

    def pad_time(field_rows):
        return padded(field_rows, (("ctx", 0),), halo_width)

    padded_m = pad_time(masked)
    conv_out = jnp.zeros((tokens, channels), jnp.float32)
    for tap_index in range(KW):
        conv_out = conv_out + conv_kernel[tap_index] * padded_m[tap_index : tap_index + tokens]
    sigmoid_c = jax.nn.sigmoid(conv_out)
    grad_conv = (
        cot_here.astype(jnp.float32) * (sigmoid_c + conv_out * sigmoid_c * (1.0 - sigmoid_c))
    ).astype(jnp.bfloat16)
    padded_g = pad_time(grad_conv)
    grad_wide = grad_conv.astype(jnp.float32)
    grad_masked = jnp.zeros((tokens, channels), jnp.float32)
    kernel_terms = []
    for tap_index in range(KW):
        start_row = 2 * halo_width - tap_index
        grad_masked = (
            grad_masked + conv_kernel[tap_index] * padded_g[start_row : start_row + tokens]
        )
        kernel_terms.append(
            jnp.sum(
                padded_m[tap_index : tap_index + tokens].astype(jnp.float32) * grad_wide, axis=0
            )
        )
    kernel_local = jnp.stack(kernel_terms, axis=0)
    grad_hidden = (
        cot_here.astype(jnp.float32) + jnp.where(valid_rows[:, None], grad_masked, 0.0)
    ).astype(jnp.bfloat16)
    proj_local = lax.dot_general(
        attended, grad_hidden, (((0,), (0,)), ((), ())), preferred_element_type=jnp.float32
    )
    members = lax.axis_size("ctx") * lax.axis_size("dp")
    proj_rows = proj_local.shape[0] // members
    kernel_rows = -(-KW // members)
    kernel_padded = jnp.pad(kernel_local, ((0, kernel_rows * members - KW), (0, 0)))
    stacked = jnp.concatenate(
        [
            proj_local.reshape(members, proj_rows, channels),
            kernel_padded.reshape(members, kernel_rows, channels),
        ],
        axis=1,
    )
    summed = lax.psum_scatter(stacked, ("ctx", "dp"), scatter_dimension=0, tiled=False)
    grad_attended = lax.dot_general(
        grad_hidden, out_proj, (((1,), (1,)), ((), ())), preferred_element_type=jnp.float32
    ).astype(jnp.bfloat16)
    grad_heads = grad_attended.reshape(tokens, HEADS, HDIM)
    attended_heads = attended.reshape(tokens, HEADS, HDIM)
    delta_rows = jnp.sum(
        grad_heads.astype(jnp.float32) * attended_heads.astype(jnp.float32), axis=2
    )
    grad_weights = jnp.einsum(
        "qhd,khd->hqk", grad_heads, value_all, preferred_element_type=jnp.float32
    )
    grad_logits = (weights.astype(jnp.float32) * (grad_weights - delta_rows.T[:, :, None])).astype(
        jnp.bfloat16
    )
    grad_query = (
        jnp.einsum("hqk,khd->qhd", grad_logits, key_all, preferred_element_type=jnp.float32)
        * scale_factor
    )
    grad_query = grad_query.reshape(tokens, width_heads).astype(jnp.bfloat16)
    grad_key_all = (
        jnp.einsum("hqk,qhd->khd", grad_logits, query_heads, preferred_element_type=jnp.float32)
        * scale_factor
    )
    grad_value_all = jnp.einsum(
        "hqk,qhd->khd", weights, grad_heads, preferred_element_type=jnp.float32
    )
    placed = jnp.stack(
        [
            grad_key_all.reshape(span_blocks, tokens, width_heads),
            grad_value_all.reshape(span_blocks, tokens, width_heads),
        ],
        axis=1,
    )

    def grad_shift(piece_rows, offset_by):
        return passed_along(piece_rows, "ctx", offset_by)

    summed, placed, grad_query = lax.optimization_barrier((summed, placed, grad_query))
    kernel_part = summed[proj_rows:]
    kernel_high = lax.reduce_precision(kernel_part, exponent_bits=8, mantissa_bits=7)
    payload = jnp.concatenate(
        [
            summed[:proj_rows].astype(jnp.bfloat16),
            kernel_high.astype(jnp.bfloat16),
            (kernel_part - kernel_high).astype(jnp.bfloat16),
        ],
        axis=0,
    )
    gathered = lax.all_gather(payload, ("ctx", "dp"), axis=0, tiled=False)
    proj_sum = gathered[:, :proj_rows].reshape(members * proj_rows, channels)
    kernel_sum = (
        gathered[:, proj_rows : proj_rows + kernel_rows].astype(jnp.float32)
        + gathered[:, proj_rows + kernel_rows :].astype(jnp.float32)
    ).reshape(members * kernel_rows, channels)[:KW]
    own_grads = give_back(placed, grad_shift)
    grad_key = own_grads[0].astype(jnp.bfloat16)
    grad_value = own_grads[1].astype(jnp.bfloat16)
    return (
        grad_query[None],
        grad_key[None],
        grad_value[None],
        proj_sum,
        kernel_sum,
    )


def solution(mesh):
    return jax.shard_map(
        on_device,
        mesh=mesh,
        in_specs=(
            P(("group", "dp"), "ctx", None),
            P(("group", "dp"), "ctx", None),
            P(("group", "dp"), "ctx", None),
            P(("group", "dp"), "ctx", None),
            P(),
            P(),
            P(("group", "dp")),
        ),
        out_specs=(
            P(("group", "dp"), "ctx", None),
            P(("group", "dp"), "ctx", None),
            P(("group", "dp"), "ctx", None),
            P("group", None),
            P("group", None),
        ),
        check_vma=False,
    )
```

```python
import math

import jax
import jax.numpy as jnp
from jax import lax
from jax.sharding import PartitionSpec as P

HEADS = 8
HDIM = 64
KW = 31
REACH = 3


def passed_along(block, axis, distance):
    devices = range(lax.axis_size(axis))
    route = [(i - distance, i) for i in devices if i - distance in devices]
    return lax.ppermute(block, axis, route)


def padded(cells, sides, width):
    for axis, dim in sides:
        count = lax.axis_size(axis)
        ends = count - 1
        head = lax.slice_in_dim(cells, 0, width, axis=dim)
        tail = lax.slice_in_dim(cells, cells.shape[dim] - width, cells.shape[dim], axis=dim)
        cells = jnp.concatenate(
            [
                lax.ppermute(tail, axis, [(i, (i + 1) % count) for i in range(ends)]),
                cells,
                lax.ppermute(head, axis, [((i + 1) % count, i) for i in range(ends)]),
            ],
            axis=dim,
        )
    return cells


def collect(piece_own, shifter):
    from_below = [shifter(piece_own, distance) for distance in range(REACH, 0, -1)]
    from_above = [shifter(piece_own, -distance) for distance in range(1, REACH + 1)]
    return jnp.stack(from_below + [piece_own] + from_above, axis=0)


def give_back(partials, shifter):
    total = partials[REACH]
    for offset in range(2 * REACH + 1):
        if offset != REACH:
            moved = shifter(partials[offset].astype(jnp.bfloat16), offset - REACH)
            total = total + moved.astype(jnp.float32)
    return total


def on_device(queries, key_rows, values, cotangent, out_proj, conv_kernel, lengths):
    tokens = queries.shape[1]
    width_heads = queries.shape[2]
    channels = out_proj.shape[1]
    span_blocks = 2 * REACH + 1
    scale_factor = 1.0 / math.sqrt(HDIM)
    halo_width = (KW - 1) // 2
    block_index = lax.axis_index("ctx")
    length_here = lengths[0]
    query_here = queries[0]
    key_here = key_rows[0]
    value_here = values[0]
    cot_here = cotangent[0]
    frames = block_index * tokens + jnp.arange(tokens, dtype=jnp.int32)
    valid_rows = frames < length_here
    key_frames = (block_index - REACH) * tokens + jnp.arange(span_blocks * tokens, dtype=jnp.int32)
    valid_keys = (key_frames >= 0) & (key_frames < length_here)

    def kv_shift(piece_rows, offset_by):
        return passed_along(piece_rows, "ctx", offset_by)

    gathered = collect(jnp.stack([key_here, value_here], axis=0), kv_shift)
    key_all = gathered[:, 0].reshape(span_blocks * tokens, HEADS, HDIM)
    value_all = gathered[:, 1].reshape(span_blocks * tokens, HEADS, HDIM)
    query_heads = query_here.reshape(tokens, HEADS, HDIM)
    scores = (
        jnp.einsum("qhd,khd->hqk", query_heads, key_all, preferred_element_type=jnp.float32)
        * scale_factor
    )
    scores = jnp.where(valid_keys[None, None, :], scores, -jnp.inf)
    row_max = jnp.max(scores, axis=2, keepdims=True)
    row_total = jnp.sum(jnp.exp(scores - row_max), axis=2, keepdims=True)
    log_total = row_max + jnp.log(row_total)
    weights = jnp.exp(scores - log_total).astype(jnp.bfloat16)
    attended = jnp.einsum("hqk,khd->qhd", weights, value_all, preferred_element_type=jnp.float32)
    attended = attended.reshape(tokens, width_heads).astype(jnp.bfloat16)
    hidden = jnp.dot(attended, out_proj, preferred_element_type=jnp.float32)
    masked = jnp.where(valid_rows[:, None], hidden, 0.0).astype(jnp.bfloat16)

    def pad_time(field_rows):
        return padded(field_rows, (("ctx", 0),), halo_width)

    padded_m = pad_time(masked)
    conv_out = jnp.zeros((tokens, channels), jnp.float32)
    for tap_index in range(KW):
        conv_out = conv_out + conv_kernel[tap_index] * padded_m[tap_index : tap_index + tokens]
    sigmoid_c = jax.nn.sigmoid(conv_out)
    grad_conv = (
        cot_here.astype(jnp.float32) * (sigmoid_c + conv_out * sigmoid_c * (1.0 - sigmoid_c))
    ).astype(jnp.bfloat16)
    padded_g = pad_time(grad_conv)
    grad_wide = grad_conv.astype(jnp.float32)
    grad_masked = jnp.zeros((tokens, channels), jnp.float32)
    kernel_terms = []
    for tap_index in range(KW):
        start_row = 2 * halo_width - tap_index
        grad_masked = (
            grad_masked + conv_kernel[tap_index] * padded_g[start_row : start_row + tokens]
        )
        kernel_terms.append(
            jnp.sum(
                padded_m[tap_index : tap_index + tokens].astype(jnp.float32) * grad_wide, axis=0
            )
        )
    kernel_local = jnp.stack(kernel_terms, axis=0)
    grad_hidden = (
        cot_here.astype(jnp.float32) + jnp.where(valid_rows[:, None], grad_masked, 0.0)
    ).astype(jnp.bfloat16)
    proj_local = lax.dot_general(
        attended, grad_hidden, (((0,), (0,)), ((), ())), preferred_element_type=jnp.float32
    )
    members = lax.axis_size("ctx") * lax.axis_size("dp")
    proj_rows = proj_local.shape[0] // members
    kernel_rows = -(-KW // members)
    kernel_padded = jnp.pad(kernel_local, ((0, kernel_rows * members - KW), (0, 0)))
    stacked = jnp.concatenate(
        [
            proj_local.reshape(members, proj_rows, channels),
            kernel_padded.reshape(members, kernel_rows, channels),
        ],
        axis=1,
    )
    summed = lax.psum_scatter(
        stacked.astype(jnp.bfloat16), ("ctx", "dp"), scatter_dimension=0, tiled=False
    )
    grad_attended = lax.dot_general(
        grad_hidden, out_proj, (((1,), (1,)), ((), ())), preferred_element_type=jnp.float32
    ).astype(jnp.bfloat16)
    grad_heads = grad_attended.reshape(tokens, HEADS, HDIM)
    attended_heads = attended.reshape(tokens, HEADS, HDIM)
    delta_rows = jnp.sum(
        grad_heads.astype(jnp.float32) * attended_heads.astype(jnp.float32), axis=2
    )
    grad_weights = jnp.einsum(
        "qhd,khd->hqk", grad_heads, value_all, preferred_element_type=jnp.float32
    )
    grad_logits = (weights.astype(jnp.float32) * (grad_weights - delta_rows.T[:, :, None])).astype(
        jnp.bfloat16
    )
    grad_query = (
        jnp.einsum("hqk,khd->qhd", grad_logits, key_all, preferred_element_type=jnp.float32)
        * scale_factor
    )
    grad_query = grad_query.reshape(tokens, width_heads).astype(jnp.bfloat16)
    grad_key_all = (
        jnp.einsum("hqk,qhd->khd", grad_logits, query_heads, preferred_element_type=jnp.float32)
        * scale_factor
    )
    grad_value_all = jnp.einsum(
        "hqk,qhd->khd", weights, grad_heads, preferred_element_type=jnp.float32
    )
    placed = jnp.stack(
        [
            grad_key_all.reshape(span_blocks, tokens, width_heads),
            grad_value_all.reshape(span_blocks, tokens, width_heads),
        ],
        axis=1,
    )

    def grad_shift(piece_rows, offset_by):
        return passed_along(piece_rows, "ctx", offset_by)

    summed, placed, grad_query = lax.optimization_barrier((summed, placed, grad_query))
    gathered = lax.all_gather(summed, ("ctx", "dp"), axis=0, tiled=False)
    proj_sum = gathered[:, :proj_rows].reshape(members * proj_rows, channels)
    kernel_sum = (
        gathered[:, proj_rows:].astype(jnp.float32).reshape(members * kernel_rows, channels)[:KW]
    )
    own_grads = give_back(placed, grad_shift)
    grad_key = own_grads[0].astype(jnp.bfloat16)
    grad_value = own_grads[1].astype(jnp.bfloat16)
    return (
        grad_query[None],
        grad_key[None],
        grad_value[None],
        proj_sum,
        kernel_sum,
    )


def solution(mesh):
    return jax.shard_map(
        on_device,
        mesh=mesh,
        in_specs=(
            P(("group", "dp"), "ctx", None),
            P(("group", "dp"), "ctx", None),
            P(("group", "dp"), "ctx", None),
            P(("group", "dp"), "ctx", None),
            P(),
            P(),
            P(("group", "dp")),
        ),
        out_specs=(
            P(("group", "dp"), "ctx", None),
            P(("group", "dp"), "ctx", None),
            P(("group", "dp"), "ctx", None),
            P("group", None),
            P("group", None),
        ),
        check_vma=False,
    )
```

```python
import math

import jax
import jax.numpy as jnp
from jax import lax
from jax.sharding import PartitionSpec as P

HEADS = 8
HDIM = 64
KW = 31
REACH = 3


def passed_along(block, axis, distance):
    devices = range(lax.axis_size(axis))
    route = [(i - distance, i) for i in devices if i - distance in devices]
    return lax.ppermute(block, axis, route)


def padded(cells, sides, width):
    for axis, dim in sides:
        count = lax.axis_size(axis)
        ends = count - 1
        head = lax.slice_in_dim(cells, 0, width, axis=dim)
        tail = lax.slice_in_dim(cells, cells.shape[dim] - width, cells.shape[dim], axis=dim)
        cells = jnp.concatenate(
            [
                lax.ppermute(tail, axis, [(i, (i + 1) % count) for i in range(ends)]),
                cells,
                lax.ppermute(head, axis, [((i + 1) % count, i) for i in range(ends)]),
            ],
            axis=dim,
        )
    return cells


def collect(piece_own, shifter):
    from_below = [shifter(piece_own, distance) for distance in range(REACH, 0, -1)]
    from_above = [shifter(piece_own, -distance) for distance in range(1, REACH + 1)]
    return jnp.stack(from_below + [piece_own] + from_above, axis=0)


def give_back(partials, shifter):
    total = partials[REACH]
    for offset in range(2 * REACH + 1):
        if offset != REACH:
            moved = shifter(partials[offset].astype(jnp.bfloat16), offset - REACH)
            total = total + moved.astype(jnp.float32)
    return total


def exchange(block, axis, bit):
    count = lax.axis_size(axis)
    return lax.ppermute(block, axis, [(i, i ^ bit) for i in range(count)])


def halving(acc, axis):
    here = lax.axis_index(axis)
    bit = 1
    while acc.shape[0] > 1:
        pairs = acc.reshape(acc.shape[0] // 2, 2, *acc.shape[1:])
        mine = (here // bit) % 2
        keep = lax.dynamic_index_in_dim(pairs, mine, 1, keepdims=False)
        send = lax.dynamic_index_in_dim(pairs, 1 - mine, 1, keepdims=False)
        acc = keep + exchange(send.astype(jnp.bfloat16), axis, bit).astype(jnp.float32)
        bit *= 2
    return acc[0]


def doubling(acc, axis):
    here = lax.axis_index(axis)
    bit = lax.axis_size(axis) // 2
    acc = acc[None]
    while bit >= 1:
        theirs = exchange(acc, axis, bit)
        first = (here // bit) % 2 == 0
        low = jnp.where(first, acc, theirs)
        high = jnp.where(first, theirs, acc)
        acc = jnp.stack([low, high], axis=1).reshape(-1, *acc.shape[1:])
        bit //= 2
    return acc


def on_device(queries, key_rows, values, cotangent, out_proj, conv_kernel, lengths):
    tokens = queries.shape[1]
    width_heads = queries.shape[2]
    channels = out_proj.shape[1]
    span_blocks = 2 * REACH + 1
    scale_factor = 1.0 / math.sqrt(HDIM)
    halo_width = (KW - 1) // 2
    block_index = lax.axis_index("ctx")
    length_here = lengths[0]
    query_here = queries[0]
    key_here = key_rows[0]
    value_here = values[0]
    cot_here = cotangent[0]
    frames = block_index * tokens + jnp.arange(tokens, dtype=jnp.int32)
    valid_rows = frames < length_here
    key_frames = (block_index - REACH) * tokens + jnp.arange(span_blocks * tokens, dtype=jnp.int32)
    valid_keys = (key_frames >= 0) & (key_frames < length_here)

    def kv_shift(piece_rows, offset_by):
        return passed_along(piece_rows, "ctx", offset_by)

    gathered = collect(jnp.stack([key_here, value_here], axis=0), kv_shift)
    key_all = gathered[:, 0].reshape(span_blocks * tokens, HEADS, HDIM)
    value_all = gathered[:, 1].reshape(span_blocks * tokens, HEADS, HDIM)
    query_heads = query_here.reshape(tokens, HEADS, HDIM)
    scores = (
        jnp.einsum("qhd,khd->hqk", query_heads, key_all, preferred_element_type=jnp.float32)
        * scale_factor
    )
    scores = jnp.where(valid_keys[None, None, :], scores, -jnp.inf)
    row_max = jnp.max(scores, axis=2, keepdims=True)
    row_total = jnp.sum(jnp.exp(scores - row_max), axis=2, keepdims=True)
    log_total = row_max + jnp.log(row_total)
    weights = jnp.exp(scores - log_total).astype(jnp.bfloat16)
    attended = jnp.einsum("hqk,khd->qhd", weights, value_all, preferred_element_type=jnp.float32)
    attended = attended.reshape(tokens, width_heads).astype(jnp.bfloat16)
    hidden = jnp.dot(attended, out_proj, preferred_element_type=jnp.float32)
    masked = jnp.where(valid_rows[:, None], hidden, 0.0).astype(jnp.bfloat16)

    def pad_time(field_rows):
        return padded(field_rows, (("ctx", 0),), halo_width)

    padded_m = pad_time(masked)
    conv_out = jnp.zeros((tokens, channels), jnp.float32)
    for tap_index in range(KW):
        conv_out = conv_out + conv_kernel[tap_index] * padded_m[tap_index : tap_index + tokens]
    sigmoid_c = jax.nn.sigmoid(conv_out)
    grad_conv = (
        cot_here.astype(jnp.float32) * (sigmoid_c + conv_out * sigmoid_c * (1.0 - sigmoid_c))
    ).astype(jnp.bfloat16)
    padded_g = pad_time(grad_conv)
    grad_wide = grad_conv.astype(jnp.float32)
    grad_masked = jnp.zeros((tokens, channels), jnp.float32)
    kernel_terms = []
    for tap_index in range(KW):
        start_row = 2 * halo_width - tap_index
        grad_masked = (
            grad_masked + conv_kernel[tap_index] * padded_g[start_row : start_row + tokens]
        )
        kernel_terms.append(
            jnp.sum(
                padded_m[tap_index : tap_index + tokens].astype(jnp.float32) * grad_wide, axis=0
            )
        )
    kernel_local = jnp.stack(kernel_terms, axis=0)
    grad_hidden = (
        cot_here.astype(jnp.float32) + jnp.where(valid_rows[:, None], grad_masked, 0.0)
    ).astype(jnp.bfloat16)
    proj_local = lax.dot_general(
        attended, grad_hidden, (((0,), (0,)), ((), ())), preferred_element_type=jnp.float32
    )
    ctx_count = lax.axis_size("ctx")
    dp_count = lax.axis_size("dp")
    members = ctx_count * dp_count
    proj_rows = proj_local.shape[0] // members
    kernel_rows = -(-KW // members)
    kernel_padded = jnp.pad(kernel_local, ((0, kernel_rows * members - KW), (0, 0)))
    stacked = jnp.concatenate(
        [
            proj_local.reshape(dp_count, ctx_count, proj_rows, channels),
            kernel_padded.reshape(dp_count, ctx_count, kernel_rows, channels),
        ],
        axis=2,
    )
    summed = halving(halving(stacked, "dp"), "ctx").astype(jnp.bfloat16)
    grad_attended = lax.dot_general(
        grad_hidden, out_proj, (((1,), (1,)), ((), ())), preferred_element_type=jnp.float32
    ).astype(jnp.bfloat16)
    grad_heads = grad_attended.reshape(tokens, HEADS, HDIM)
    attended_heads = attended.reshape(tokens, HEADS, HDIM)
    delta_rows = jnp.sum(
        grad_heads.astype(jnp.float32) * attended_heads.astype(jnp.float32), axis=2
    )
    grad_weights = jnp.einsum(
        "qhd,khd->hqk", grad_heads, value_all, preferred_element_type=jnp.float32
    )
    grad_logits = (weights.astype(jnp.float32) * (grad_weights - delta_rows.T[:, :, None])).astype(
        jnp.bfloat16
    )
    grad_query = (
        jnp.einsum("hqk,khd->qhd", grad_logits, key_all, preferred_element_type=jnp.float32)
        * scale_factor
    )
    grad_query = grad_query.reshape(tokens, width_heads).astype(jnp.bfloat16)
    grad_key_all = (
        jnp.einsum("hqk,qhd->khd", grad_logits, query_heads, preferred_element_type=jnp.float32)
        * scale_factor
    )
    grad_value_all = jnp.einsum(
        "hqk,qhd->khd", weights, grad_heads, preferred_element_type=jnp.float32
    )
    placed = jnp.stack(
        [
            grad_key_all.reshape(span_blocks, tokens, width_heads),
            grad_value_all.reshape(span_blocks, tokens, width_heads),
        ],
        axis=1,
    )

    def grad_shift(piece_rows, offset_by):
        return passed_along(piece_rows, "ctx", offset_by)

    gathered = doubling(doubling(summed, "ctx"), "dp")
    proj_sum = gathered[:, :, :proj_rows].reshape(members * proj_rows, channels)
    kernel_sum = (
        gathered[:, :, proj_rows:].astype(jnp.float32).reshape(members * kernel_rows, channels)[:KW]
    )
    own_grads = give_back(placed, grad_shift)
    grad_key = own_grads[0].astype(jnp.bfloat16)
    grad_value = own_grads[1].astype(jnp.bfloat16)
    return (
        grad_query[None],
        grad_key[None],
        grad_value[None],
        proj_sum,
        kernel_sum,
    )


def solution(mesh):
    return jax.shard_map(
        on_device,
        mesh=mesh,
        in_specs=(
            P(("group", "dp"), "ctx", None),
            P(("group", "dp"), "ctx", None),
            P(("group", "dp"), "ctx", None),
            P(("group", "dp"), "ctx", None),
            P(),
            P(),
            P(("group", "dp")),
        ),
        out_specs=(
            P(("group", "dp"), "ctx", None),
            P(("group", "dp"), "ctx", None),
            P(("group", "dp"), "ctx", None),
            P("group", None),
            P("group", None),
        ),
        check_vma=False,
    )
```

```python
import math

import jax
import jax.numpy as jnp
from jax import lax
from jax.sharding import PartitionSpec as P

HEADS = 8
HDIM = 64
KW = 31
REACH = 3


def passed_along(block, axis, distance):
    devices = range(lax.axis_size(axis))
    route = [(i - distance, i) for i in devices if i - distance in devices]
    return lax.ppermute(block, axis, route)


def padded(cells, sides, width):
    for axis, dim in sides:
        count = lax.axis_size(axis)
        ends = count - 1
        head = lax.slice_in_dim(cells, 0, width, axis=dim)
        tail = lax.slice_in_dim(cells, cells.shape[dim] - width, cells.shape[dim], axis=dim)
        cells = jnp.concatenate(
            [
                lax.ppermute(tail, axis, [(i, (i + 1) % count) for i in range(ends)]),
                cells,
                lax.ppermute(head, axis, [((i + 1) % count, i) for i in range(ends)]),
            ],
            axis=dim,
        )
    return cells


def collect(piece_own, shifter):
    from_below = [shifter(piece_own, distance) for distance in range(REACH, 0, -1)]
    from_above = [shifter(piece_own, -distance) for distance in range(1, REACH + 1)]
    return jnp.stack(from_below + [piece_own] + from_above, axis=0)


def give_back(partials, shifter):
    total = partials[REACH]
    for offset in range(2 * REACH + 1):
        if offset != REACH:
            moved = shifter(partials[offset].astype(jnp.bfloat16), offset - REACH)
            total = total + moved.astype(jnp.float32)
    return total


def exchange(block, axis, bit):
    count = lax.axis_size(axis)
    return lax.ppermute(block, axis, [(i, i ^ bit) for i in range(count)])


def halving(acc, axis):
    here = lax.axis_index(axis)
    bit = 1
    while acc.shape[0] > 1:
        pairs = acc.reshape(acc.shape[0] // 2, 2, *acc.shape[1:])
        mine = (here // bit) % 2
        keep = lax.dynamic_index_in_dim(pairs, mine, 1, keepdims=False)
        send = lax.dynamic_index_in_dim(pairs, 1 - mine, 1, keepdims=False)
        acc = keep + exchange(send.astype(jnp.bfloat16), axis, bit).astype(jnp.float32)
        bit *= 2
    return acc[0]


def doubling(acc, axis):
    here = lax.axis_index(axis)
    bit = lax.axis_size(axis) // 2
    acc = acc[None]
    while bit >= 1:
        theirs = exchange(acc, axis, bit)
        first = (here // bit) % 2 == 0
        low = jnp.where(first, acc, theirs)
        high = jnp.where(first, theirs, acc)
        acc = jnp.stack([low, high], axis=1).reshape(-1, *acc.shape[1:])
        bit //= 2
    return acc


def on_device(queries, key_rows, values, cotangent, out_proj, conv_kernel, lengths):
    tokens = queries.shape[1]
    width_heads = queries.shape[2]
    channels = out_proj.shape[1]
    span_blocks = 2 * REACH + 1
    scale_factor = 1.0 / math.sqrt(HDIM)
    halo_width = (KW - 1) // 2
    block_index = lax.axis_index("ctx")
    length_here = lengths[0]
    query_here = queries[0]
    key_here = key_rows[0]
    value_here = values[0]
    cot_here = cotangent[0]
    frames = block_index * tokens + jnp.arange(tokens, dtype=jnp.int32)
    valid_rows = frames < length_here
    key_frames = (block_index - REACH) * tokens + jnp.arange(span_blocks * tokens, dtype=jnp.int32)
    valid_keys = (key_frames >= 0) & (key_frames < length_here)

    def kv_shift(piece_rows, offset_by):
        return passed_along(piece_rows, "ctx", offset_by)

    own_kv = jnp.stack([key_here, value_here], axis=0)
    if lax.axis_size("ctx") <= span_blocks + 1:
        ctx_count = lax.axis_size("ctx")
        spread = jnp.broadcast_to(own_kv[None], (ctx_count,) + own_kv.shape)
        everyone = lax.all_to_all(spread, "ctx", 0, 0, tiled=True)
        everyone = jnp.pad(everyone, ((REACH, REACH), (0, 0), (0, 0), (0, 0)))
        gathered = lax.dynamic_slice_in_dim(everyone, block_index, span_blocks, 0)
    else:
        gathered = collect(own_kv, kv_shift)
    key_all = gathered[:, 0].reshape(span_blocks * tokens, HEADS, HDIM)
    value_all = gathered[:, 1].reshape(span_blocks * tokens, HEADS, HDIM)
    query_heads = query_here.reshape(tokens, HEADS, HDIM)
    scores = (
        jnp.einsum("qhd,khd->hqk", query_heads, key_all, preferred_element_type=jnp.float32)
        * scale_factor
    )
    scores = jnp.where(valid_keys[None, None, :], scores, -jnp.inf)
    row_max = jnp.max(scores, axis=2, keepdims=True)
    row_total = jnp.sum(jnp.exp(scores - row_max), axis=2, keepdims=True)
    log_total = row_max + jnp.log(row_total)
    weights = jnp.exp(scores - log_total).astype(jnp.bfloat16)
    attended = jnp.einsum("hqk,khd->qhd", weights, value_all, preferred_element_type=jnp.float32)
    attended = attended.reshape(tokens, width_heads).astype(jnp.bfloat16)
    hidden = jnp.dot(attended, out_proj, preferred_element_type=jnp.float32)
    masked = jnp.where(valid_rows[:, None], hidden, 0.0).astype(jnp.bfloat16)

    def pad_time(field_rows):
        return padded(field_rows, (("ctx", 0),), halo_width)

    padded_m = pad_time(masked)
    conv_out = jnp.zeros((tokens, channels), jnp.float32)
    for tap_index in range(KW):
        conv_out = conv_out + conv_kernel[tap_index] * padded_m[tap_index : tap_index + tokens]
    sigmoid_c = jax.nn.sigmoid(conv_out)
    grad_conv = (
        cot_here.astype(jnp.float32) * (sigmoid_c + conv_out * sigmoid_c * (1.0 - sigmoid_c))
    ).astype(jnp.bfloat16)
    padded_g = pad_time(grad_conv)
    grad_wide = grad_conv.astype(jnp.float32)
    grad_masked = jnp.zeros((tokens, channels), jnp.float32)
    kernel_terms = []
    for tap_index in range(KW):
        start_row = 2 * halo_width - tap_index
        grad_masked = (
            grad_masked + conv_kernel[tap_index] * padded_g[start_row : start_row + tokens]
        )
        kernel_terms.append(
            jnp.sum(
                padded_m[tap_index : tap_index + tokens].astype(jnp.float32) * grad_wide, axis=0
            )
        )
    kernel_local = jnp.stack(kernel_terms, axis=0)
    grad_hidden = (
        cot_here.astype(jnp.float32) + jnp.where(valid_rows[:, None], grad_masked, 0.0)
    ).astype(jnp.bfloat16)
    proj_local = lax.dot_general(
        attended, grad_hidden, (((0,), (0,)), ((), ())), preferred_element_type=jnp.float32
    )
    ctx_count = lax.axis_size("ctx")
    dp_count = lax.axis_size("dp")
    members = ctx_count * dp_count
    proj_rows = proj_local.shape[0] // members
    kernel_rows = -(-KW // members)
    kernel_padded = jnp.pad(kernel_local, ((0, kernel_rows * members - KW), (0, 0)))
    stacked = jnp.concatenate(
        [
            proj_local.reshape(dp_count, ctx_count, proj_rows, channels),
            kernel_padded.reshape(dp_count, ctx_count, kernel_rows, channels),
        ],
        axis=2,
    )
    summed = halving(halving(stacked, "dp"), "ctx").astype(jnp.bfloat16)
    grad_attended = lax.dot_general(
        grad_hidden, out_proj, (((1,), (1,)), ((), ())), preferred_element_type=jnp.float32
    ).astype(jnp.bfloat16)
    grad_heads = grad_attended.reshape(tokens, HEADS, HDIM)
    attended_heads = attended.reshape(tokens, HEADS, HDIM)
    delta_rows = jnp.sum(
        grad_heads.astype(jnp.float32) * attended_heads.astype(jnp.float32), axis=2
    )
    grad_weights = jnp.einsum(
        "qhd,khd->hqk", grad_heads, value_all, preferred_element_type=jnp.float32
    )
    grad_logits = (weights.astype(jnp.float32) * (grad_weights - delta_rows.T[:, :, None])).astype(
        jnp.bfloat16
    )
    grad_query = (
        jnp.einsum("hqk,khd->qhd", grad_logits, key_all, preferred_element_type=jnp.float32)
        * scale_factor
    )
    grad_query = grad_query.reshape(tokens, width_heads).astype(jnp.bfloat16)
    grad_key_all = (
        jnp.einsum("hqk,qhd->khd", grad_logits, query_heads, preferred_element_type=jnp.float32)
        * scale_factor
    )
    grad_value_all = jnp.einsum(
        "hqk,qhd->khd", weights, grad_heads, preferred_element_type=jnp.float32
    )
    placed = jnp.stack(
        [
            grad_key_all.reshape(span_blocks, tokens, width_heads),
            grad_value_all.reshape(span_blocks, tokens, width_heads),
        ],
        axis=1,
    )

    def grad_shift(piece_rows, offset_by):
        return passed_along(piece_rows, "ctx", offset_by)

    gathered = doubling(doubling(summed, "ctx"), "dp")
    proj_sum = gathered[:, :, :proj_rows].reshape(members * proj_rows, channels)
    kernel_sum = (
        gathered[:, :, proj_rows:].astype(jnp.float32).reshape(members * kernel_rows, channels)[:KW]
    )
    own_grads = give_back(placed, grad_shift)
    grad_key = own_grads[0].astype(jnp.bfloat16)
    grad_value = own_grads[1].astype(jnp.bfloat16)
    return (
        grad_query[None],
        grad_key[None],
        grad_value[None],
        proj_sum,
        kernel_sum,
    )


def solution(mesh):
    return jax.shard_map(
        on_device,
        mesh=mesh,
        in_specs=(
            P(("group", "dp"), "ctx", None),
            P(("group", "dp"), "ctx", None),
            P(("group", "dp"), "ctx", None),
            P(("group", "dp"), "ctx", None),
            P(),
            P(),
            P(("group", "dp")),
        ),
        out_specs=(
            P(("group", "dp"), "ctx", None),
            P(("group", "dp"), "ctx", None),
            P(("group", "dp"), "ctx", None),
            P("group", None),
            P("group", None),
        ),
        check_vma=False,
    )
```

```python
import math

import jax
import jax.numpy as jnp
from jax import lax
from jax.sharding import PartitionSpec as P

HEADS = 8
HDIM = 64
KW = 31
REACH = 3


def passed_along(block, axis, distance):
    devices = range(lax.axis_size(axis))
    route = [(i - distance, i) for i in devices if i - distance in devices]
    return lax.ppermute(block, axis, route)


def padded(cells, sides, width):
    for axis, dim in sides:
        count = lax.axis_size(axis)
        ends = count - 1
        head = lax.slice_in_dim(cells, 0, width, axis=dim)
        tail = lax.slice_in_dim(cells, cells.shape[dim] - width, cells.shape[dim], axis=dim)
        cells = jnp.concatenate(
            [
                lax.ppermute(tail, axis, [(i, (i + 1) % count) for i in range(ends)]),
                cells,
                lax.ppermute(head, axis, [((i + 1) % count, i) for i in range(ends)]),
            ],
            axis=dim,
        )
    return cells


def collect(piece_own, shifter):
    below_one = shifter(piece_own, 1)
    above_one = shifter(piece_own, -1)
    below = shifter(jnp.stack([below_one, piece_own], axis=0), 2)
    above = shifter(jnp.stack([piece_own, above_one], axis=0), -2)
    return jnp.stack(
        [below[0], below[1], below_one, piece_own, above_one, above[0], above[1]], axis=0
    )


def give_back(partials, shifter):
    narrow = partials.astype(jnp.bfloat16)
    from_below = shifter(narrow[REACH + 2 :], 2).astype(jnp.float32)
    from_above = shifter(narrow[REACH - 2 :: -1], -2).astype(jnp.float32)
    upward = (partials[REACH + 1] + from_below[1]).astype(jnp.bfloat16)
    downward = (partials[REACH - 1] + from_above[1]).astype(jnp.bfloat16)
    return (
        partials[REACH]
        + from_below[0]
        + from_above[0]
        + shifter(upward, 1).astype(jnp.float32)
        + shifter(downward, -1).astype(jnp.float32)
    )


def exchange(block, axis, bit):
    count = lax.axis_size(axis)
    return lax.ppermute(block, axis, [(i, i ^ bit) for i in range(count)])


def halving(acc, axis):
    here = lax.axis_index(axis)
    bit = 1
    while acc.shape[0] > 1:
        pairs = acc.reshape(acc.shape[0] // 2, 2, *acc.shape[1:])
        mine = (here // bit) % 2
        keep = lax.dynamic_index_in_dim(pairs, mine, 1, keepdims=False)
        send = lax.dynamic_index_in_dim(pairs, 1 - mine, 1, keepdims=False)
        acc = keep + exchange(send.astype(jnp.bfloat16), axis, bit).astype(jnp.float32)
        bit *= 2
    return acc[0]


def doubling(acc, axis):
    here = lax.axis_index(axis)
    bit = lax.axis_size(axis) // 2
    acc = acc[None]
    while bit >= 1:
        theirs = exchange(acc, axis, bit)
        first = (here // bit) % 2 == 0
        low = jnp.where(first, acc, theirs)
        high = jnp.where(first, theirs, acc)
        acc = jnp.stack([low, high], axis=1).reshape(-1, *acc.shape[1:])
        bit //= 2
    return acc


def on_device(queries, key_rows, values, cotangent, out_proj, conv_kernel, lengths):
    tokens = queries.shape[1]
    width_heads = queries.shape[2]
    channels = out_proj.shape[1]
    span_blocks = 2 * REACH + 1
    scale_factor = 1.0 / math.sqrt(HDIM)
    halo_width = (KW - 1) // 2
    block_index = lax.axis_index("ctx")
    length_here = lengths[0]
    query_here = queries[0]
    key_here = key_rows[0]
    value_here = values[0]
    cot_here = cotangent[0]
    frames = block_index * tokens + jnp.arange(tokens, dtype=jnp.int32)
    valid_rows = frames < length_here
    key_frames = (block_index - REACH) * tokens + jnp.arange(span_blocks * tokens, dtype=jnp.int32)
    valid_keys = (key_frames >= 0) & (key_frames < length_here)

    def kv_shift(piece_rows, offset_by):
        return passed_along(piece_rows, "ctx", offset_by)

    gathered = collect(jnp.stack([key_here, value_here], axis=0), kv_shift)
    key_all = gathered[:, 0].reshape(span_blocks * tokens, HEADS, HDIM)
    value_all = gathered[:, 1].reshape(span_blocks * tokens, HEADS, HDIM)
    query_heads = query_here.reshape(tokens, HEADS, HDIM)
    scores = (
        jnp.einsum("qhd,khd->hqk", query_heads, key_all, preferred_element_type=jnp.float32)
        * scale_factor
    )
    scores = jnp.where(valid_keys[None, None, :], scores, -jnp.inf)
    row_max = jnp.max(scores, axis=2, keepdims=True)
    row_total = jnp.sum(jnp.exp(scores - row_max), axis=2, keepdims=True)
    log_total = row_max + jnp.log(row_total)
    weights = jnp.exp(scores - log_total).astype(jnp.bfloat16)
    attended = jnp.einsum("hqk,khd->qhd", weights, value_all, preferred_element_type=jnp.float32)
    attended = attended.reshape(tokens, width_heads).astype(jnp.bfloat16)
    hidden = jnp.dot(attended, out_proj, preferred_element_type=jnp.float32)
    masked = jnp.where(valid_rows[:, None], hidden, 0.0).astype(jnp.bfloat16)

    def pad_time(field_rows):
        return padded(field_rows, (("ctx", 0),), halo_width)

    padded_m = pad_time(masked)
    conv_out = jnp.zeros((tokens, channels), jnp.float32)
    for tap_index in range(KW):
        conv_out = conv_out + conv_kernel[tap_index] * padded_m[tap_index : tap_index + tokens]
    sigmoid_c = jax.nn.sigmoid(conv_out)
    grad_conv = (
        cot_here.astype(jnp.float32) * (sigmoid_c + conv_out * sigmoid_c * (1.0 - sigmoid_c))
    ).astype(jnp.bfloat16)
    padded_g = pad_time(grad_conv)
    grad_wide = grad_conv.astype(jnp.float32)
    grad_masked = jnp.zeros((tokens, channels), jnp.float32)
    kernel_terms = []
    for tap_index in range(KW):
        start_row = 2 * halo_width - tap_index
        grad_masked = (
            grad_masked + conv_kernel[tap_index] * padded_g[start_row : start_row + tokens]
        )
        kernel_terms.append(
            jnp.sum(
                padded_m[tap_index : tap_index + tokens].astype(jnp.float32) * grad_wide, axis=0
            )
        )
    kernel_local = jnp.stack(kernel_terms, axis=0)
    grad_hidden = (
        cot_here.astype(jnp.float32) + jnp.where(valid_rows[:, None], grad_masked, 0.0)
    ).astype(jnp.bfloat16)
    proj_local = lax.dot_general(
        attended, grad_hidden, (((0,), (0,)), ((), ())), preferred_element_type=jnp.float32
    )
    ctx_count = lax.axis_size("ctx")
    dp_count = lax.axis_size("dp")
    members = ctx_count * dp_count
    proj_rows = proj_local.shape[0] // members
    kernel_rows = -(-KW // members)
    kernel_padded = jnp.pad(kernel_local, ((0, kernel_rows * members - KW), (0, 0)))
    stacked = jnp.concatenate(
        [
            proj_local.reshape(dp_count, ctx_count, proj_rows, channels),
            kernel_padded.reshape(dp_count, ctx_count, kernel_rows, channels),
        ],
        axis=2,
    )
    summed = halving(halving(stacked, "dp"), "ctx").astype(jnp.bfloat16)
    grad_attended = lax.dot_general(
        grad_hidden, out_proj, (((1,), (1,)), ((), ())), preferred_element_type=jnp.float32
    ).astype(jnp.bfloat16)
    grad_heads = grad_attended.reshape(tokens, HEADS, HDIM)
    attended_heads = attended.reshape(tokens, HEADS, HDIM)
    delta_rows = jnp.sum(
        grad_heads.astype(jnp.float32) * attended_heads.astype(jnp.float32), axis=2
    )
    grad_weights = jnp.einsum(
        "qhd,khd->hqk", grad_heads, value_all, preferred_element_type=jnp.float32
    )
    grad_logits = (weights.astype(jnp.float32) * (grad_weights - delta_rows.T[:, :, None])).astype(
        jnp.bfloat16
    )
    grad_query = (
        jnp.einsum("hqk,khd->qhd", grad_logits, key_all, preferred_element_type=jnp.float32)
        * scale_factor
    )
    grad_query = grad_query.reshape(tokens, width_heads).astype(jnp.bfloat16)
    grad_key_all = (
        jnp.einsum("hqk,qhd->khd", grad_logits, query_heads, preferred_element_type=jnp.float32)
        * scale_factor
    )
    grad_value_all = jnp.einsum(
        "hqk,qhd->khd", weights, grad_heads, preferred_element_type=jnp.float32
    )
    placed = jnp.stack(
        [
            grad_key_all.reshape(span_blocks, tokens, width_heads),
            grad_value_all.reshape(span_blocks, tokens, width_heads),
        ],
        axis=1,
    )

    def grad_shift(piece_rows, offset_by):
        return passed_along(piece_rows, "ctx", offset_by)

    gathered = doubling(doubling(summed, "ctx"), "dp")
    proj_sum = gathered[:, :, :proj_rows].reshape(members * proj_rows, channels)
    kernel_sum = (
        gathered[:, :, proj_rows:].astype(jnp.float32).reshape(members * kernel_rows, channels)[:KW]
    )
    own_grads = give_back(placed, grad_shift)
    grad_key = own_grads[0].astype(jnp.bfloat16)
    grad_value = own_grads[1].astype(jnp.bfloat16)
    return (
        grad_query[None],
        grad_key[None],
        grad_value[None],
        proj_sum,
        kernel_sum,
    )


def solution(mesh):
    return jax.shard_map(
        on_device,
        mesh=mesh,
        in_specs=(
            P(("group", "dp"), "ctx", None),
            P(("group", "dp"), "ctx", None),
            P(("group", "dp"), "ctx", None),
            P(("group", "dp"), "ctx", None),
            P(),
            P(),
            P(("group", "dp")),
        ),
        out_specs=(
            P(("group", "dp"), "ctx", None),
            P(("group", "dp"), "ctx", None),
            P(("group", "dp"), "ctx", None),
            P("group", None),
            P("group", None),
        ),
        check_vma=False,
    )
```

```python
import math

import jax
import jax.numpy as jnp
from jax import lax
from jax.sharding import PartitionSpec as P

HEADS = 8
HDIM = 64
KW = 31
REACH = 3


def passed_along(block, axis, distance):
    devices = range(lax.axis_size(axis))
    route = [(i - distance, i) for i in devices if i - distance in devices]
    return lax.ppermute(block, axis, route)


def padded(cells, sides, width):
    for axis, dim in sides:
        count = lax.axis_size(axis)
        ends = count - 1
        head = lax.slice_in_dim(cells, 0, width, axis=dim)
        tail = lax.slice_in_dim(cells, cells.shape[dim] - width, cells.shape[dim], axis=dim)
        cells = jnp.concatenate(
            [
                lax.ppermute(tail, axis, [(i, (i + 1) % count) for i in range(ends)]),
                cells,
                lax.ppermute(head, axis, [((i + 1) % count, i) for i in range(ends)]),
            ],
            axis=dim,
        )
    return cells


def collect(piece_own, shifter):
    below_one = shifter(piece_own, 1)
    above_one = shifter(piece_own, -1)
    below = shifter(jnp.stack([below_one, piece_own], axis=0), 2)
    above = shifter(jnp.stack([piece_own, above_one], axis=0), -2)
    return jnp.stack(
        [below[0], below[1], below_one, piece_own, above_one, above[0], above[1]], axis=0
    )


def give_back(near, narrow, shifter):
    from_below = shifter(narrow[REACH + 2 :], 2).astype(jnp.float32)
    from_above = shifter(narrow[REACH - 2 :: -1], -2).astype(jnp.float32)
    upward = (near[2] + from_below[1]).astype(jnp.bfloat16)
    downward = (near[0] + from_above[1]).astype(jnp.bfloat16)
    return (
        near[1]
        + from_below[0]
        + from_above[0]
        + shifter(upward, 1).astype(jnp.float32)
        + shifter(downward, -1).astype(jnp.float32)
    )


def exchange(block, axis, bit):
    count = lax.axis_size(axis)
    return lax.ppermute(block, axis, [(i, i ^ bit) for i in range(count)])


def halving(acc, axis):
    here = lax.axis_index(axis)
    bit = lax.axis_size(axis) // 2
    while bit >= 1:
        half = acc.shape[0] // 2
        mine = (here // bit) % 2
        keep = lax.dynamic_slice_in_dim(acc, mine * half, half, 0)
        send = lax.dynamic_slice_in_dim(acc, (1 - mine) * half, half, 0)
        acc = keep + exchange(send.astype(jnp.bfloat16), axis, bit).astype(jnp.float32)
        bit //= 2
    return acc[0]


def doubling(acc, axis):
    here = lax.axis_index(axis)
    count = lax.axis_size(axis)
    acc = acc[None]
    bit = 1
    while bit < count:
        theirs = exchange(acc, axis, bit)
        first = (here // bit) % 2 == 0
        acc = jnp.concatenate(
            [jnp.where(first, acc, theirs), jnp.where(first, theirs, acc)], axis=0
        )
        bit *= 2
    return acc


def on_device(queries, key_rows, values, cotangent, out_proj, conv_kernel, lengths):
    tokens = queries.shape[1]
    width_heads = queries.shape[2]
    channels = out_proj.shape[1]
    span_blocks = 2 * REACH + 1
    scale_factor = 1.0 / math.sqrt(HDIM)
    halo_width = (KW - 1) // 2
    block_index = lax.axis_index("ctx")
    length_here = lengths[0]
    query_here = queries[0]
    key_here = key_rows[0]
    value_here = values[0]
    cot_here = cotangent[0]
    frames = block_index * tokens + jnp.arange(tokens, dtype=jnp.int32)
    valid_rows = frames < length_here
    key_frames = (block_index - REACH) * tokens + jnp.arange(span_blocks * tokens, dtype=jnp.int32)
    valid_keys = (key_frames >= 0) & (key_frames < length_here)

    def kv_shift(piece_rows, offset_by):
        return passed_along(piece_rows, "ctx", offset_by)

    gathered = collect(jnp.stack([key_here, value_here], axis=0), kv_shift)
    key_all = gathered[:, 0].reshape(span_blocks * tokens, HEADS, HDIM)
    value_all = gathered[:, 1].reshape(span_blocks * tokens, HEADS, HDIM)
    query_heads = query_here.reshape(tokens, HEADS, HDIM)
    scores = (
        jnp.einsum("qhd,khd->hqk", query_heads, key_all, preferred_element_type=jnp.float32)
        * scale_factor
    )
    scores = jnp.where(valid_keys[None, None, :], scores, -jnp.inf)
    row_max = jnp.max(scores, axis=2, keepdims=True)
    row_total = jnp.sum(jnp.exp(scores - row_max), axis=2, keepdims=True)
    log_total = row_max + jnp.log(row_total)
    weights = jnp.exp(scores - log_total).astype(jnp.bfloat16)
    attended = jnp.einsum("hqk,khd->qhd", weights, value_all, preferred_element_type=jnp.float32)
    attended = attended.reshape(tokens, width_heads).astype(jnp.bfloat16)
    hidden = jnp.dot(attended, out_proj, preferred_element_type=jnp.float32)
    masked = jnp.where(valid_rows[:, None], hidden, 0.0).astype(jnp.bfloat16)

    def pad_time(field_rows):
        return padded(field_rows, (("ctx", 0),), halo_width)

    padded_m = pad_time(masked)
    conv_out = jnp.zeros((tokens, channels), jnp.float32)
    for tap_index in range(KW):
        conv_out = conv_out + conv_kernel[tap_index] * padded_m[tap_index : tap_index + tokens]
    sigmoid_c = jax.nn.sigmoid(conv_out)
    grad_conv = (
        cot_here.astype(jnp.float32) * (sigmoid_c + conv_out * sigmoid_c * (1.0 - sigmoid_c))
    ).astype(jnp.bfloat16)
    padded_g = pad_time(grad_conv)
    grad_wide = grad_conv.astype(jnp.float32)
    grad_masked = jnp.zeros((tokens, channels), jnp.float32)
    kernel_terms = []
    for tap_index in range(KW):
        start_row = 2 * halo_width - tap_index
        grad_masked = (
            grad_masked + conv_kernel[tap_index] * padded_g[start_row : start_row + tokens]
        )
        kernel_terms.append(
            jnp.sum(
                padded_m[tap_index : tap_index + tokens].astype(jnp.float32) * grad_wide, axis=0
            )
        )
    kernel_local = jnp.stack(kernel_terms, axis=0)
    grad_hidden = (
        cot_here.astype(jnp.float32) + jnp.where(valid_rows[:, None], grad_masked, 0.0)
    ).astype(jnp.bfloat16)
    proj_local = lax.dot_general(
        attended, grad_hidden, (((0,), (0,)), ((), ())), preferred_element_type=jnp.float32
    )
    ctx_count = lax.axis_size("ctx")
    dp_count = lax.axis_size("dp")
    members = ctx_count * dp_count
    proj_rows = proj_local.shape[0] // members
    kernel_rows = -(-KW // members)
    kernel_padded = jnp.pad(kernel_local, ((0, kernel_rows * members - KW), (0, 0)))
    stacked = jnp.concatenate(
        [
            proj_local.reshape(dp_count, ctx_count, proj_rows, channels),
            kernel_padded.reshape(dp_count, ctx_count, kernel_rows, channels),
        ],
        axis=2,
    )
    summed = halving(halving(stacked, "dp"), "ctx").astype(jnp.bfloat16)
    grad_attended = lax.dot_general(
        grad_hidden, out_proj, (((1,), (1,)), ((), ())), preferred_element_type=jnp.float32
    ).astype(jnp.bfloat16)
    grad_heads = grad_attended.reshape(tokens, HEADS, HDIM)
    attended_heads = attended.reshape(tokens, HEADS, HDIM)
    delta_rows = jnp.sum(
        grad_heads.astype(jnp.float32) * attended_heads.astype(jnp.float32), axis=2
    )
    grad_weights = jnp.einsum(
        "qhd,khd->hqk", grad_heads, value_all, preferred_element_type=jnp.float32
    )
    grad_logits = (weights.astype(jnp.float32) * (grad_weights - delta_rows.T[:, :, None])).astype(
        jnp.bfloat16
    )
    grad_query = (
        jnp.einsum("hqk,khd->qhd", grad_logits, key_all, preferred_element_type=jnp.float32)
        * scale_factor
    )
    grad_query = grad_query.reshape(tokens, width_heads).astype(jnp.bfloat16)
    grad_key_all = (
        jnp.einsum("hqk,qhd->khd", grad_logits, query_heads, preferred_element_type=jnp.float32)
        * scale_factor
    )
    grad_value_all = jnp.einsum(
        "hqk,qhd->khd", weights, grad_heads, preferred_element_type=jnp.float32
    )
    key_blocks = grad_key_all.reshape(span_blocks, tokens, width_heads)
    value_blocks = grad_value_all.reshape(span_blocks, tokens, width_heads)
    narrow = jnp.stack([key_blocks, value_blocks], axis=1).astype(jnp.bfloat16)
    near = jnp.stack(
        [key_blocks[REACH - 1 : REACH + 2], value_blocks[REACH - 1 : REACH + 2]], axis=1
    )

    def grad_shift(piece_rows, offset_by):
        return passed_along(piece_rows, "ctx", offset_by)

    gathered = doubling(doubling(summed, "ctx"), "dp")
    proj_sum = gathered[:, :, :proj_rows].reshape(members * proj_rows, channels)
    kernel_sum = (
        gathered[:, :, proj_rows:].astype(jnp.float32).reshape(members * kernel_rows, channels)[:KW]
    )
    own_grads = give_back(near, narrow, grad_shift)
    grad_key = own_grads[0].astype(jnp.bfloat16)
    grad_value = own_grads[1].astype(jnp.bfloat16)
    return (
        grad_query[None],
        grad_key[None],
        grad_value[None],
        proj_sum,
        kernel_sum,
    )


def solution(mesh):
    return jax.shard_map(
        on_device,
        mesh=mesh,
        in_specs=(
            P(("group", "dp"), "ctx", None),
            P(("group", "dp"), "ctx", None),
            P(("group", "dp"), "ctx", None),
            P(("group", "dp"), "ctx", None),
            P(),
            P(),
            P(("group", "dp")),
        ),
        out_specs=(
            P(("group", "dp"), "ctx", None),
            P(("group", "dp"), "ctx", None),
            P(("group", "dp"), "ctx", None),
            P("group", None),
            P("group", None),
        ),
        check_vma=False,
    )
```

```python
import math

import jax
import jax.numpy as jnp
from jax import lax
from jax.sharding import PartitionSpec as P

HEADS = 8
HDIM = 64
KW = 31
REACH = 3


def passed_along(block, axis, distance):
    devices = range(lax.axis_size(axis))
    route = [(i - distance, i) for i in devices if i - distance in devices]
    return lax.ppermute(block, axis, route)


def padded(cells, sides, width):
    for axis, dim in sides:
        count = lax.axis_size(axis)
        ends = count - 1
        head = lax.slice_in_dim(cells, 0, width, axis=dim)
        tail = lax.slice_in_dim(cells, cells.shape[dim] - width, cells.shape[dim], axis=dim)
        cells = jnp.concatenate(
            [
                lax.ppermute(tail, axis, [(i, (i + 1) % count) for i in range(ends)]),
                cells,
                lax.ppermute(head, axis, [((i + 1) % count, i) for i in range(ends)]),
            ],
            axis=dim,
        )
    return cells


def collect(piece_own, shifter):
    below_one = shifter(piece_own, 1)
    above_one = shifter(piece_own, -1)
    below = shifter(jnp.stack([below_one, piece_own], axis=0), 2)
    above = shifter(jnp.stack([piece_own, above_one], axis=0), -2)
    return jnp.stack(
        [below[0], below[1], below_one, piece_own, above_one, above[0], above[1]], axis=0
    )


def give_back(near, narrow, shifter):
    from_below = shifter(narrow[REACH + 2 :], 2).astype(jnp.float32)
    from_above = shifter(narrow[REACH - 2 :: -1], -2).astype(jnp.float32)
    upward = (near[2] + from_below[1]).astype(jnp.bfloat16)
    downward = (near[0] + from_above[1]).astype(jnp.bfloat16)
    return (
        near[1]
        + from_below[0]
        + from_above[0]
        + shifter(upward, 1).astype(jnp.float32)
        + shifter(downward, -1).astype(jnp.float32)
    )


def exchange(block, axis, bit):
    count = lax.axis_size(axis)
    return lax.ppermute(block, axis, [(i, i ^ bit) for i in range(count)])


def halving(acc, axis):
    here = lax.axis_index(axis)
    bit = lax.axis_size(axis) // 2
    while bit >= 1:
        half = acc.shape[0] // 2
        mine = (here // bit) % 2
        keep = lax.dynamic_slice_in_dim(acc, mine * half, half, 0)
        send = lax.dynamic_slice_in_dim(acc, (1 - mine) * half, half, 0)
        acc = keep + exchange(send.astype(jnp.bfloat16), axis, bit).astype(jnp.float32)
        bit //= 2
    return acc[0]


def doubling(acc, axis):
    here = lax.axis_index(axis)
    count = lax.axis_size(axis)
    acc = acc[None]
    bit = 1
    while bit < count:
        theirs = exchange(acc, axis, bit)
        first = (here // bit) % 2 == 0
        acc = jnp.concatenate(
            [jnp.where(first, acc, theirs), jnp.where(first, theirs, acc)], axis=0
        )
        bit *= 2
    return acc


def on_device(queries, key_rows, values, cotangent, out_proj, conv_kernel, lengths):
    tokens = queries.shape[1]
    width_heads = queries.shape[2]
    channels = out_proj.shape[1]
    span_blocks = 2 * REACH + 1
    scale_factor = 1.0 / math.sqrt(HDIM)
    halo_width = (KW - 1) // 2
    block_index = lax.axis_index("ctx")
    length_here = lengths[0]
    query_here = queries[0]
    key_here = key_rows[0]
    value_here = values[0]
    cot_here = cotangent[0]
    frames = block_index * tokens + jnp.arange(tokens, dtype=jnp.int32)
    valid_rows = frames < length_here
    key_frames = (block_index - REACH) * tokens + jnp.arange(span_blocks * tokens, dtype=jnp.int32)
    valid_keys = (key_frames >= 0) & (key_frames < length_here)

    def kv_shift(piece_rows, offset_by):
        return passed_along(piece_rows, "ctx", offset_by)

    gathered = collect(jnp.stack([key_here, value_here], axis=0), kv_shift)
    key_all = gathered[:, 0].reshape(span_blocks * tokens, HEADS, HDIM)
    value_all = gathered[:, 1].reshape(span_blocks * tokens, HEADS, HDIM)
    query_heads = query_here.reshape(tokens, HEADS, HDIM)
    scores = (
        jnp.einsum("qhd,khd->hqk", query_heads, key_all, preferred_element_type=jnp.float32)
        * scale_factor
    )
    scores = jnp.where(valid_keys[None, None, :], scores, -jnp.inf)
    row_max = jnp.max(scores, axis=2, keepdims=True)
    row_total = jnp.sum(jnp.exp(scores - row_max), axis=2, keepdims=True)
    log_total = row_max + jnp.log(row_total)
    weights = jnp.exp(scores - log_total).astype(jnp.bfloat16)
    attended = jnp.einsum("hqk,khd->qhd", weights, value_all, preferred_element_type=jnp.float32)
    attended = attended.reshape(tokens, width_heads).astype(jnp.bfloat16)
    hidden = jnp.dot(attended, out_proj, preferred_element_type=jnp.float32)
    masked = jnp.where(valid_rows[:, None], hidden, 0.0).astype(jnp.bfloat16)

    def pad_time(field_rows):
        return padded(field_rows, (("ctx", 0),), halo_width)

    padded_m = pad_time(masked)
    conv_out = jnp.zeros((tokens, channels), jnp.float32)
    for tap_index in range(KW):
        conv_out = conv_out + conv_kernel[tap_index] * padded_m[tap_index : tap_index + tokens]
    sigmoid_c = jax.nn.sigmoid(conv_out)
    grad_conv = (
        cot_here.astype(jnp.float32) * (sigmoid_c + conv_out * sigmoid_c * (1.0 - sigmoid_c))
    ).astype(jnp.bfloat16)
    padded_g = pad_time(grad_conv)
    grad_wide = grad_conv.astype(jnp.float32)
    grad_masked = jnp.zeros((tokens, channels), jnp.float32)
    for tap_index in range(KW):
        start_row = 2 * halo_width - tap_index
        grad_masked = (
            grad_masked + conv_kernel[tap_index] * padded_g[start_row : start_row + tokens]
        )
    kernel_local = lax.conv_general_dilated(
        padded_m[None],
        grad_conv[:, None, :],
        window_strides=(1,),
        padding="VALID",
        dimension_numbers=("NWC", "WIO", "NWC"),
        feature_group_count=channels,
        preferred_element_type=jnp.float32,
    )[0]
    grad_hidden = (
        cot_here.astype(jnp.float32) + jnp.where(valid_rows[:, None], grad_masked, 0.0)
    ).astype(jnp.bfloat16)
    proj_local = lax.dot_general(
        attended, grad_hidden, (((0,), (0,)), ((), ())), preferred_element_type=jnp.float32
    )
    ctx_count = lax.axis_size("ctx")
    dp_count = lax.axis_size("dp")
    members = ctx_count * dp_count
    proj_rows = proj_local.shape[0] // members
    kernel_rows = -(-KW // members)
    kernel_padded = jnp.pad(kernel_local, ((0, kernel_rows * members - KW), (0, 0)))
    stacked = jnp.concatenate(
        [
            proj_local.reshape(dp_count, ctx_count, proj_rows, channels),
            kernel_padded.reshape(dp_count, ctx_count, kernel_rows, channels),
        ],
        axis=2,
    )
    summed = halving(halving(stacked, "dp"), "ctx").astype(jnp.bfloat16)
    grad_attended = lax.dot_general(
        grad_hidden, out_proj, (((1,), (1,)), ((), ())), preferred_element_type=jnp.float32
    ).astype(jnp.bfloat16)
    grad_heads = grad_attended.reshape(tokens, HEADS, HDIM)
    attended_heads = attended.reshape(tokens, HEADS, HDIM)
    delta_rows = jnp.sum(
        grad_heads.astype(jnp.float32) * attended_heads.astype(jnp.float32), axis=2
    )
    grad_weights = jnp.einsum(
        "qhd,khd->hqk", grad_heads, value_all, preferred_element_type=jnp.float32
    )
    grad_logits = (weights.astype(jnp.float32) * (grad_weights - delta_rows.T[:, :, None])).astype(
        jnp.bfloat16
    )
    grad_query = (
        jnp.einsum("hqk,khd->qhd", grad_logits, key_all, preferred_element_type=jnp.float32)
        * scale_factor
    )
    grad_query = grad_query.reshape(tokens, width_heads).astype(jnp.bfloat16)
    grad_key_all = (
        jnp.einsum("hqk,qhd->khd", grad_logits, query_heads, preferred_element_type=jnp.float32)
        * scale_factor
    )
    grad_value_all = jnp.einsum(
        "hqk,qhd->khd", weights, grad_heads, preferred_element_type=jnp.float32
    )
    key_blocks = grad_key_all.reshape(span_blocks, tokens, width_heads)
    value_blocks = grad_value_all.reshape(span_blocks, tokens, width_heads)
    narrow = jnp.stack([key_blocks, value_blocks], axis=1).astype(jnp.bfloat16)
    near = jnp.stack(
        [key_blocks[REACH - 1 : REACH + 2], value_blocks[REACH - 1 : REACH + 2]], axis=1
    )

    def grad_shift(piece_rows, offset_by):
        return passed_along(piece_rows, "ctx", offset_by)

    gathered = doubling(doubling(summed, "ctx"), "dp")
    proj_sum = gathered[:, :, :proj_rows].reshape(members * proj_rows, channels)
    kernel_sum = (
        gathered[:, :, proj_rows:].astype(jnp.float32).reshape(members * kernel_rows, channels)[:KW]
    )
    own_grads = give_back(near, narrow, grad_shift)
    grad_key = own_grads[0].astype(jnp.bfloat16)
    grad_value = own_grads[1].astype(jnp.bfloat16)
    return (
        grad_query[None],
        grad_key[None],
        grad_value[None],
        proj_sum,
        kernel_sum,
    )


def solution(mesh):
    return jax.shard_map(
        on_device,
        mesh=mesh,
        in_specs=(
            P(("group", "dp"), "ctx", None),
            P(("group", "dp"), "ctx", None),
            P(("group", "dp"), "ctx", None),
            P(("group", "dp"), "ctx", None),
            P(),
            P(),
            P(("group", "dp")),
        ),
        out_specs=(
            P(("group", "dp"), "ctx", None),
            P(("group", "dp"), "ctx", None),
            P(("group", "dp"), "ctx", None),
            P("group", None),
            P("group", None),
        ),
        check_vma=False,
    )
```

```python
import math

import jax
import jax.numpy as jnp
from jax import lax
from jax.sharding import PartitionSpec as P

HEADS = 8
HDIM = 64
KW = 31
REACH = 3


def passed_along(block, axis, distance):
    devices = range(lax.axis_size(axis))
    route = [(i - distance, i) for i in devices if i - distance in devices]
    return lax.ppermute(block, axis, route)


def padded(cells, sides, width):
    for axis, dim in sides:
        count = lax.axis_size(axis)
        ends = count - 1
        head = lax.slice_in_dim(cells, 0, width, axis=dim)
        tail = lax.slice_in_dim(cells, cells.shape[dim] - width, cells.shape[dim], axis=dim)
        cells = jnp.concatenate(
            [
                lax.ppermute(tail, axis, [(i, (i + 1) % count) for i in range(ends)]),
                cells,
                lax.ppermute(head, axis, [((i + 1) % count, i) for i in range(ends)]),
            ],
            axis=dim,
        )
    return cells


def collect(piece_own, shifter):
    from_below = [shifter(piece_own, distance) for distance in range(REACH, 0, -1)]
    from_above = [shifter(piece_own, -distance) for distance in range(1, REACH + 1)]
    return jnp.stack(from_below + [piece_own] + from_above, axis=0)


def give_back(near, narrow, shifter):
    from_below = shifter(narrow[REACH + 2 :], 2).astype(jnp.float32)
    from_above = shifter(narrow[REACH - 2 :: -1], -2).astype(jnp.float32)
    upward = (near[2] + from_below[1]).astype(jnp.bfloat16)
    downward = (near[0] + from_above[1]).astype(jnp.bfloat16)
    return (
        near[1]
        + from_below[0]
        + from_above[0]
        + shifter(upward, 1).astype(jnp.float32)
        + shifter(downward, -1).astype(jnp.float32)
    )


def exchange(block, axis, bit):
    count = lax.axis_size(axis)
    return lax.ppermute(block, axis, [(i, i ^ bit) for i in range(count)])


def halving(acc, axis):
    here = lax.axis_index(axis)
    bit = lax.axis_size(axis) // 2
    while bit >= 1:
        half = acc.shape[0] // 2
        mine = (here // bit) % 2
        keep = lax.dynamic_slice_in_dim(acc, mine * half, half, 0)
        send = lax.dynamic_slice_in_dim(acc, (1 - mine) * half, half, 0)
        acc = keep + exchange(send.astype(jnp.bfloat16), axis, bit).astype(jnp.float32)
        bit //= 2
    return acc[0]


def doubling(acc, axis):
    here = lax.axis_index(axis)
    count = lax.axis_size(axis)
    acc = acc[None]
    bit = 1
    while bit < count:
        theirs = exchange(acc, axis, bit)
        first = (here // bit) % 2 == 0
        acc = jnp.concatenate(
            [jnp.where(first, acc, theirs), jnp.where(first, theirs, acc)], axis=0
        )
        bit *= 2
    return acc


def on_device(queries, key_rows, values, cotangent, out_proj, conv_kernel, lengths):
    tokens = queries.shape[1]
    width_heads = queries.shape[2]
    channels = out_proj.shape[1]
    span_blocks = 2 * REACH + 1
    scale_factor = 1.0 / math.sqrt(HDIM)
    halo_width = (KW - 1) // 2
    block_index = lax.axis_index("ctx")
    length_here = lengths[0]
    query_here = queries[0]
    key_here = key_rows[0]
    value_here = values[0]
    cot_here = cotangent[0]
    frames = block_index * tokens + jnp.arange(tokens, dtype=jnp.int32)
    valid_rows = frames < length_here
    key_frames = (block_index - REACH) * tokens + jnp.arange(span_blocks * tokens, dtype=jnp.int32)
    valid_keys = (key_frames >= 0) & (key_frames < length_here)

    def kv_shift(piece_rows, offset_by):
        return passed_along(piece_rows, "ctx", offset_by)

    gathered = collect(jnp.stack([key_here, value_here], axis=0), kv_shift)
    key_all = gathered[:, 0].reshape(span_blocks * tokens, HEADS, HDIM)
    value_all = gathered[:, 1].reshape(span_blocks * tokens, HEADS, HDIM)
    query_heads = query_here.reshape(tokens, HEADS, HDIM)
    scores = (
        jnp.einsum("qhd,khd->hqk", query_heads, key_all, preferred_element_type=jnp.float32)
        * scale_factor
    )
    scores = jnp.where(valid_keys[None, None, :], scores, -jnp.inf)
    row_max = jnp.max(scores, axis=2, keepdims=True)
    row_total = jnp.sum(jnp.exp(scores - row_max), axis=2, keepdims=True)
    log_total = row_max + jnp.log(row_total)
    weights = jnp.exp(scores - log_total).astype(jnp.bfloat16)
    attended = jnp.einsum("hqk,khd->qhd", weights, value_all, preferred_element_type=jnp.float32)
    attended = attended.reshape(tokens, width_heads).astype(jnp.bfloat16)
    hidden = jnp.dot(attended, out_proj, preferred_element_type=jnp.float32)
    masked = jnp.where(valid_rows[:, None], hidden, 0.0).astype(jnp.bfloat16)

    def pad_time(field_rows):
        return padded(field_rows, (("ctx", 0),), halo_width)

    padded_m = pad_time(masked)
    conv_out = jnp.zeros((tokens, channels), jnp.float32)
    for tap_index in range(KW):
        conv_out = conv_out + conv_kernel[tap_index] * padded_m[tap_index : tap_index + tokens]
    sigmoid_c = jax.nn.sigmoid(conv_out)
    grad_conv = (
        cot_here.astype(jnp.float32) * (sigmoid_c + conv_out * sigmoid_c * (1.0 - sigmoid_c))
    ).astype(jnp.bfloat16)
    padded_g = pad_time(grad_conv)
    grad_wide = grad_conv.astype(jnp.float32)
    grad_masked = jnp.zeros((tokens, channels), jnp.float32)
    for tap_index in range(KW):
        start_row = 2 * halo_width - tap_index
        grad_masked = (
            grad_masked + conv_kernel[tap_index] * padded_g[start_row : start_row + tokens]
        )
    kernel_local = lax.conv_general_dilated(
        padded_m[None],
        grad_conv[:, None, :],
        window_strides=(1,),
        padding="VALID",
        dimension_numbers=("NWC", "WIO", "NWC"),
        feature_group_count=channels,
        preferred_element_type=jnp.float32,
    )[0]
    grad_hidden = (
        cot_here.astype(jnp.float32) + jnp.where(valid_rows[:, None], grad_masked, 0.0)
    ).astype(jnp.bfloat16)
    proj_local = lax.dot_general(
        attended, grad_hidden, (((0,), (0,)), ((), ())), preferred_element_type=jnp.float32
    )
    ctx_count = lax.axis_size("ctx")
    dp_count = lax.axis_size("dp")
    members = ctx_count * dp_count
    proj_rows = proj_local.shape[0] // members
    kernel_rows = -(-KW // members)
    kernel_padded = jnp.pad(kernel_local, ((0, kernel_rows * members - KW), (0, 0)))
    stacked = jnp.concatenate(
        [
            proj_local.reshape(dp_count, ctx_count, proj_rows, channels),
            kernel_padded.reshape(dp_count, ctx_count, kernel_rows, channels),
        ],
        axis=2,
    )
    summed = halving(halving(stacked, "dp"), "ctx").astype(jnp.bfloat16)
    grad_attended = lax.dot_general(
        grad_hidden, out_proj, (((1,), (1,)), ((), ())), preferred_element_type=jnp.float32
    ).astype(jnp.bfloat16)
    grad_heads = grad_attended.reshape(tokens, HEADS, HDIM)
    attended_heads = attended.reshape(tokens, HEADS, HDIM)
    delta_rows = jnp.sum(
        grad_heads.astype(jnp.float32) * attended_heads.astype(jnp.float32), axis=2
    )
    grad_weights = jnp.einsum(
        "qhd,khd->hqk", grad_heads, value_all, preferred_element_type=jnp.float32
    )
    grad_logits = (weights.astype(jnp.float32) * (grad_weights - delta_rows.T[:, :, None])).astype(
        jnp.bfloat16
    )
    grad_query = (
        jnp.einsum("hqk,khd->qhd", grad_logits, key_all, preferred_element_type=jnp.float32)
        * scale_factor
    )
    grad_query = grad_query.reshape(tokens, width_heads).astype(jnp.bfloat16)
    grad_key_all = (
        jnp.einsum("hqk,qhd->khd", grad_logits, query_heads, preferred_element_type=jnp.float32)
        * scale_factor
    )
    grad_value_all = jnp.einsum(
        "hqk,qhd->khd", weights, grad_heads, preferred_element_type=jnp.float32
    )
    key_blocks = grad_key_all.reshape(span_blocks, tokens, width_heads)
    value_blocks = grad_value_all.reshape(span_blocks, tokens, width_heads)
    narrow = jnp.stack([key_blocks, value_blocks], axis=1).astype(jnp.bfloat16)
    near = jnp.stack(
        [key_blocks[REACH - 1 : REACH + 2], value_blocks[REACH - 1 : REACH + 2]], axis=1
    )

    def grad_shift(piece_rows, offset_by):
        return passed_along(piece_rows, "ctx", offset_by)

    gathered = doubling(doubling(summed, "ctx"), "dp")
    proj_sum = gathered[:, :, :proj_rows].reshape(members * proj_rows, channels)
    kernel_sum = (
        gathered[:, :, proj_rows:].astype(jnp.float32).reshape(members * kernel_rows, channels)[:KW]
    )
    own_grads = give_back(near, narrow, grad_shift)
    grad_key = own_grads[0].astype(jnp.bfloat16)
    grad_value = own_grads[1].astype(jnp.bfloat16)
    return (
        grad_query[None],
        grad_key[None],
        grad_value[None],
        proj_sum,
        kernel_sum,
    )


def solution(mesh):
    return jax.shard_map(
        on_device,
        mesh=mesh,
        in_specs=(
            P(("group", "dp"), "ctx", None),
            P(("group", "dp"), "ctx", None),
            P(("group", "dp"), "ctx", None),
            P(("group", "dp"), "ctx", None),
            P(),
            P(),
            P(("group", "dp")),
        ),
        out_specs=(
            P(("group", "dp"), "ctx", None),
            P(("group", "dp"), "ctx", None),
            P(("group", "dp"), "ctx", None),
            P("group", None),
            P("group", None),
        ),
        check_vma=False,
    )
```

```python
import math

import jax
import jax.numpy as jnp
from jax import lax
from jax.sharding import PartitionSpec as P

HEADS = 8
HDIM = 64
KW = 31
REACH = 3


def passed_along(block, axis, distance):
    devices = range(lax.axis_size(axis))
    route = [(i - distance, i) for i in devices if i - distance in devices]
    return lax.ppermute(block, axis, route)


def padded(cells, sides, width):
    for axis, dim in sides:
        count = lax.axis_size(axis)
        ends = count - 1
        head = lax.slice_in_dim(cells, 0, width, axis=dim)
        tail = lax.slice_in_dim(cells, cells.shape[dim] - width, cells.shape[dim], axis=dim)
        cells = jnp.concatenate(
            [
                lax.ppermute(tail, axis, [(i, (i + 1) % count) for i in range(ends)]),
                cells,
                lax.ppermute(head, axis, [((i + 1) % count, i) for i in range(ends)]),
            ],
            axis=dim,
        )
    return cells


def collect(piece_own, shifter, up_extra, down_extra):
    rows = piece_own.shape[0] * piece_own.shape[1]
    flat = piece_own.reshape(rows, piece_own.shape[2])
    got_below = shifter(jnp.concatenate([flat, up_extra], axis=0), 1)
    got_above = shifter(jnp.concatenate([flat, down_extra], axis=0), -1)
    below_one = got_below[:rows].reshape(piece_own.shape)
    above_one = got_above[:rows].reshape(piece_own.shape)
    below = shifter(jnp.stack([below_one, piece_own], axis=0), 2)
    above = shifter(jnp.stack([piece_own, above_one], axis=0), -2)
    window = jnp.stack(
        [below[0], below[1], below_one, piece_own, above_one, above[0], above[1]], axis=0
    )
    return window, got_below[rows:], got_above[rows:]


def give_back(near, narrow, shifter):
    from_below = shifter(narrow[REACH + 2 :], 2).astype(jnp.float32)
    from_above = shifter(narrow[REACH - 2 :: -1], -2).astype(jnp.float32)
    upward = (near[2] + from_below[1]).astype(jnp.bfloat16)
    downward = (near[0] + from_above[1]).astype(jnp.bfloat16)
    return (
        near[1]
        + from_below[0]
        + from_above[0]
        + shifter(upward, 1).astype(jnp.float32)
        + shifter(downward, -1).astype(jnp.float32)
    )


def exchange(block, axis, bit):
    count = lax.axis_size(axis)
    return lax.ppermute(block, axis, [(i, i ^ bit) for i in range(count)])


def halving(acc, axis):
    here = lax.axis_index(axis)
    bit = lax.axis_size(axis) // 2
    while bit >= 1:
        half = acc.shape[0] // 2
        mine = (here // bit) % 2
        keep = lax.dynamic_slice_in_dim(acc, mine * half, half, 0)
        send = lax.dynamic_slice_in_dim(acc, (1 - mine) * half, half, 0)
        acc = keep + exchange(send.astype(jnp.bfloat16), axis, bit).astype(jnp.float32)
        bit //= 2
    return acc[0]


def doubling(acc, axis):
    here = lax.axis_index(axis)
    count = lax.axis_size(axis)
    acc = acc[None]
    bit = 1
    while bit < count:
        theirs = exchange(acc, axis, bit)
        first = (here // bit) % 2 == 0
        acc = jnp.concatenate(
            [jnp.where(first, acc, theirs), jnp.where(first, theirs, acc)], axis=0
        )
        bit *= 2
    return acc


def on_device(queries, key_rows, values, cotangent, out_proj, conv_kernel, lengths):
    tokens = queries.shape[1]
    width_heads = queries.shape[2]
    channels = out_proj.shape[1]
    span_blocks = 2 * REACH + 1
    scale_factor = 1.0 / math.sqrt(HDIM)
    halo_width = (KW - 1) // 2
    block_index = lax.axis_index("ctx")
    length_here = lengths[0]
    query_here = queries[0]
    key_here = key_rows[0]
    value_here = values[0]
    cot_here = cotangent[0]
    frames = block_index * tokens + jnp.arange(tokens, dtype=jnp.int32)
    valid_rows = frames < length_here
    key_frames = (block_index - REACH) * tokens + jnp.arange(span_blocks * tokens, dtype=jnp.int32)
    valid_keys = (key_frames >= 0) & (key_frames < length_here)

    def kv_shift(piece_rows, offset_by):
        return passed_along(piece_rows, "ctx", offset_by)

    halo_rows = -(-halo_width // 8) * 8

    def edge_rows(rows_here):
        padded_rows = jnp.pad(rows_here, ((0, halo_rows - halo_width), (0, 0)))
        return padded_rows.reshape(-1, width_heads)

    def edge_back(packed):
        return packed.reshape(halo_rows, channels)[:halo_width]

    gathered, cot_low, cot_high = collect(
        jnp.stack([key_here, value_here], axis=0),
        kv_shift,
        edge_rows(cot_here[tokens - halo_width :]),
        edge_rows(cot_here[:halo_width]),
    )
    cot_wide = jnp.concatenate([edge_back(cot_low), cot_here, edge_back(cot_high)], axis=0)
    key_all = gathered[:, 0].reshape(span_blocks * tokens, HEADS, HDIM)
    value_all = gathered[:, 1].reshape(span_blocks * tokens, HEADS, HDIM)
    query_heads = query_here.reshape(tokens, HEADS, HDIM)
    scores = (
        jnp.einsum("qhd,khd->hqk", query_heads, key_all, preferred_element_type=jnp.float32)
        * scale_factor
    )
    scores = jnp.where(valid_keys[None, None, :], scores, -jnp.inf)
    row_max = jnp.max(scores, axis=2, keepdims=True)
    row_total = jnp.sum(jnp.exp(scores - row_max), axis=2, keepdims=True)
    log_total = row_max + jnp.log(row_total)
    weights = jnp.exp(scores - log_total).astype(jnp.bfloat16)
    attended = jnp.einsum("hqk,khd->qhd", weights, value_all, preferred_element_type=jnp.float32)
    attended = attended.reshape(tokens, width_heads).astype(jnp.bfloat16)
    hidden = jnp.dot(attended, out_proj, preferred_element_type=jnp.float32)
    masked = jnp.where(valid_rows[:, None], hidden, 0.0).astype(jnp.bfloat16)

    wide_rows = tokens + 2 * halo_width
    padded_m = padded(masked, (("ctx", 0),), 2 * halo_width)
    conv_out = jnp.zeros((wide_rows, channels), jnp.float32)
    for tap_index in range(KW):
        conv_out = conv_out + conv_kernel[tap_index] * padded_m[tap_index : tap_index + wide_rows]
    sigmoid_c = jax.nn.sigmoid(conv_out)
    grad_conv = (
        cot_wide.astype(jnp.float32) * (sigmoid_c + conv_out * sigmoid_c * (1.0 - sigmoid_c))
    ).astype(jnp.bfloat16)
    grad_masked = jnp.zeros((tokens, channels), jnp.float32)
    for tap_index in range(KW):
        start_row = 2 * halo_width - tap_index
        grad_masked = (
            grad_masked + conv_kernel[tap_index] * grad_conv[start_row : start_row + tokens]
        )
    kernel_local = lax.conv_general_dilated(
        padded_m[None, halo_width : halo_width + wide_rows],
        grad_conv[halo_width : halo_width + tokens, None, :],
        window_strides=(1,),
        padding="VALID",
        dimension_numbers=("NWC", "WIO", "NWC"),
        feature_group_count=channels,
        preferred_element_type=jnp.float32,
    )[0]
    grad_hidden = (
        cot_here.astype(jnp.float32) + jnp.where(valid_rows[:, None], grad_masked, 0.0)
    ).astype(jnp.bfloat16)
    proj_local = lax.dot_general(
        attended, grad_hidden, (((0,), (0,)), ((), ())), preferred_element_type=jnp.float32
    )
    ctx_count = lax.axis_size("ctx")
    dp_count = lax.axis_size("dp")
    members = ctx_count * dp_count
    proj_rows = proj_local.shape[0] // members
    kernel_rows = -(-KW // members)
    kernel_padded = jnp.pad(kernel_local, ((0, kernel_rows * members - KW), (0, 0)))
    stacked = jnp.concatenate(
        [
            proj_local.reshape(dp_count, ctx_count, proj_rows, channels),
            kernel_padded.reshape(dp_count, ctx_count, kernel_rows, channels),
        ],
        axis=2,
    )
    summed = halving(halving(stacked, "dp"), "ctx").astype(jnp.bfloat16)
    grad_attended = lax.dot_general(
        grad_hidden, out_proj, (((1,), (1,)), ((), ())), preferred_element_type=jnp.float32
    ).astype(jnp.bfloat16)
    grad_heads = grad_attended.reshape(tokens, HEADS, HDIM)
    attended_heads = attended.reshape(tokens, HEADS, HDIM)
    delta_rows = jnp.sum(
        grad_heads.astype(jnp.float32) * attended_heads.astype(jnp.float32), axis=2
    )
    grad_weights = jnp.einsum(
        "qhd,khd->hqk", grad_heads, value_all, preferred_element_type=jnp.float32
    )
    grad_logits = (weights.astype(jnp.float32) * (grad_weights - delta_rows.T[:, :, None])).astype(
        jnp.bfloat16
    )
    grad_query = (
        jnp.einsum("hqk,khd->qhd", grad_logits, key_all, preferred_element_type=jnp.float32)
        * scale_factor
    )
    grad_query = grad_query.reshape(tokens, width_heads).astype(jnp.bfloat16)
    grad_key_all = (
        jnp.einsum("hqk,qhd->khd", grad_logits, query_heads, preferred_element_type=jnp.float32)
        * scale_factor
    )
    grad_value_all = jnp.einsum(
        "hqk,qhd->khd", weights, grad_heads, preferred_element_type=jnp.float32
    )
    key_blocks = grad_key_all.reshape(span_blocks, tokens, width_heads)
    value_blocks = grad_value_all.reshape(span_blocks, tokens, width_heads)
    narrow = jnp.stack([key_blocks, value_blocks], axis=1).astype(jnp.bfloat16)
    near = jnp.stack(
        [key_blocks[REACH - 1 : REACH + 2], value_blocks[REACH - 1 : REACH + 2]], axis=1
    )

    def grad_shift(piece_rows, offset_by):
        return passed_along(piece_rows, "ctx", offset_by)

    gathered = doubling(doubling(summed, "ctx"), "dp")
    proj_sum = gathered[:, :, :proj_rows].reshape(members * proj_rows, channels)
    kernel_sum = (
        gathered[:, :, proj_rows:].astype(jnp.float32).reshape(members * kernel_rows, channels)[:KW]
    )
    own_grads = give_back(near, narrow, grad_shift)
    grad_key = own_grads[0].astype(jnp.bfloat16)
    grad_value = own_grads[1].astype(jnp.bfloat16)
    return (
        grad_query[None],
        grad_key[None],
        grad_value[None],
        proj_sum,
        kernel_sum,
    )


def solution(mesh):
    return jax.shard_map(
        on_device,
        mesh=mesh,
        in_specs=(
            P(("group", "dp"), "ctx", None),
            P(("group", "dp"), "ctx", None),
            P(("group", "dp"), "ctx", None),
            P(("group", "dp"), "ctx", None),
            P(),
            P(),
            P(("group", "dp")),
        ),
        out_specs=(
            P(("group", "dp"), "ctx", None),
            P(("group", "dp"), "ctx", None),
            P(("group", "dp"), "ctx", None),
            P("group", None),
            P("group", None),
        ),
        check_vma=False,
    )
```

```python
import math

import jax
import jax.numpy as jnp
from jax import lax
from jax.sharding import PartitionSpec as P

HEADS = 8
HDIM = 64
KW = 31
REACH = 3


def passed_along(block, axis, distance):
    devices = range(lax.axis_size(axis))
    route = [(i - distance, i) for i in devices if i - distance in devices]
    return lax.ppermute(block, axis, route)


def padded(cells, sides, width):
    for axis, dim in sides:
        count = lax.axis_size(axis)
        ends = count - 1
        head = lax.slice_in_dim(cells, 0, width, axis=dim)
        tail = lax.slice_in_dim(cells, cells.shape[dim] - width, cells.shape[dim], axis=dim)
        cells = jnp.concatenate(
            [
                lax.ppermute(tail, axis, [(i, (i + 1) % count) for i in range(ends)]),
                cells,
                lax.ppermute(head, axis, [((i + 1) % count, i) for i in range(ends)]),
            ],
            axis=dim,
        )
    return cells


def collect(piece_own, shifter, up_extra, down_extra):
    rows = piece_own.shape[0] * piece_own.shape[1]
    flat = piece_own.reshape(rows, piece_own.shape[2])
    got_below = shifter(jnp.concatenate([flat, up_extra], axis=0), 1)
    got_above = shifter(jnp.concatenate([flat, down_extra], axis=0), -1)
    below_one = got_below[:rows].reshape(piece_own.shape)
    above_one = got_above[:rows].reshape(piece_own.shape)
    below = shifter(jnp.stack([below_one, piece_own], axis=0), 2)
    above = shifter(jnp.stack([piece_own, above_one], axis=0), -2)
    window = jnp.stack(
        [below[0], below[1], below_one, piece_own, above_one, above[0], above[1]], axis=0
    )
    return window, got_below[rows:], got_above[rows:]


def give_back(near, narrow, shifter):
    from_below = shifter(narrow[REACH + 2 :], 2).astype(jnp.float32)
    from_above = shifter(narrow[REACH - 2 :: -1], -2).astype(jnp.float32)
    upward = (near[2] + from_below[1]).astype(jnp.bfloat16)
    downward = (near[0] + from_above[1]).astype(jnp.bfloat16)
    return (
        near[1]
        + from_below[0]
        + from_above[0]
        + shifter(upward, 1).astype(jnp.float32)
        + shifter(downward, -1).astype(jnp.float32)
    )


def exchange(block, axis, bit):
    count = lax.axis_size(axis)
    return lax.ppermute(block, axis, [(i, i ^ bit) for i in range(count)])


def halving(acc, axis):
    here = lax.axis_index(axis)
    bit = lax.axis_size(axis) // 2
    while bit >= 1:
        half = acc.shape[0] // 2
        mine = (here // bit) % 2
        keep = lax.dynamic_slice_in_dim(acc, mine * half, half, 0)
        send = lax.dynamic_slice_in_dim(acc, (1 - mine) * half, half, 0)
        acc = keep + exchange(send.astype(jnp.bfloat16), axis, bit).astype(jnp.float32)
        bit //= 2
    return acc[0]


def doubling(acc, axis):
    here = lax.axis_index(axis)
    count = lax.axis_size(axis)
    acc = acc[None]
    bit = 1
    while bit < count:
        theirs = exchange(acc, axis, bit)
        first = (here // bit) % 2 == 0
        acc = jnp.concatenate(
            [jnp.where(first, acc, theirs), jnp.where(first, theirs, acc)], axis=0
        )
        bit *= 2
    return acc


def on_device(queries, key_rows, values, cotangent, out_proj, conv_kernel, lengths):
    tokens = queries.shape[1]
    width_heads = queries.shape[2]
    channels = out_proj.shape[1]
    span_blocks = 2 * REACH + 1
    scale_factor = 1.0 / math.sqrt(HDIM)
    halo_width = (KW - 1) // 2
    block_index = lax.axis_index("ctx")
    length_here = lengths[0]
    query_here = queries[0]
    key_here = key_rows[0]
    value_here = values[0]
    cot_here = cotangent[0]
    frames = block_index * tokens + jnp.arange(tokens, dtype=jnp.int32)
    valid_rows = frames < length_here
    key_frames = (block_index - REACH) * tokens + jnp.arange(span_blocks * tokens, dtype=jnp.int32)
    valid_keys = (key_frames >= 0) & (key_frames < length_here)

    def kv_shift(piece_rows, offset_by):
        return passed_along(piece_rows, "ctx", offset_by)

    halo_rows = -(-halo_width // 8) * 8

    def edge_rows(rows_here):
        padded_rows = jnp.pad(rows_here, ((0, halo_rows - halo_width), (0, 0)))
        return padded_rows.reshape(-1, width_heads)

    def edge_back(packed):
        return packed.reshape(halo_rows, channels)[:halo_width]

    gathered, cot_low, cot_high = collect(
        jnp.stack([key_here, value_here], axis=0),
        kv_shift,
        edge_rows(cot_here[tokens - halo_width :]),
        edge_rows(cot_here[:halo_width]),
    )
    cot_wide = jnp.concatenate([edge_back(cot_low), cot_here, edge_back(cot_high)], axis=0)
    kv_rows = span_blocks * tokens
    key_all = gathered[:, 0].reshape(kv_rows, width_heads)
    value_all = gathered[:, 1].reshape(kv_rows, width_heads)
    head_mask = (
        jnp.arange(HEADS, dtype=jnp.int32)[:, None, None]
        == (jnp.arange(width_heads, dtype=jnp.int32) // HDIM)[None, None, :]
    )

    def spread(rows):
        return jnp.where(head_mask, rows[None], jnp.zeros((), rows.dtype)).reshape(
            HEADS * tokens, width_heads
        )

    def own_heads(stacked_rows):
        picked = jnp.where(head_mask, stacked_rows.reshape(HEADS, tokens, width_heads), 0.0)
        return jnp.sum(picked, axis=0)

    def contract(lhs, rhs, lhs_dim, rhs_dim):
        return lax.dot_general(
            lhs, rhs, (((lhs_dim,), (rhs_dim,)), ((), ())), preferred_element_type=jnp.float32
        )

    query_spread = spread(query_here)
    scores = contract(query_spread, key_all, 1, 1) * scale_factor
    scores = jnp.where(valid_keys[None, :], scores, -jnp.inf)
    row_max = jnp.max(scores, axis=1, keepdims=True)
    row_total = jnp.sum(jnp.exp(scores - row_max), axis=1, keepdims=True)
    log_total = row_max + jnp.log(row_total)
    weights = jnp.exp(scores - log_total).astype(jnp.bfloat16)
    attended = own_heads(contract(weights, value_all, 1, 0)).astype(jnp.bfloat16)
    hidden = jnp.dot(attended, out_proj, preferred_element_type=jnp.float32)
    masked = jnp.where(valid_rows[:, None], hidden, 0.0).astype(jnp.bfloat16)

    wide_rows = tokens + 2 * halo_width
    padded_m = padded(masked, (("ctx", 0),), 2 * halo_width)
    conv_out = jnp.zeros((wide_rows, channels), jnp.float32)
    for tap_index in range(KW):
        conv_out = conv_out + conv_kernel[tap_index] * padded_m[tap_index : tap_index + wide_rows]
    sigmoid_c = jax.nn.sigmoid(conv_out)
    grad_conv = (
        cot_wide.astype(jnp.float32) * (sigmoid_c + conv_out * sigmoid_c * (1.0 - sigmoid_c))
    ).astype(jnp.bfloat16)
    grad_masked = jnp.zeros((tokens, channels), jnp.float32)
    for tap_index in range(KW):
        start_row = 2 * halo_width - tap_index
        grad_masked = (
            grad_masked + conv_kernel[tap_index] * grad_conv[start_row : start_row + tokens]
        )
    kernel_local = lax.conv_general_dilated(
        padded_m[None, halo_width : halo_width + wide_rows],
        grad_conv[halo_width : halo_width + tokens, None, :],
        window_strides=(1,),
        padding="VALID",
        dimension_numbers=("NWC", "WIO", "NWC"),
        feature_group_count=channels,
        preferred_element_type=jnp.float32,
    )[0]
    grad_hidden = (
        cot_here.astype(jnp.float32) + jnp.where(valid_rows[:, None], grad_masked, 0.0)
    ).astype(jnp.bfloat16)
    proj_local = lax.dot_general(
        attended, grad_hidden, (((0,), (0,)), ((), ())), preferred_element_type=jnp.float32
    )
    ctx_count = lax.axis_size("ctx")
    dp_count = lax.axis_size("dp")
    members = ctx_count * dp_count
    proj_rows = proj_local.shape[0] // members
    kernel_rows = -(-KW // members)
    kernel_padded = jnp.pad(kernel_local, ((0, kernel_rows * members - KW), (0, 0)))
    stacked = jnp.concatenate(
        [
            proj_local.reshape(dp_count, ctx_count, proj_rows, channels),
            kernel_padded.reshape(dp_count, ctx_count, kernel_rows, channels),
        ],
        axis=2,
    )
    summed = halving(halving(stacked, "dp"), "ctx").astype(jnp.bfloat16)
    grad_attended = lax.dot_general(
        grad_hidden, out_proj, (((1,), (1,)), ((), ())), preferred_element_type=jnp.float32
    ).astype(jnp.bfloat16)
    delta_rows = jnp.sum(
        (grad_attended.astype(jnp.float32) * attended.astype(jnp.float32)).reshape(
            tokens, HEADS, HDIM
        ),
        axis=2,
    )
    grad_spread = spread(grad_attended)
    grad_weights = contract(grad_spread, value_all, 1, 1)
    grad_logits = (
        weights.astype(jnp.float32) * (grad_weights - delta_rows.T.reshape(HEADS * tokens, 1))
    ).astype(jnp.bfloat16)
    grad_query = (own_heads(contract(grad_logits, key_all, 1, 0)) * scale_factor).astype(
        jnp.bfloat16
    )
    grad_key_all = contract(grad_logits, query_spread, 0, 0) * scale_factor
    grad_value_all = contract(weights, grad_spread, 0, 0)
    key_blocks = grad_key_all.reshape(span_blocks, tokens, width_heads)
    value_blocks = grad_value_all.reshape(span_blocks, tokens, width_heads)
    narrow = jnp.stack([key_blocks, value_blocks], axis=1).astype(jnp.bfloat16)
    near = jnp.stack(
        [key_blocks[REACH - 1 : REACH + 2], value_blocks[REACH - 1 : REACH + 2]], axis=1
    )

    def grad_shift(piece_rows, offset_by):
        return passed_along(piece_rows, "ctx", offset_by)

    gathered = doubling(doubling(summed, "ctx"), "dp")
    proj_sum = gathered[:, :, :proj_rows].reshape(members * proj_rows, channels)
    kernel_sum = (
        gathered[:, :, proj_rows:].astype(jnp.float32).reshape(members * kernel_rows, channels)[:KW]
    )
    own_grads = give_back(near, narrow, grad_shift)
    grad_key = own_grads[0].astype(jnp.bfloat16)
    grad_value = own_grads[1].astype(jnp.bfloat16)
    return (
        grad_query[None],
        grad_key[None],
        grad_value[None],
        proj_sum,
        kernel_sum,
    )


def solution(mesh):
    return jax.shard_map(
        on_device,
        mesh=mesh,
        in_specs=(
            P(("group", "dp"), "ctx", None),
            P(("group", "dp"), "ctx", None),
            P(("group", "dp"), "ctx", None),
            P(("group", "dp"), "ctx", None),
            P(),
            P(),
            P(("group", "dp")),
        ),
        out_specs=(
            P(("group", "dp"), "ctx", None),
            P(("group", "dp"), "ctx", None),
            P(("group", "dp"), "ctx", None),
            P("group", None),
            P("group", None),
        ),
        check_vma=False,
    )
```

```python
import math

import jax
import jax.numpy as jnp
from jax import lax
from jax.sharding import PartitionSpec as P

HEADS = 8
HDIM = 64
KW = 31
REACH = 3


def passed_along(block, axis, distance):
    devices = range(lax.axis_size(axis))
    route = [(i - distance, i) for i in devices if i - distance in devices]
    return lax.ppermute(block, axis, route)


def padded(cells, sides, width):
    for axis, dim in sides:
        count = lax.axis_size(axis)
        ends = count - 1
        head = lax.slice_in_dim(cells, 0, width, axis=dim)
        tail = lax.slice_in_dim(cells, cells.shape[dim] - width, cells.shape[dim], axis=dim)
        cells = jnp.concatenate(
            [
                lax.ppermute(tail, axis, [(i, (i + 1) % count) for i in range(ends)]),
                cells,
                lax.ppermute(head, axis, [((i + 1) % count, i) for i in range(ends)]),
            ],
            axis=dim,
        )
    return cells


def collect(piece_own, shifter, up_extra, down_extra):
    rows = piece_own.shape[0] * piece_own.shape[1]
    flat = piece_own.reshape(rows, piece_own.shape[2])
    got_below = shifter(jnp.concatenate([flat, up_extra], axis=0), 1)
    got_above = shifter(jnp.concatenate([flat, down_extra], axis=0), -1)
    below_one = got_below[:rows].reshape(piece_own.shape)
    above_one = got_above[:rows].reshape(piece_own.shape)
    below = shifter(jnp.stack([below_one, piece_own], axis=0), 2)
    above = shifter(jnp.stack([piece_own, above_one], axis=0), -2)
    window = jnp.stack(
        [below[0], below[1], below_one, piece_own, above_one, above[0], above[1]], axis=0
    )
    return window, got_below[rows:], got_above[rows:]


def give_back(near, narrow, shifter):
    from_below = shifter(narrow[REACH + 2 :], 2).astype(jnp.float32)
    from_above = shifter(narrow[REACH - 2 :: -1], -2).astype(jnp.float32)
    upward = (near[2] + from_below[1]).astype(jnp.bfloat16)
    downward = (near[0] + from_above[1]).astype(jnp.bfloat16)
    return (
        near[1]
        + from_below[0]
        + from_above[0]
        + shifter(upward, 1).astype(jnp.float32)
        + shifter(downward, -1).astype(jnp.float32)
    )


def exchange(block, axis, bit):
    count = lax.axis_size(axis)
    return lax.ppermute(block, axis, [(i, i ^ bit) for i in range(count)])


def halving(acc, axis):
    here = lax.axis_index(axis)
    count = lax.axis_size(axis)
    levels = count.bit_length() - 1
    for level in range(levels):
        half = acc.shape[0] // 2
        mine = (here >> level) % 2
        keep = lax.dynamic_slice_in_dim(acc, mine * half, half, 0)
        send = lax.dynamic_slice_in_dim(acc, (1 - mine) * half, half, 0)
        acc = keep + exchange(send.astype(jnp.bfloat16), axis, 1 << level).astype(jnp.float32)
    return acc[0]


def doubling(acc, axis):
    here = lax.axis_index(axis)
    count = lax.axis_size(axis)
    levels = count.bit_length() - 1
    acc = acc[None]
    for level in range(levels - 1, -1, -1):
        theirs = exchange(acc, axis, 1 << level)
        first = (here >> level) % 2 == 0
        acc = jnp.concatenate(
            [jnp.where(first, acc, theirs), jnp.where(first, theirs, acc)], axis=0
        )
    return acc


def on_device(queries, key_rows, values, cotangent, out_proj, conv_kernel, lengths):
    tokens = queries.shape[1]
    width_heads = queries.shape[2]
    channels = out_proj.shape[1]
    span_blocks = 2 * REACH + 1
    scale_factor = 1.0 / math.sqrt(HDIM)
    halo_width = (KW - 1) // 2
    block_index = lax.axis_index("ctx")
    length_here = lengths[0]
    query_here = queries[0]
    key_here = key_rows[0]
    value_here = values[0]
    cot_here = cotangent[0]
    frames = block_index * tokens + jnp.arange(tokens, dtype=jnp.int32)
    valid_rows = frames < length_here
    key_frames = (block_index - REACH) * tokens + jnp.arange(span_blocks * tokens, dtype=jnp.int32)
    valid_keys = (key_frames >= 0) & (key_frames < length_here)

    def kv_shift(piece_rows, offset_by):
        return passed_along(piece_rows, "ctx", offset_by)

    halo_rows = -(-halo_width // 8) * 8

    def edge_rows(rows_here):
        padded_rows = jnp.pad(rows_here, ((0, halo_rows - halo_width), (0, 0)))
        return padded_rows.reshape(-1, width_heads)

    def edge_back(packed):
        return packed.reshape(halo_rows, channels)[:halo_width]

    gathered, cot_low, cot_high = collect(
        jnp.stack([key_here, value_here], axis=0),
        kv_shift,
        edge_rows(cot_here[tokens - halo_width :]),
        edge_rows(cot_here[:halo_width]),
    )
    cot_wide = jnp.concatenate([edge_back(cot_low), cot_here, edge_back(cot_high)], axis=0)
    kv_rows = span_blocks * tokens
    key_all = gathered[:, 0].reshape(kv_rows, width_heads)
    value_all = gathered[:, 1].reshape(kv_rows, width_heads)
    head_mask = (
        jnp.arange(HEADS, dtype=jnp.int32)[:, None, None]
        == (jnp.arange(width_heads, dtype=jnp.int32) // HDIM)[None, None, :]
    )

    def spread(rows):
        return jnp.where(head_mask, rows[None], jnp.zeros((), rows.dtype)).reshape(
            HEADS * tokens, width_heads
        )

    def own_heads(stacked_rows):
        picked = jnp.where(head_mask, stacked_rows.reshape(HEADS, tokens, width_heads), 0.0)
        return jnp.sum(picked, axis=0)

    def contract(lhs, rhs, lhs_dim, rhs_dim):
        return lax.dot_general(
            lhs, rhs, (((lhs_dim,), (rhs_dim,)), ((), ())), preferred_element_type=jnp.float32
        )

    query_spread = spread(query_here)
    scores = contract(query_spread, key_all, 1, 1) * scale_factor
    scores = jnp.where(valid_keys[None, :], scores, -jnp.inf)
    row_max = jnp.max(scores, axis=1, keepdims=True)
    row_total = jnp.sum(jnp.exp(scores - row_max), axis=1, keepdims=True)
    log_total = row_max + jnp.log(row_total)
    weights = jnp.exp(scores - log_total).astype(jnp.bfloat16)
    attended = own_heads(contract(weights, value_all, 1, 0)).astype(jnp.bfloat16)
    hidden = jnp.dot(attended, out_proj, preferred_element_type=jnp.float32)
    masked = jnp.where(valid_rows[:, None], hidden, 0.0).astype(jnp.bfloat16)

    wide_rows = tokens + 2 * halo_width
    padded_m = padded(masked, (("ctx", 0),), 2 * halo_width)
    conv_out = jnp.zeros((wide_rows, channels), jnp.float32)
    for tap_index in range(KW):
        conv_out = conv_out + conv_kernel[tap_index] * padded_m[tap_index : tap_index + wide_rows]
    sigmoid_c = jax.nn.sigmoid(conv_out)
    grad_conv = (
        cot_wide.astype(jnp.float32) * (sigmoid_c + conv_out * sigmoid_c * (1.0 - sigmoid_c))
    ).astype(jnp.bfloat16)
    grad_masked = jnp.zeros((tokens, channels), jnp.float32)
    for tap_index in range(KW):
        start_row = 2 * halo_width - tap_index
        grad_masked = (
            grad_masked + conv_kernel[tap_index] * grad_conv[start_row : start_row + tokens]
        )
    kernel_local = lax.conv_general_dilated(
        padded_m[None, halo_width : halo_width + wide_rows],
        grad_conv[halo_width : halo_width + tokens, None, :],
        window_strides=(1,),
        padding="VALID",
        dimension_numbers=("NWC", "WIO", "NWC"),
        feature_group_count=channels,
        preferred_element_type=jnp.float32,
    )[0]
    grad_hidden = (
        cot_here.astype(jnp.float32) + jnp.where(valid_rows[:, None], grad_masked, 0.0)
    ).astype(jnp.bfloat16)
    proj_local = lax.dot_general(
        attended, grad_hidden, (((0,), (0,)), ((), ())), preferred_element_type=jnp.float32
    )
    ctx_count = lax.axis_size("ctx")
    dp_count = lax.axis_size("dp")
    members = ctx_count * dp_count
    proj_rows = proj_local.shape[0] // members
    kernel_rows = -(-KW // members)
    kernel_padded = jnp.pad(kernel_local, ((0, kernel_rows * members - KW), (0, 0)))
    stacked = jnp.concatenate(
        [
            proj_local.reshape(dp_count, ctx_count, proj_rows, channels),
            kernel_padded.reshape(dp_count, ctx_count, kernel_rows, channels),
        ],
        axis=2,
    )
    summed = halving(halving(stacked, "dp"), "ctx").astype(jnp.bfloat16)
    grad_attended = lax.dot_general(
        grad_hidden, out_proj, (((1,), (1,)), ((), ())), preferred_element_type=jnp.float32
    ).astype(jnp.bfloat16)
    delta_rows = jnp.sum(
        (grad_attended.astype(jnp.float32) * attended.astype(jnp.float32)).reshape(
            tokens, HEADS, HDIM
        ),
        axis=2,
    )
    grad_spread = spread(grad_attended)
    grad_weights = contract(grad_spread, value_all, 1, 1)
    grad_logits = (
        weights.astype(jnp.float32) * (grad_weights - delta_rows.T.reshape(HEADS * tokens, 1))
    ).astype(jnp.bfloat16)
    grad_query = (own_heads(contract(grad_logits, key_all, 1, 0)) * scale_factor).astype(
        jnp.bfloat16
    )
    grad_key_all = contract(grad_logits, query_spread, 0, 0) * scale_factor
    grad_value_all = contract(weights, grad_spread, 0, 0)
    key_blocks = grad_key_all.reshape(span_blocks, tokens, width_heads)
    value_blocks = grad_value_all.reshape(span_blocks, tokens, width_heads)
    narrow = jnp.stack([key_blocks, value_blocks], axis=1).astype(jnp.bfloat16)
    near = jnp.stack(
        [key_blocks[REACH - 1 : REACH + 2], value_blocks[REACH - 1 : REACH + 2]], axis=1
    )

    def grad_shift(piece_rows, offset_by):
        return passed_along(piece_rows, "ctx", offset_by)

    gathered = doubling(doubling(summed, "ctx"), "dp")
    proj_sum = gathered[:, :, :proj_rows].reshape(members * proj_rows, channels)
    kernel_sum = (
        gathered[:, :, proj_rows:].astype(jnp.float32).reshape(members * kernel_rows, channels)[:KW]
    )
    own_grads = give_back(near, narrow, grad_shift)
    grad_key = own_grads[0].astype(jnp.bfloat16)
    grad_value = own_grads[1].astype(jnp.bfloat16)
    return (
        grad_query[None],
        grad_key[None],
        grad_value[None],
        proj_sum,
        kernel_sum,
    )


def solution(mesh):
    return jax.shard_map(
        on_device,
        mesh=mesh,
        in_specs=(
            P(("group", "dp"), "ctx", None),
            P(("group", "dp"), "ctx", None),
            P(("group", "dp"), "ctx", None),
            P(("group", "dp"), "ctx", None),
            P(),
            P(),
            P(("group", "dp")),
        ),
        out_specs=(
            P(("group", "dp"), "ctx", None),
            P(("group", "dp"), "ctx", None),
            P(("group", "dp"), "ctx", None),
            P("group", None),
            P("group", None),
        ),
        check_vma=False,
    )
```

```python
import math

import jax
import jax.numpy as jnp
from jax import lax
from jax.sharding import PartitionSpec as P

HEADS = 8
HDIM = 64
KW = 31
REACH = 3


def passed_along(block, axis, distance):
    devices = range(lax.axis_size(axis))
    route = [(i - distance, i) for i in devices if i - distance in devices]
    return lax.ppermute(block, axis, route)


def padded(cells, sides, width):
    for axis, dim in sides:
        count = lax.axis_size(axis)
        ends = count - 1
        head = lax.slice_in_dim(cells, 0, width, axis=dim)
        tail = lax.slice_in_dim(cells, cells.shape[dim] - width, cells.shape[dim], axis=dim)
        cells = jnp.concatenate(
            [
                lax.ppermute(tail, axis, [(i, (i + 1) % count) for i in range(ends)]),
                cells,
                lax.ppermute(head, axis, [((i + 1) % count, i) for i in range(ends)]),
            ],
            axis=dim,
        )
    return cells


def collect(piece_own, shifter, up_extra, down_extra):
    rows = piece_own.shape[0] * piece_own.shape[1]
    flat = piece_own.reshape(rows, piece_own.shape[2])
    got_below = shifter(jnp.concatenate([flat, up_extra], axis=0), 1)
    got_above = shifter(jnp.concatenate([flat, down_extra], axis=0), -1)
    below_one = got_below[:rows].reshape(piece_own.shape)
    above_one = got_above[:rows].reshape(piece_own.shape)
    below = shifter(jnp.stack([below_one, piece_own], axis=0), 2)
    above = shifter(jnp.stack([piece_own, above_one], axis=0), -2)
    window = jnp.stack(
        [below[0], below[1], below_one, piece_own, above_one, above[0], above[1]], axis=0
    )
    return window, got_below[rows:], got_above[rows:]


def give_back(near, narrow, shifter):
    from_below = shifter(narrow[REACH + 2 :], 2).astype(jnp.float32)
    from_above = shifter(narrow[REACH - 2 :: -1], -2).astype(jnp.float32)
    upward = (near[2] + from_below[1]).astype(jnp.bfloat16)
    downward = (near[0] + from_above[1]).astype(jnp.bfloat16)
    return (
        near[1]
        + from_below[0]
        + from_above[0]
        + shifter(upward, 1).astype(jnp.float32)
        + shifter(downward, -1).astype(jnp.float32)
    )


def exchange(block, axis, bit):
    count = lax.axis_size(axis)
    return lax.ppermute(block, axis, [(i, i ^ bit) for i in range(count)])


def halving(acc, axis, first=0, last=None):
    here = lax.axis_index(axis)
    count = lax.axis_size(axis)
    levels = count.bit_length() - 1
    for level in range(first, levels if last is None else min(last, levels)):
        half = acc.shape[0] // 2
        mine = (here >> level) % 2
        keep = lax.dynamic_slice_in_dim(acc, mine * half, half, 0)
        send = lax.dynamic_slice_in_dim(acc, (1 - mine) * half, half, 0)
        acc = keep + exchange(send.astype(jnp.bfloat16), axis, 1 << level).astype(jnp.float32)
    return acc[0] if acc.shape[0] == 1 else acc


def doubling(acc, axis):
    here = lax.axis_index(axis)
    count = lax.axis_size(axis)
    levels = count.bit_length() - 1
    acc = acc[None]
    for level in range(levels - 1, -1, -1):
        theirs = exchange(acc, axis, 1 << level)
        first = (here >> level) % 2 == 0
        acc = jnp.concatenate(
            [jnp.where(first, acc, theirs), jnp.where(first, theirs, acc)], axis=0
        )
    return acc


def on_device(queries, key_rows, values, cotangent, out_proj, conv_kernel, lengths):
    tokens = queries.shape[1]
    width_heads = queries.shape[2]
    channels = out_proj.shape[1]
    span_blocks = 2 * REACH + 1
    scale_factor = 1.0 / math.sqrt(HDIM)
    halo_width = (KW - 1) // 2
    block_index = lax.axis_index("ctx")
    length_here = lengths[0]
    query_here = queries[0]
    key_here = key_rows[0]
    value_here = values[0]
    cot_here = cotangent[0]
    frames = block_index * tokens + jnp.arange(tokens, dtype=jnp.int32)
    valid_rows = frames < length_here
    key_frames = (block_index - REACH) * tokens + jnp.arange(span_blocks * tokens, dtype=jnp.int32)
    valid_keys = (key_frames >= 0) & (key_frames < length_here)

    def kv_shift(piece_rows, offset_by):
        return passed_along(piece_rows, "ctx", offset_by)

    halo_rows = -(-halo_width // 8) * 8

    def edge_rows(rows_here):
        padded_rows = jnp.pad(rows_here, ((0, halo_rows - halo_width), (0, 0)))
        return padded_rows.reshape(-1, width_heads)

    def edge_back(packed):
        return packed.reshape(halo_rows, channels)[:halo_width]

    gathered, cot_low, cot_high = collect(
        jnp.stack([key_here, value_here], axis=0),
        kv_shift,
        edge_rows(cot_here[tokens - halo_width :]),
        edge_rows(cot_here[:halo_width]),
    )
    cot_wide = jnp.concatenate([edge_back(cot_low), cot_here, edge_back(cot_high)], axis=0)
    kv_rows = span_blocks * tokens
    key_all = gathered[:, 0].reshape(kv_rows, width_heads)
    value_all = gathered[:, 1].reshape(kv_rows, width_heads)
    head_mask = (
        jnp.arange(HEADS, dtype=jnp.int32)[:, None, None]
        == (jnp.arange(width_heads, dtype=jnp.int32) // HDIM)[None, None, :]
    )

    def spread(rows):
        return jnp.where(head_mask, rows[None], jnp.zeros((), rows.dtype)).reshape(
            HEADS * tokens, width_heads
        )

    def own_heads(stacked_rows):
        picked = jnp.where(head_mask, stacked_rows.reshape(HEADS, tokens, width_heads), 0.0)
        return jnp.sum(picked, axis=0)

    def contract(lhs, rhs, lhs_dim, rhs_dim):
        return lax.dot_general(
            lhs, rhs, (((lhs_dim,), (rhs_dim,)), ((), ())), preferred_element_type=jnp.float32
        )

    query_spread = spread(query_here)
    scores = contract(query_spread, key_all, 1, 1) * scale_factor
    scores = jnp.where(valid_keys[None, :], scores, -jnp.inf)
    row_max = jnp.max(scores, axis=1, keepdims=True)
    row_total = jnp.sum(jnp.exp(scores - row_max), axis=1, keepdims=True)
    log_total = row_max + jnp.log(row_total)
    weights = jnp.exp(scores - log_total).astype(jnp.bfloat16)
    attended = own_heads(contract(weights, value_all, 1, 0)).astype(jnp.bfloat16)
    hidden = jnp.dot(attended, out_proj, preferred_element_type=jnp.float32)
    masked = jnp.where(valid_rows[:, None], hidden, 0.0).astype(jnp.bfloat16)

    wide_rows = tokens + 2 * halo_width
    padded_m = padded(masked, (("ctx", 0),), 2 * halo_width)
    conv_out = jnp.zeros((wide_rows, channels), jnp.float32)
    for tap_index in range(KW):
        conv_out = conv_out + conv_kernel[tap_index] * padded_m[tap_index : tap_index + wide_rows]
    sigmoid_c = jax.nn.sigmoid(conv_out)
    grad_conv = (
        cot_wide.astype(jnp.float32) * (sigmoid_c + conv_out * sigmoid_c * (1.0 - sigmoid_c))
    ).astype(jnp.bfloat16)
    grad_masked = jnp.zeros((tokens, channels), jnp.float32)
    for tap_index in range(KW):
        start_row = 2 * halo_width - tap_index
        grad_masked = (
            grad_masked + conv_kernel[tap_index] * grad_conv[start_row : start_row + tokens]
        )
    kernel_local = lax.conv_general_dilated(
        padded_m[None, halo_width : halo_width + wide_rows],
        grad_conv[halo_width : halo_width + tokens, None, :],
        window_strides=(1,),
        padding="VALID",
        dimension_numbers=("NWC", "WIO", "NWC"),
        feature_group_count=channels,
        preferred_element_type=jnp.float32,
    )[0]
    grad_hidden = (
        cot_here.astype(jnp.float32) + jnp.where(valid_rows[:, None], grad_masked, 0.0)
    ).astype(jnp.bfloat16)
    proj_local = lax.dot_general(
        attended, grad_hidden, (((0,), (0,)), ((), ())), preferred_element_type=jnp.float32
    )
    ctx_count = lax.axis_size("ctx")
    dp_count = lax.axis_size("dp")
    members = ctx_count * dp_count
    proj_rows = proj_local.shape[0] // members
    kernel_rows = -(-KW // members)
    kernel_padded = jnp.pad(kernel_local, ((0, kernel_rows * members - KW), (0, 0)))
    stacked = jnp.concatenate(
        [
            proj_local.reshape(dp_count, ctx_count, proj_rows, channels),
            kernel_padded.reshape(dp_count, ctx_count, kernel_rows, channels),
        ],
        axis=2,
    )
    partly = halving(halving(stacked, "dp"), "ctx", 0, 1)
    grad_attended = lax.dot_general(
        grad_hidden, out_proj, (((1,), (1,)), ((), ())), preferred_element_type=jnp.float32
    ).astype(jnp.bfloat16)
    delta_rows = jnp.sum(
        (grad_attended.astype(jnp.float32) * attended.astype(jnp.float32)).reshape(
            tokens, HEADS, HDIM
        ),
        axis=2,
    )
    grad_spread = spread(grad_attended)
    grad_weights = contract(grad_spread, value_all, 1, 1)
    grad_logits = (
        weights.astype(jnp.float32) * (grad_weights - delta_rows.T.reshape(HEADS * tokens, 1))
    ).astype(jnp.bfloat16)
    grad_query = (own_heads(contract(grad_logits, key_all, 1, 0)) * scale_factor).astype(
        jnp.bfloat16
    )
    grad_key_all = contract(grad_logits, query_spread, 0, 0) * scale_factor
    grad_value_all = contract(weights, grad_spread, 0, 0)
    key_blocks = grad_key_all.reshape(span_blocks, tokens, width_heads)
    value_blocks = grad_value_all.reshape(span_blocks, tokens, width_heads)
    narrow = jnp.stack([key_blocks, value_blocks], axis=1).astype(jnp.bfloat16)
    near = jnp.stack(
        [key_blocks[REACH - 1 : REACH + 2], value_blocks[REACH - 1 : REACH + 2]], axis=1
    )
    partly, narrow = lax.optimization_barrier((partly, narrow))
    summed = halving(partly, "ctx", 1).astype(jnp.bfloat16)

    def grad_shift(piece_rows, offset_by):
        return passed_along(piece_rows, "ctx", offset_by)

    gathered = doubling(doubling(summed, "ctx"), "dp")
    proj_sum = gathered[:, :, :proj_rows].reshape(members * proj_rows, channels)
    kernel_sum = (
        gathered[:, :, proj_rows:].astype(jnp.float32).reshape(members * kernel_rows, channels)[:KW]
    )
    own_grads = give_back(near, narrow, grad_shift)
    grad_key = own_grads[0].astype(jnp.bfloat16)
    grad_value = own_grads[1].astype(jnp.bfloat16)
    return (
        grad_query[None],
        grad_key[None],
        grad_value[None],
        proj_sum,
        kernel_sum,
    )


def solution(mesh):
    return jax.shard_map(
        on_device,
        mesh=mesh,
        in_specs=(
            P(("group", "dp"), "ctx", None),
            P(("group", "dp"), "ctx", None),
            P(("group", "dp"), "ctx", None),
            P(("group", "dp"), "ctx", None),
            P(),
            P(),
            P(("group", "dp")),
        ),
        out_specs=(
            P(("group", "dp"), "ctx", None),
            P(("group", "dp"), "ctx", None),
            P(("group", "dp"), "ctx", None),
            P("group", None),
            P("group", None),
        ),
        check_vma=False,
    )
```

```python
import math

import jax
import jax.numpy as jnp
from jax import lax
from jax.sharding import PartitionSpec as P

HEADS = 8
HDIM = 64
KW = 31
REACH = 3


def passed_along(block, axis, distance):
    devices = range(lax.axis_size(axis))
    route = [(i - distance, i) for i in devices if i - distance in devices]
    return lax.ppermute(block, axis, route)


def padded(cells, sides, width):
    for axis, dim in sides:
        count = lax.axis_size(axis)
        ends = count - 1
        head = lax.slice_in_dim(cells, 0, width, axis=dim)
        tail = lax.slice_in_dim(cells, cells.shape[dim] - width, cells.shape[dim], axis=dim)
        cells = jnp.concatenate(
            [
                lax.ppermute(tail, axis, [(i, (i + 1) % count) for i in range(ends)]),
                cells,
                lax.ppermute(head, axis, [((i + 1) % count, i) for i in range(ends)]),
            ],
            axis=dim,
        )
    return cells


def collect(piece_own, shifter, up_extra, down_extra):
    rows = piece_own.shape[0] * piece_own.shape[1]
    flat = piece_own.reshape(rows, piece_own.shape[2])
    got_below = shifter(jnp.concatenate([flat, up_extra], axis=0), 1)
    got_above = shifter(jnp.concatenate([flat, down_extra], axis=0), -1)
    below_one = got_below[:rows].reshape(piece_own.shape)
    above_one = got_above[:rows].reshape(piece_own.shape)
    below = shifter(jnp.stack([below_one, piece_own], axis=0), 2)
    above = shifter(jnp.stack([piece_own, above_one], axis=0), -2)
    window = jnp.stack(
        [below[0], below[1], below_one, piece_own, above_one, above[0], above[1]], axis=0
    )
    return window, got_below[rows:], got_above[rows:]


def give_back(near, narrow, shifter):
    total = near[1]
    for offset in range(2 * REACH + 1):
        if offset != REACH:
            total = total + shifter(narrow[offset], offset - REACH).astype(jnp.float32)
    return total


def exchange(block, axis, bit):
    count = lax.axis_size(axis)
    return lax.ppermute(block, axis, [(i, i ^ bit) for i in range(count)])


def halving(acc, axis):
    here = lax.axis_index(axis)
    count = lax.axis_size(axis)
    levels = count.bit_length() - 1
    for level in range(levels):
        half = acc.shape[0] // 2
        mine = (here >> level) % 2
        keep = lax.dynamic_slice_in_dim(acc, mine * half, half, 0)
        send = lax.dynamic_slice_in_dim(acc, (1 - mine) * half, half, 0)
        acc = keep + exchange(send.astype(jnp.bfloat16), axis, 1 << level).astype(jnp.float32)
    return acc[0]


def doubling(acc, axis):
    here = lax.axis_index(axis)
    count = lax.axis_size(axis)
    levels = count.bit_length() - 1
    acc = acc[None]
    for level in range(levels - 1, -1, -1):
        theirs = exchange(acc, axis, 1 << level)
        first = (here >> level) % 2 == 0
        acc = jnp.concatenate(
            [jnp.where(first, acc, theirs), jnp.where(first, theirs, acc)], axis=0
        )
    return acc


def on_device(queries, key_rows, values, cotangent, out_proj, conv_kernel, lengths):
    tokens = queries.shape[1]
    width_heads = queries.shape[2]
    channels = out_proj.shape[1]
    span_blocks = 2 * REACH + 1
    scale_factor = 1.0 / math.sqrt(HDIM)
    halo_width = (KW - 1) // 2
    block_index = lax.axis_index("ctx")
    length_here = lengths[0]
    query_here = queries[0]
    key_here = key_rows[0]
    value_here = values[0]
    cot_here = cotangent[0]
    frames = block_index * tokens + jnp.arange(tokens, dtype=jnp.int32)
    valid_rows = frames < length_here
    key_frames = (block_index - REACH) * tokens + jnp.arange(span_blocks * tokens, dtype=jnp.int32)
    valid_keys = (key_frames >= 0) & (key_frames < length_here)

    def kv_shift(piece_rows, offset_by):
        return passed_along(piece_rows, "ctx", offset_by)

    halo_rows = -(-halo_width // 8) * 8

    def edge_rows(rows_here):
        padded_rows = jnp.pad(rows_here, ((0, halo_rows - halo_width), (0, 0)))
        return padded_rows.reshape(-1, width_heads)

    def edge_back(packed):
        return packed.reshape(halo_rows, channels)[:halo_width]

    gathered, cot_low, cot_high = collect(
        jnp.stack([key_here, value_here], axis=0),
        kv_shift,
        edge_rows(cot_here[tokens - halo_width :]),
        edge_rows(cot_here[:halo_width]),
    )
    cot_wide = jnp.concatenate([edge_back(cot_low), cot_here, edge_back(cot_high)], axis=0)
    kv_rows = span_blocks * tokens
    key_all = gathered[:, 0].reshape(kv_rows, width_heads)
    value_all = gathered[:, 1].reshape(kv_rows, width_heads)
    head_mask = (
        jnp.arange(HEADS, dtype=jnp.int32)[:, None, None]
        == (jnp.arange(width_heads, dtype=jnp.int32) // HDIM)[None, None, :]
    )

    def spread(rows):
        return jnp.where(head_mask, rows[None], jnp.zeros((), rows.dtype)).reshape(
            HEADS * tokens, width_heads
        )

    def own_heads(stacked_rows):
        picked = jnp.where(head_mask, stacked_rows.reshape(HEADS, tokens, width_heads), 0.0)
        return jnp.sum(picked, axis=0)

    def contract(lhs, rhs, lhs_dim, rhs_dim):
        return lax.dot_general(
            lhs, rhs, (((lhs_dim,), (rhs_dim,)), ((), ())), preferred_element_type=jnp.float32
        )

    query_spread = spread(query_here)
    scores = contract(query_spread, key_all, 1, 1) * scale_factor
    scores = jnp.where(valid_keys[None, :], scores, -jnp.inf)
    row_max = jnp.max(scores, axis=1, keepdims=True)
    row_total = jnp.sum(jnp.exp(scores - row_max), axis=1, keepdims=True)
    log_total = row_max + jnp.log(row_total)
    weights = jnp.exp(scores - log_total).astype(jnp.bfloat16)
    attended = own_heads(contract(weights, value_all, 1, 0)).astype(jnp.bfloat16)
    hidden = jnp.dot(attended, out_proj, preferred_element_type=jnp.float32)
    masked = jnp.where(valid_rows[:, None], hidden, 0.0).astype(jnp.bfloat16)

    wide_rows = tokens + 2 * halo_width
    padded_m = padded(masked, (("ctx", 0),), 2 * halo_width)
    conv_out = jnp.zeros((wide_rows, channels), jnp.float32)
    for tap_index in range(KW):
        conv_out = conv_out + conv_kernel[tap_index] * padded_m[tap_index : tap_index + wide_rows]
    sigmoid_c = jax.nn.sigmoid(conv_out)
    grad_conv = (
        cot_wide.astype(jnp.float32) * (sigmoid_c + conv_out * sigmoid_c * (1.0 - sigmoid_c))
    ).astype(jnp.bfloat16)
    grad_masked = jnp.zeros((tokens, channels), jnp.float32)
    for tap_index in range(KW):
        start_row = 2 * halo_width - tap_index
        grad_masked = (
            grad_masked + conv_kernel[tap_index] * grad_conv[start_row : start_row + tokens]
        )
    kernel_local = lax.conv_general_dilated(
        padded_m[None, halo_width : halo_width + wide_rows],
        grad_conv[halo_width : halo_width + tokens, None, :],
        window_strides=(1,),
        padding="VALID",
        dimension_numbers=("NWC", "WIO", "NWC"),
        feature_group_count=channels,
        preferred_element_type=jnp.float32,
    )[0]
    grad_hidden = (
        cot_here.astype(jnp.float32) + jnp.where(valid_rows[:, None], grad_masked, 0.0)
    ).astype(jnp.bfloat16)
    proj_local = lax.dot_general(
        attended, grad_hidden, (((0,), (0,)), ((), ())), preferred_element_type=jnp.float32
    )
    ctx_count = lax.axis_size("ctx")
    dp_count = lax.axis_size("dp")
    members = ctx_count * dp_count
    proj_rows = proj_local.shape[0] // members
    kernel_rows = -(-KW // members)
    kernel_padded = jnp.pad(kernel_local, ((0, kernel_rows * members - KW), (0, 0)))
    stacked = jnp.concatenate(
        [
            proj_local.reshape(dp_count, ctx_count, proj_rows, channels),
            kernel_padded.reshape(dp_count, ctx_count, kernel_rows, channels),
        ],
        axis=2,
    )
    summed = halving(halving(stacked, "dp"), "ctx").astype(jnp.bfloat16)
    grad_attended = lax.dot_general(
        grad_hidden, out_proj, (((1,), (1,)), ((), ())), preferred_element_type=jnp.float32
    ).astype(jnp.bfloat16)
    delta_rows = jnp.sum(
        (grad_attended.astype(jnp.float32) * attended.astype(jnp.float32)).reshape(
            tokens, HEADS, HDIM
        ),
        axis=2,
    )
    grad_spread = spread(grad_attended)
    grad_weights = contract(grad_spread, value_all, 1, 1)
    grad_logits = (
        weights.astype(jnp.float32) * (grad_weights - delta_rows.T.reshape(HEADS * tokens, 1))
    ).astype(jnp.bfloat16)
    grad_query = (own_heads(contract(grad_logits, key_all, 1, 0)) * scale_factor).astype(
        jnp.bfloat16
    )
    grad_key_all = contract(grad_logits, query_spread, 0, 0) * scale_factor
    grad_value_all = contract(weights, grad_spread, 0, 0)
    key_blocks = grad_key_all.reshape(span_blocks, tokens, width_heads)
    value_blocks = grad_value_all.reshape(span_blocks, tokens, width_heads)
    narrow = jnp.stack([key_blocks, value_blocks], axis=1).astype(jnp.bfloat16)
    near = jnp.stack(
        [key_blocks[REACH - 1 : REACH + 2], value_blocks[REACH - 1 : REACH + 2]], axis=1
    )

    def grad_shift(piece_rows, offset_by):
        return passed_along(piece_rows, "ctx", offset_by)

    gathered = doubling(doubling(summed, "ctx"), "dp")
    proj_sum = gathered[:, :, :proj_rows].reshape(members * proj_rows, channels)
    kernel_sum = (
        gathered[:, :, proj_rows:].astype(jnp.float32).reshape(members * kernel_rows, channels)[:KW]
    )
    own_grads = give_back(near, narrow, grad_shift)
    grad_key = own_grads[0].astype(jnp.bfloat16)
    grad_value = own_grads[1].astype(jnp.bfloat16)
    return (
        grad_query[None],
        grad_key[None],
        grad_value[None],
        proj_sum,
        kernel_sum,
    )


def solution(mesh):
    return jax.shard_map(
        on_device,
        mesh=mesh,
        in_specs=(
            P(("group", "dp"), "ctx", None),
            P(("group", "dp"), "ctx", None),
            P(("group", "dp"), "ctx", None),
            P(("group", "dp"), "ctx", None),
            P(),
            P(),
            P(("group", "dp")),
        ),
        out_specs=(
            P(("group", "dp"), "ctx", None),
            P(("group", "dp"), "ctx", None),
            P(("group", "dp"), "ctx", None),
            P("group", None),
            P("group", None),
        ),
        check_vma=False,
    )
```

```python
import math

import jax
import jax.numpy as jnp
from jax import lax
from jax.sharding import PartitionSpec as P

HEADS = 8
HDIM = 64
KW = 31
REACH = 3


def passed_along(block, axis, distance):
    devices = range(lax.axis_size(axis))
    route = [(i - distance, i) for i in devices if i - distance in devices]
    return lax.ppermute(block, axis, route)


def padded(cells, sides, width):
    for axis, dim in sides:
        count = lax.axis_size(axis)
        ends = count - 1
        head = lax.slice_in_dim(cells, 0, width, axis=dim)
        tail = lax.slice_in_dim(cells, cells.shape[dim] - width, cells.shape[dim], axis=dim)
        cells = jnp.concatenate(
            [
                lax.ppermute(tail, axis, [(i, (i + 1) % count) for i in range(ends)]),
                cells,
                lax.ppermute(head, axis, [((i + 1) % count, i) for i in range(ends)]),
            ],
            axis=dim,
        )
    return cells


def collect(piece_own, shifter, up_extra, down_extra):
    rows = piece_own.shape[0] * piece_own.shape[1]
    flat = piece_own.reshape(rows, piece_own.shape[2])
    got_below = shifter(jnp.concatenate([flat, up_extra], axis=0), 1)
    got_above = shifter(jnp.concatenate([flat, down_extra], axis=0), -1)
    below_one = got_below[:rows].reshape(piece_own.shape)
    above_one = got_above[:rows].reshape(piece_own.shape)
    below = shifter(jnp.stack([below_one, piece_own], axis=0), 2)
    above = shifter(jnp.stack([piece_own, above_one], axis=0), -2)
    window = jnp.stack(
        [below[0], below[1], below_one, piece_own, above_one, above[0], above[1]], axis=0
    )
    return window, got_below[rows:], got_above[rows:]


def give_back(near, narrow, shifter):
    from_below = shifter(narrow[REACH + 2 :], 2).astype(jnp.float32)
    from_above = shifter(narrow[: REACH - 1], -2).astype(jnp.float32)
    upward = (near[2] + from_below[1]).astype(jnp.bfloat16)
    downward = (near[0] + from_above[0]).astype(jnp.bfloat16)
    return (
        near[1]
        + from_below[0]
        + from_above[1]
        + shifter(upward, 1).astype(jnp.float32)
        + shifter(downward, -1).astype(jnp.float32)
    )


def exchange(block, axis, bit):
    count = lax.axis_size(axis)
    return lax.ppermute(block, axis, [(i, i ^ bit) for i in range(count)])


def halving(acc, axis):
    here = lax.axis_index(axis)
    count = lax.axis_size(axis)
    levels = count.bit_length() - 1
    for level in range(levels):
        half = acc.shape[0] // 2
        mine = (here >> level) % 2
        keep = lax.dynamic_slice_in_dim(acc, mine * half, half, 0)
        send = lax.dynamic_slice_in_dim(acc, (1 - mine) * half, half, 0)
        acc = keep + exchange(send.astype(jnp.bfloat16), axis, 1 << level).astype(jnp.float32)
    return acc[0]


def doubling(acc, axis):
    here = lax.axis_index(axis)
    count = lax.axis_size(axis)
    levels = count.bit_length() - 1
    acc = acc[None]
    for level in range(levels - 1, -1, -1):
        theirs = exchange(acc, axis, 1 << level)
        first = (here >> level) % 2 == 0
        acc = jnp.concatenate(
            [jnp.where(first, acc, theirs), jnp.where(first, theirs, acc)], axis=0
        )
    return acc


def on_device(queries, key_rows, values, cotangent, out_proj, conv_kernel, lengths):
    tokens = queries.shape[1]
    width_heads = queries.shape[2]
    channels = out_proj.shape[1]
    span_blocks = 2 * REACH + 1
    scale_factor = 1.0 / math.sqrt(HDIM)
    halo_width = (KW - 1) // 2
    block_index = lax.axis_index("ctx")
    length_here = lengths[0]
    query_here = queries[0]
    key_here = key_rows[0]
    value_here = values[0]
    cot_here = cotangent[0]
    frames = block_index * tokens + jnp.arange(tokens, dtype=jnp.int32)
    valid_rows = frames < length_here
    key_frames = (block_index - REACH) * tokens + jnp.arange(span_blocks * tokens, dtype=jnp.int32)
    valid_keys = (key_frames >= 0) & (key_frames < length_here)

    def kv_shift(piece_rows, offset_by):
        return passed_along(piece_rows, "ctx", offset_by)

    halo_rows = -(-halo_width // 8) * 8

    def edge_rows(rows_here):
        padded_rows = jnp.pad(rows_here, ((0, halo_rows - halo_width), (0, 0)))
        return padded_rows.reshape(-1, width_heads)

    def edge_back(packed):
        return packed.reshape(halo_rows, channels)[:halo_width]

    gathered, cot_low, cot_high = collect(
        jnp.stack([key_here, value_here], axis=0),
        kv_shift,
        edge_rows(cot_here[tokens - halo_width :]),
        edge_rows(cot_here[:halo_width]),
    )
    cot_wide = jnp.concatenate([edge_back(cot_low), cot_here, edge_back(cot_high)], axis=0)
    kv_rows = span_blocks * tokens
    key_all = gathered[:, 0].reshape(kv_rows, width_heads)
    value_all = gathered[:, 1].reshape(kv_rows, width_heads)
    head_mask = (
        jnp.arange(HEADS, dtype=jnp.int32)[:, None, None]
        == (jnp.arange(width_heads, dtype=jnp.int32) // HDIM)[None, None, :]
    )

    def spread(rows):
        return jnp.where(head_mask, rows[None], jnp.zeros((), rows.dtype)).reshape(
            HEADS * tokens, width_heads
        )

    def own_heads(stacked_rows):
        picked = jnp.where(head_mask, stacked_rows.reshape(HEADS, tokens, width_heads), 0.0)
        return jnp.sum(picked, axis=0)

    def contract(lhs, rhs, lhs_dim, rhs_dim):
        return lax.dot_general(
            lhs, rhs, (((lhs_dim,), (rhs_dim,)), ((), ())), preferred_element_type=jnp.float32
        )

    query_spread = spread(query_here)
    scores = contract(query_spread, key_all, 1, 1) * scale_factor
    scores = jnp.where(valid_keys[None, :], scores, -jnp.inf)
    row_max = jnp.max(scores, axis=1, keepdims=True)
    row_total = jnp.sum(jnp.exp(scores - row_max), axis=1, keepdims=True)
    log_total = row_max + jnp.log(row_total)
    weights = jnp.exp(scores - log_total).astype(jnp.bfloat16)
    attended = own_heads(contract(weights, value_all, 1, 0)).astype(jnp.bfloat16)
    hidden = jnp.dot(attended, out_proj, preferred_element_type=jnp.float32)
    masked = jnp.where(valid_rows[:, None], hidden, 0.0).astype(jnp.bfloat16)

    wide_rows = tokens + 2 * halo_width
    padded_m = padded(masked, (("ctx", 0),), 2 * halo_width)
    conv_out = jnp.zeros((wide_rows, channels), jnp.float32)
    for tap_index in range(KW):
        conv_out = conv_out + conv_kernel[tap_index] * padded_m[tap_index : tap_index + wide_rows]
    sigmoid_c = jax.nn.sigmoid(conv_out)
    grad_conv = (
        cot_wide.astype(jnp.float32) * (sigmoid_c + conv_out * sigmoid_c * (1.0 - sigmoid_c))
    ).astype(jnp.bfloat16)
    grad_masked = jnp.zeros((tokens, channels), jnp.float32)
    for tap_index in range(KW):
        start_row = 2 * halo_width - tap_index
        grad_masked = (
            grad_masked + conv_kernel[tap_index] * grad_conv[start_row : start_row + tokens]
        )
    kernel_local = lax.conv_general_dilated(
        padded_m[None, halo_width : halo_width + wide_rows],
        grad_conv[halo_width : halo_width + tokens, None, :],
        window_strides=(1,),
        padding="VALID",
        dimension_numbers=("NWC", "WIO", "NWC"),
        feature_group_count=channels,
        preferred_element_type=jnp.float32,
    )[0]
    grad_hidden = (
        cot_here.astype(jnp.float32) + jnp.where(valid_rows[:, None], grad_masked, 0.0)
    ).astype(jnp.bfloat16)
    proj_local = lax.dot_general(
        attended, grad_hidden, (((0,), (0,)), ((), ())), preferred_element_type=jnp.float32
    )
    ctx_count = lax.axis_size("ctx")
    dp_count = lax.axis_size("dp")
    members = ctx_count * dp_count
    proj_rows = proj_local.shape[0] // members
    kernel_rows = -(-KW // members)
    kernel_padded = jnp.pad(kernel_local, ((0, kernel_rows * members - KW), (0, 0)))
    stacked = jnp.concatenate(
        [
            proj_local.reshape(dp_count, ctx_count, proj_rows, channels),
            kernel_padded.reshape(dp_count, ctx_count, kernel_rows, channels),
        ],
        axis=2,
    )
    summed = halving(halving(stacked, "dp"), "ctx").astype(jnp.bfloat16)
    grad_attended = lax.dot_general(
        grad_hidden, out_proj, (((1,), (1,)), ((), ())), preferred_element_type=jnp.float32
    ).astype(jnp.bfloat16)
    delta_rows = jnp.sum(
        (grad_attended.astype(jnp.float32) * attended.astype(jnp.float32)).reshape(
            tokens, HEADS, HDIM
        ),
        axis=2,
    )
    grad_spread = spread(grad_attended)
    grad_weights = contract(grad_spread, value_all, 1, 1)
    grad_logits = (
        weights.astype(jnp.float32) * (grad_weights - delta_rows.T.reshape(HEADS * tokens, 1))
    ).astype(jnp.bfloat16)
    grad_query = (own_heads(contract(grad_logits, key_all, 1, 0)) * scale_factor).astype(
        jnp.bfloat16
    )
    grad_key_all = contract(grad_logits, query_spread, 0, 0) * scale_factor
    grad_value_all = contract(weights, grad_spread, 0, 0)
    key_blocks = grad_key_all.reshape(span_blocks, tokens, width_heads)
    value_blocks = grad_value_all.reshape(span_blocks, tokens, width_heads)
    narrow = jnp.stack([key_blocks, value_blocks], axis=1).astype(jnp.bfloat16)
    near = jnp.stack(
        [key_blocks[REACH - 1 : REACH + 2], value_blocks[REACH - 1 : REACH + 2]], axis=1
    )

    def grad_shift(piece_rows, offset_by):
        return passed_along(piece_rows, "ctx", offset_by)

    gathered = doubling(doubling(summed, "ctx"), "dp")
    proj_sum = gathered[:, :, :proj_rows].reshape(members * proj_rows, channels)
    kernel_sum = (
        gathered[:, :, proj_rows:].astype(jnp.float32).reshape(members * kernel_rows, channels)[:KW]
    )
    own_grads = give_back(near, narrow, grad_shift)
    grad_key = own_grads[0].astype(jnp.bfloat16)
    grad_value = own_grads[1].astype(jnp.bfloat16)
    return (
        grad_query[None],
        grad_key[None],
        grad_value[None],
        proj_sum,
        kernel_sum,
    )


def solution(mesh):
    return jax.shard_map(
        on_device,
        mesh=mesh,
        in_specs=(
            P(("group", "dp"), "ctx", None),
            P(("group", "dp"), "ctx", None),
            P(("group", "dp"), "ctx", None),
            P(("group", "dp"), "ctx", None),
            P(),
            P(),
            P(("group", "dp")),
        ),
        out_specs=(
            P(("group", "dp"), "ctx", None),
            P(("group", "dp"), "ctx", None),
            P(("group", "dp"), "ctx", None),
            P("group", None),
            P("group", None),
        ),
        check_vma=False,
    )
```

```python
import math

import jax
import jax.numpy as jnp
from jax import lax
from jax.sharding import PartitionSpec as P

HEADS = 8
HDIM = 64
KW = 31
REACH = 3


def passed_along(block, axis, distance):
    devices = range(lax.axis_size(axis))
    route = [(i - distance, i) for i in devices if i - distance in devices]
    return lax.ppermute(block, axis, route)


def padded(cells, sides, width):
    for axis, dim in sides:
        count = lax.axis_size(axis)
        ends = count - 1
        head = lax.slice_in_dim(cells, 0, width, axis=dim)
        tail = lax.slice_in_dim(cells, cells.shape[dim] - width, cells.shape[dim], axis=dim)
        cells = jnp.concatenate(
            [
                lax.ppermute(tail, axis, [(i, (i + 1) % count) for i in range(ends)]),
                cells,
                lax.ppermute(head, axis, [((i + 1) % count, i) for i in range(ends)]),
            ],
            axis=dim,
        )
    return cells


def collect(piece_own, shifter, up_extra, down_extra):
    rows = piece_own.shape[0] * piece_own.shape[1]
    flat = piece_own.reshape(rows, piece_own.shape[2])
    got_below = shifter(jnp.concatenate([flat, up_extra], axis=0), 1)
    got_above = shifter(jnp.concatenate([flat, down_extra], axis=0), -1)
    below_one = got_below[:rows].reshape(piece_own.shape)
    above_one = got_above[:rows].reshape(piece_own.shape)
    below = shifter(jnp.stack([below_one, piece_own], axis=0), 2)
    above = shifter(jnp.stack([piece_own, above_one], axis=0), -2)
    window = jnp.stack(
        [below[0], below[1], below_one, piece_own, above_one, above[0], above[1]], axis=0
    )
    return window, got_below[rows:], got_above[rows:]


def give_back(near, narrow, shifter):
    from_below = shifter(narrow[REACH + 2 :], 2).astype(jnp.float32)
    from_above = shifter(narrow[: REACH - 1], -2).astype(jnp.float32)
    upward = (near[2] + from_below[1]).astype(jnp.bfloat16)
    downward = (near[0] + from_above[0]).astype(jnp.bfloat16)
    return (
        near[1]
        + from_below[0]
        + from_above[1]
        + shifter(upward, 1).astype(jnp.float32)
        + shifter(downward, -1).astype(jnp.float32)
    )


def exchange(block, axis, bit):
    count = lax.axis_size(axis)
    return lax.ppermute(block, axis, [(i, i ^ bit) for i in range(count)])


def halving(acc, axis):
    here = lax.axis_index(axis)
    count = lax.axis_size(axis)
    levels = count.bit_length() - 1
    for level in range(levels):
        half = acc.shape[0] // 2
        mine = (here >> level) % 2
        keep = lax.dynamic_slice_in_dim(acc, mine * half, half, 0)
        send = lax.dynamic_slice_in_dim(acc, (1 - mine) * half, half, 0)
        acc = keep + exchange(send.astype(jnp.bfloat16), axis, 1 << level).astype(jnp.float32)
    return acc[0]


def doubling(acc, axis):
    here = lax.axis_index(axis)
    count = lax.axis_size(axis)
    levels = count.bit_length() - 1
    acc = acc[None]
    for level in range(levels - 1, -1, -1):
        theirs = exchange(acc, axis, 1 << level)
        mine = (here >> level) % 2
        width = acc.shape[0]
        joined = jnp.zeros((2 * width,) + acc.shape[1:], acc.dtype)
        joined = lax.dynamic_update_slice_in_dim(joined, acc, mine * width, 0)
        acc = lax.dynamic_update_slice_in_dim(joined, theirs, (1 - mine) * width, 0)
    return acc


def on_device(queries, key_rows, values, cotangent, out_proj, conv_kernel, lengths):
    tokens = queries.shape[1]
    width_heads = queries.shape[2]
    channels = out_proj.shape[1]
    span_blocks = 2 * REACH + 1
    scale_factor = 1.0 / math.sqrt(HDIM)
    halo_width = (KW - 1) // 2
    block_index = lax.axis_index("ctx")
    length_here = lengths[0]
    query_here = queries[0]
    key_here = key_rows[0]
    value_here = values[0]
    cot_here = cotangent[0]
    frames = block_index * tokens + jnp.arange(tokens, dtype=jnp.int32)
    valid_rows = frames < length_here
    key_frames = (block_index - REACH) * tokens + jnp.arange(span_blocks * tokens, dtype=jnp.int32)
    valid_keys = (key_frames >= 0) & (key_frames < length_here)

    def kv_shift(piece_rows, offset_by):
        return passed_along(piece_rows, "ctx", offset_by)

    halo_rows = -(-halo_width // 8) * 8

    def edge_rows(rows_here):
        padded_rows = jnp.pad(rows_here, ((0, halo_rows - halo_width), (0, 0)))
        return padded_rows.reshape(-1, width_heads)

    def edge_back(packed):
        return packed.reshape(halo_rows, channels)[:halo_width]

    gathered, cot_low, cot_high = collect(
        jnp.stack([key_here, value_here], axis=0),
        kv_shift,
        edge_rows(cot_here[tokens - halo_width :]),
        edge_rows(cot_here[:halo_width]),
    )
    cot_wide = jnp.concatenate([edge_back(cot_low), cot_here, edge_back(cot_high)], axis=0)
    kv_rows = span_blocks * tokens
    key_all = gathered[:, 0].reshape(kv_rows, width_heads)
    value_all = gathered[:, 1].reshape(kv_rows, width_heads)
    head_mask = (
        jnp.arange(HEADS, dtype=jnp.int32)[:, None, None]
        == (jnp.arange(width_heads, dtype=jnp.int32) // HDIM)[None, None, :]
    )

    def spread(rows):
        return jnp.where(head_mask, rows[None], jnp.zeros((), rows.dtype)).reshape(
            HEADS * tokens, width_heads
        )

    def own_heads(stacked_rows):
        picked = jnp.where(head_mask, stacked_rows.reshape(HEADS, tokens, width_heads), 0.0)
        return jnp.sum(picked, axis=0)

    def contract(lhs, rhs, lhs_dim, rhs_dim):
        return lax.dot_general(
            lhs, rhs, (((lhs_dim,), (rhs_dim,)), ((), ())), preferred_element_type=jnp.float32
        )

    query_spread = spread(query_here)
    scores = contract(query_spread, key_all, 1, 1) * scale_factor
    scores = jnp.where(valid_keys[None, :], scores, -jnp.inf)
    row_max = jnp.max(scores, axis=1, keepdims=True)
    row_total = jnp.sum(jnp.exp(scores - row_max), axis=1, keepdims=True)
    log_total = row_max + jnp.log(row_total)
    weights = jnp.exp(scores - log_total).astype(jnp.bfloat16)
    attended = own_heads(contract(weights, value_all, 1, 0)).astype(jnp.bfloat16)
    hidden = jnp.dot(attended, out_proj, preferred_element_type=jnp.float32)
    masked = jnp.where(valid_rows[:, None], hidden, 0.0).astype(jnp.bfloat16)

    wide_rows = tokens + 2 * halo_width
    padded_m = padded(masked, (("ctx", 0),), 2 * halo_width)
    conv_out = jnp.zeros((wide_rows, channels), jnp.float32)
    for tap_index in range(KW):
        conv_out = conv_out + conv_kernel[tap_index] * padded_m[tap_index : tap_index + wide_rows]
    sigmoid_c = jax.nn.sigmoid(conv_out)
    grad_conv = (
        cot_wide.astype(jnp.float32) * (sigmoid_c + conv_out * sigmoid_c * (1.0 - sigmoid_c))
    ).astype(jnp.bfloat16)
    grad_masked = jnp.zeros((tokens, channels), jnp.float32)
    for tap_index in range(KW):
        start_row = 2 * halo_width - tap_index
        grad_masked = (
            grad_masked + conv_kernel[tap_index] * grad_conv[start_row : start_row + tokens]
        )
    kernel_local = lax.conv_general_dilated(
        padded_m[None, halo_width : halo_width + wide_rows],
        grad_conv[halo_width : halo_width + tokens, None, :],
        window_strides=(1,),
        padding="VALID",
        dimension_numbers=("NWC", "WIO", "NWC"),
        feature_group_count=channels,
        preferred_element_type=jnp.float32,
    )[0]
    grad_hidden = (
        cot_here.astype(jnp.float32) + jnp.where(valid_rows[:, None], grad_masked, 0.0)
    ).astype(jnp.bfloat16)
    proj_local = lax.dot_general(
        attended, grad_hidden, (((0,), (0,)), ((), ())), preferred_element_type=jnp.float32
    )
    ctx_count = lax.axis_size("ctx")
    dp_count = lax.axis_size("dp")
    members = ctx_count * dp_count
    proj_rows = proj_local.shape[0] // members
    kernel_rows = -(-KW // members)
    kernel_padded = jnp.pad(kernel_local, ((0, kernel_rows * members - KW), (0, 0)))
    stacked = jnp.concatenate(
        [
            proj_local.reshape(dp_count, ctx_count, proj_rows, channels),
            kernel_padded.reshape(dp_count, ctx_count, kernel_rows, channels),
        ],
        axis=2,
    )
    summed = halving(halving(stacked, "dp"), "ctx").astype(jnp.bfloat16)
    grad_attended = lax.dot_general(
        grad_hidden, out_proj, (((1,), (1,)), ((), ())), preferred_element_type=jnp.float32
    ).astype(jnp.bfloat16)
    delta_rows = jnp.sum(
        (grad_attended.astype(jnp.float32) * attended.astype(jnp.float32)).reshape(
            tokens, HEADS, HDIM
        ),
        axis=2,
    )
    grad_spread = spread(grad_attended)
    grad_weights = contract(grad_spread, value_all, 1, 1)
    grad_logits = (
        weights.astype(jnp.float32) * (grad_weights - delta_rows.T.reshape(HEADS * tokens, 1))
    ).astype(jnp.bfloat16)
    grad_query = (own_heads(contract(grad_logits, key_all, 1, 0)) * scale_factor).astype(
        jnp.bfloat16
    )
    grad_key_all = contract(grad_logits, query_spread, 0, 0) * scale_factor
    grad_value_all = contract(weights, grad_spread, 0, 0)
    key_blocks = grad_key_all.reshape(span_blocks, tokens, width_heads)
    value_blocks = grad_value_all.reshape(span_blocks, tokens, width_heads)
    narrow = jnp.stack([key_blocks, value_blocks], axis=1).astype(jnp.bfloat16)
    near = jnp.stack(
        [key_blocks[REACH - 1 : REACH + 2], value_blocks[REACH - 1 : REACH + 2]], axis=1
    )

    def grad_shift(piece_rows, offset_by):
        return passed_along(piece_rows, "ctx", offset_by)

    gathered = doubling(doubling(summed, "ctx"), "dp")
    proj_sum = gathered[:, :, :proj_rows].reshape(members * proj_rows, channels)
    kernel_sum = (
        gathered[:, :, proj_rows:].astype(jnp.float32).reshape(members * kernel_rows, channels)[:KW]
    )
    own_grads = give_back(near, narrow, grad_shift)
    grad_key = own_grads[0].astype(jnp.bfloat16)
    grad_value = own_grads[1].astype(jnp.bfloat16)
    return (
        grad_query[None],
        grad_key[None],
        grad_value[None],
        proj_sum,
        kernel_sum,
    )


def solution(mesh):
    return jax.shard_map(
        on_device,
        mesh=mesh,
        in_specs=(
            P(("group", "dp"), "ctx", None),
            P(("group", "dp"), "ctx", None),
            P(("group", "dp"), "ctx", None),
            P(("group", "dp"), "ctx", None),
            P(),
            P(),
            P(("group", "dp")),
        ),
        out_specs=(
            P(("group", "dp"), "ctx", None),
            P(("group", "dp"), "ctx", None),
            P(("group", "dp"), "ctx", None),
            P("group", None),
            P("group", None),
        ),
        check_vma=False,
    )
```

```python
import math

import jax
import jax.numpy as jnp
from jax import lax
from jax.sharding import PartitionSpec as P

HEADS = 8
HDIM = 64
KW = 31
REACH = 3


def passed_along(block, axis, distance):
    devices = range(lax.axis_size(axis))
    route = [(i - distance, i) for i in devices if i - distance in devices]
    return lax.ppermute(block, axis, route)


def padded(cells, sides, width):
    for axis, dim in sides:
        count = lax.axis_size(axis)
        ends = count - 1
        head = lax.slice_in_dim(cells, 0, width, axis=dim)
        tail = lax.slice_in_dim(cells, cells.shape[dim] - width, cells.shape[dim], axis=dim)
        cells = jnp.concatenate(
            [
                lax.ppermute(tail, axis, [(i, (i + 1) % count) for i in range(ends)]),
                cells,
                lax.ppermute(head, axis, [((i + 1) % count, i) for i in range(ends)]),
            ],
            axis=dim,
        )
    return cells


def collect(piece_own, shifter, up_extra, down_extra):
    rows = piece_own.shape[0] * piece_own.shape[1]
    flat = piece_own.reshape(rows, piece_own.shape[2])
    got_below = shifter(jnp.concatenate([flat, up_extra], axis=0), 1)
    got_above = shifter(jnp.concatenate([flat, down_extra], axis=0), -1)
    below_one = got_below[:rows].reshape(piece_own.shape)
    above_one = got_above[:rows].reshape(piece_own.shape)
    below = shifter(jnp.stack([below_one, piece_own], axis=0), 2)
    above = shifter(jnp.stack([piece_own, above_one], axis=0), -2)
    window = [below[0], below[1], below_one, piece_own, above_one, above[0], above[1]]
    return window, got_below[rows:], got_above[rows:]


def give_back(near, narrow, shifter):
    from_below = shifter(narrow[REACH + 2 :], 2).astype(jnp.float32)
    from_above = shifter(narrow[: REACH - 1], -2).astype(jnp.float32)
    upward = (near[2] + from_below[1]).astype(jnp.bfloat16)
    downward = (near[0] + from_above[0]).astype(jnp.bfloat16)
    return (
        near[1]
        + from_below[0]
        + from_above[1]
        + shifter(upward, 1).astype(jnp.float32)
        + shifter(downward, -1).astype(jnp.float32)
    )


def exchange(block, axis, bit):
    count = lax.axis_size(axis)
    return lax.ppermute(block, axis, [(i, i ^ bit) for i in range(count)])


def halving(acc, axis):
    here = lax.axis_index(axis)
    count = lax.axis_size(axis)
    levels = count.bit_length() - 1
    for level in range(levels):
        half = acc.shape[0] // 2
        mine = (here >> level) % 2
        keep = lax.dynamic_slice_in_dim(acc, mine * half, half, 0)
        send = lax.dynamic_slice_in_dim(acc, (1 - mine) * half, half, 0)
        acc = keep + exchange(send.astype(jnp.bfloat16), axis, 1 << level).astype(jnp.float32)
    return acc[0]


def doubling(acc, axis):
    here = lax.axis_index(axis)
    count = lax.axis_size(axis)
    levels = count.bit_length() - 1
    acc = acc[None]
    for level in range(levels - 1, -1, -1):
        theirs = exchange(acc, axis, 1 << level)
        first = (here >> level) % 2 == 0
        acc = jnp.concatenate(
            [jnp.where(first, acc, theirs), jnp.where(first, theirs, acc)], axis=0
        )
    return acc


def on_device(queries, key_rows, values, cotangent, out_proj, conv_kernel, lengths):
    tokens = queries.shape[1]
    width_heads = queries.shape[2]
    channels = out_proj.shape[1]
    span_blocks = 2 * REACH + 1
    scale_factor = 1.0 / math.sqrt(HDIM)
    halo_width = (KW - 1) // 2
    block_index = lax.axis_index("ctx")
    length_here = lengths[0]
    query_here = queries[0]
    key_here = key_rows[0]
    value_here = values[0]
    cot_here = cotangent[0]
    frames = block_index * tokens + jnp.arange(tokens, dtype=jnp.int32)
    valid_rows = frames < length_here
    key_frames = (block_index - REACH) * tokens + jnp.arange(span_blocks * tokens, dtype=jnp.int32)
    valid_keys = (key_frames >= 0) & (key_frames < length_here)

    def kv_shift(piece_rows, offset_by):
        return passed_along(piece_rows, "ctx", offset_by)

    halo_rows = -(-halo_width // 8) * 8

    def edge_rows(rows_here):
        padded_rows = jnp.pad(rows_here, ((0, halo_rows - halo_width), (0, 0)))
        return padded_rows.reshape(-1, width_heads)

    def edge_back(packed):
        return packed.reshape(halo_rows, channels)[:halo_width]

    gathered, cot_low, cot_high = collect(
        jnp.stack([key_here, value_here], axis=0),
        kv_shift,
        edge_rows(cot_here[tokens - halo_width :]),
        edge_rows(cot_here[:halo_width]),
    )
    cot_wide = jnp.concatenate([edge_back(cot_low), cot_here, edge_back(cot_high)], axis=0)
    kv_rows = span_blocks * tokens
    key_all = jnp.concatenate([block[0] for block in gathered], axis=0)
    value_all = jnp.concatenate([block[1] for block in gathered], axis=0)
    head_mask = (
        jnp.arange(HEADS, dtype=jnp.int32)[:, None, None]
        == (jnp.arange(width_heads, dtype=jnp.int32) // HDIM)[None, None, :]
    )

    def spread(rows):
        return jnp.where(head_mask, rows[None], jnp.zeros((), rows.dtype)).reshape(
            HEADS * tokens, width_heads
        )

    def own_heads(stacked_rows):
        picked = jnp.where(head_mask, stacked_rows.reshape(HEADS, tokens, width_heads), 0.0)
        return jnp.sum(picked, axis=0)

    def contract(lhs, rhs, lhs_dim, rhs_dim):
        return lax.dot_general(
            lhs, rhs, (((lhs_dim,), (rhs_dim,)), ((), ())), preferred_element_type=jnp.float32
        )

    query_spread = spread(query_here)
    scores = contract(query_spread, key_all, 1, 1) * scale_factor
    scores = jnp.where(valid_keys[None, :], scores, -jnp.inf)
    row_max = jnp.max(scores, axis=1, keepdims=True)
    row_total = jnp.sum(jnp.exp(scores - row_max), axis=1, keepdims=True)
    log_total = row_max + jnp.log(row_total)
    weights = jnp.exp(scores - log_total).astype(jnp.bfloat16)
    attended = own_heads(contract(weights, value_all, 1, 0)).astype(jnp.bfloat16)
    hidden = jnp.dot(attended, out_proj, preferred_element_type=jnp.float32)
    masked = jnp.where(valid_rows[:, None], hidden, 0.0).astype(jnp.bfloat16)

    wide_rows = tokens + 2 * halo_width
    padded_m = padded(masked, (("ctx", 0),), 2 * halo_width)
    conv_out = jnp.zeros((wide_rows, channels), jnp.float32)
    for tap_index in range(KW):
        conv_out = conv_out + conv_kernel[tap_index] * padded_m[tap_index : tap_index + wide_rows]
    sigmoid_c = jax.nn.sigmoid(conv_out)
    grad_conv = (
        cot_wide.astype(jnp.float32) * (sigmoid_c + conv_out * sigmoid_c * (1.0 - sigmoid_c))
    ).astype(jnp.bfloat16)
    grad_masked = jnp.zeros((tokens, channels), jnp.float32)
    for tap_index in range(KW):
        start_row = 2 * halo_width - tap_index
        grad_masked = (
            grad_masked + conv_kernel[tap_index] * grad_conv[start_row : start_row + tokens]
        )
    kernel_local = lax.conv_general_dilated(
        padded_m[None, halo_width : halo_width + wide_rows],
        grad_conv[halo_width : halo_width + tokens, None, :],
        window_strides=(1,),
        padding="VALID",
        dimension_numbers=("NWC", "WIO", "NWC"),
        feature_group_count=channels,
        preferred_element_type=jnp.float32,
    )[0]
    grad_hidden = (
        cot_here.astype(jnp.float32) + jnp.where(valid_rows[:, None], grad_masked, 0.0)
    ).astype(jnp.bfloat16)
    proj_local = lax.dot_general(
        attended, grad_hidden, (((0,), (0,)), ((), ())), preferred_element_type=jnp.float32
    )
    ctx_count = lax.axis_size("ctx")
    dp_count = lax.axis_size("dp")
    members = ctx_count * dp_count
    proj_rows = proj_local.shape[0] // members
    kernel_rows = -(-KW // members)
    kernel_padded = jnp.pad(kernel_local, ((0, kernel_rows * members - KW), (0, 0)))
    stacked = jnp.concatenate(
        [
            proj_local.reshape(dp_count, ctx_count, proj_rows, channels),
            kernel_padded.reshape(dp_count, ctx_count, kernel_rows, channels),
        ],
        axis=2,
    )
    summed = halving(halving(stacked, "dp"), "ctx").astype(jnp.bfloat16)
    grad_attended = lax.dot_general(
        grad_hidden, out_proj, (((1,), (1,)), ((), ())), preferred_element_type=jnp.float32
    ).astype(jnp.bfloat16)
    delta_rows = jnp.sum(
        (grad_attended.astype(jnp.float32) * attended.astype(jnp.float32)).reshape(
            tokens, HEADS, HDIM
        ),
        axis=2,
    )
    grad_spread = spread(grad_attended)
    grad_weights = contract(grad_spread, value_all, 1, 1)
    grad_logits = (
        weights.astype(jnp.float32) * (grad_weights - delta_rows.T.reshape(HEADS * tokens, 1))
    ).astype(jnp.bfloat16)
    grad_query = (own_heads(contract(grad_logits, key_all, 1, 0)) * scale_factor).astype(
        jnp.bfloat16
    )
    grad_key_all = contract(grad_logits, query_spread, 0, 0) * scale_factor
    grad_value_all = contract(weights, grad_spread, 0, 0)
    key_blocks = grad_key_all.reshape(span_blocks, tokens, width_heads)
    value_blocks = grad_value_all.reshape(span_blocks, tokens, width_heads)
    narrow = jnp.stack([key_blocks, value_blocks], axis=1).astype(jnp.bfloat16)
    near = jnp.stack(
        [key_blocks[REACH - 1 : REACH + 2], value_blocks[REACH - 1 : REACH + 2]], axis=1
    )

    def grad_shift(piece_rows, offset_by):
        return passed_along(piece_rows, "ctx", offset_by)

    gathered = doubling(doubling(summed, "ctx"), "dp")
    proj_sum = gathered[:, :, :proj_rows].reshape(members * proj_rows, channels)
    kernel_sum = (
        gathered[:, :, proj_rows:].astype(jnp.float32).reshape(members * kernel_rows, channels)[:KW]
    )
    own_grads = give_back(near, narrow, grad_shift)
    grad_key = own_grads[0].astype(jnp.bfloat16)
    grad_value = own_grads[1].astype(jnp.bfloat16)
    return (
        grad_query[None],
        grad_key[None],
        grad_value[None],
        proj_sum,
        kernel_sum,
    )


def solution(mesh):
    return jax.shard_map(
        on_device,
        mesh=mesh,
        in_specs=(
            P(("group", "dp"), "ctx", None),
            P(("group", "dp"), "ctx", None),
            P(("group", "dp"), "ctx", None),
            P(("group", "dp"), "ctx", None),
            P(),
            P(),
            P(("group", "dp")),
        ),
        out_specs=(
            P(("group", "dp"), "ctx", None),
            P(("group", "dp"), "ctx", None),
            P(("group", "dp"), "ctx", None),
            P("group", None),
            P("group", None),
        ),
        check_vma=False,
    )
```

```python
import math

import jax
import jax.numpy as jnp
from jax import lax
from jax.sharding import PartitionSpec as P

HEADS = 8
HDIM = 64
KW = 31
REACH = 3


def passed_along(block, axis, distance):
    devices = range(lax.axis_size(axis))
    route = [(i - distance, i) for i in devices if i - distance in devices]
    return lax.ppermute(block, axis, route)


def padded(cells, sides, width):
    for axis, dim in sides:
        count = lax.axis_size(axis)
        ends = count - 1
        head = lax.slice_in_dim(cells, 0, width, axis=dim)
        tail = lax.slice_in_dim(cells, cells.shape[dim] - width, cells.shape[dim], axis=dim)
        cells = jnp.concatenate(
            [
                lax.ppermute(tail, axis, [(i, (i + 1) % count) for i in range(ends)]),
                cells,
                lax.ppermute(head, axis, [((i + 1) % count, i) for i in range(ends)]),
            ],
            axis=dim,
        )
    return cells


def collect(piece_own, shifter, up_extra, down_extra):
    rows = piece_own.shape[0] * piece_own.shape[1]
    flat = piece_own.reshape(rows, piece_own.shape[2])
    got_below = shifter(jnp.concatenate([flat, up_extra], axis=0), 1)
    got_above = shifter(jnp.concatenate([flat, down_extra], axis=0), -1)
    below_one = got_below[:rows].reshape(piece_own.shape)
    above_one = got_above[:rows].reshape(piece_own.shape)
    below = shifter(jnp.stack([below_one, piece_own], axis=0), 2)
    above = shifter(jnp.stack([piece_own, above_one], axis=0), -2)
    window = [below[0], below[1], below_one, piece_own, above_one, above[0], above[1]]
    return window, got_below[rows:], got_above[rows:]


def give_back(near, far_down, far_up, shifter):
    from_below = shifter(far_up, 2).astype(jnp.float32)
    from_above = shifter(far_down, -2).astype(jnp.float32)
    upward = (near[2] + from_below[1]).astype(jnp.bfloat16)
    downward = (near[0] + from_above[0]).astype(jnp.bfloat16)
    return (
        near[1]
        + from_below[0]
        + from_above[1]
        + shifter(upward, 1).astype(jnp.float32)
        + shifter(downward, -1).astype(jnp.float32)
    )


def exchange(block, axis, bit):
    count = lax.axis_size(axis)
    return lax.ppermute(block, axis, [(i, i ^ bit) for i in range(count)])


def halving(acc, axis):
    here = lax.axis_index(axis)
    count = lax.axis_size(axis)
    levels = count.bit_length() - 1
    for level in range(levels):
        half = acc.shape[0] // 2
        mine = (here >> level) % 2
        keep = lax.dynamic_slice_in_dim(acc, mine * half, half, 0)
        send = lax.dynamic_slice_in_dim(acc, (1 - mine) * half, half, 0)
        acc = keep + exchange(send.astype(jnp.bfloat16), axis, 1 << level).astype(jnp.float32)
    return acc[0]


def doubling(acc, axis):
    here = lax.axis_index(axis)
    count = lax.axis_size(axis)
    levels = count.bit_length() - 1
    acc = acc[None]
    for level in range(levels - 1, -1, -1):
        theirs = exchange(acc, axis, 1 << level)
        first = (here >> level) % 2 == 0
        acc = jnp.concatenate(
            [jnp.where(first, acc, theirs), jnp.where(first, theirs, acc)], axis=0
        )
    return acc


def on_device(queries, key_rows, values, cotangent, out_proj, conv_kernel, lengths):
    tokens = queries.shape[1]
    width_heads = queries.shape[2]
    channels = out_proj.shape[1]
    span_blocks = 2 * REACH + 1
    scale_factor = 1.0 / math.sqrt(HDIM)
    halo_width = (KW - 1) // 2
    block_index = lax.axis_index("ctx")
    length_here = lengths[0]
    query_here = queries[0]
    key_here = key_rows[0]
    value_here = values[0]
    cot_here = cotangent[0]
    frames = block_index * tokens + jnp.arange(tokens, dtype=jnp.int32)
    valid_rows = frames < length_here
    key_frames = (block_index - REACH) * tokens + jnp.arange(span_blocks * tokens, dtype=jnp.int32)
    valid_keys = (key_frames >= 0) & (key_frames < length_here)

    def kv_shift(piece_rows, offset_by):
        return passed_along(piece_rows, "ctx", offset_by)

    halo_rows = -(-halo_width // 8) * 8

    def edge_rows(rows_here):
        padded_rows = jnp.pad(rows_here, ((0, halo_rows - halo_width), (0, 0)))
        return padded_rows.reshape(-1, width_heads)

    def edge_back(packed):
        return packed.reshape(halo_rows, channels)[:halo_width]

    gathered, cot_low, cot_high = collect(
        jnp.stack([key_here, value_here], axis=0),
        kv_shift,
        edge_rows(cot_here[tokens - halo_width :]),
        edge_rows(cot_here[:halo_width]),
    )
    cot_wide = jnp.concatenate([edge_back(cot_low), cot_here, edge_back(cot_high)], axis=0)
    kv_rows = span_blocks * tokens
    key_all = jnp.concatenate([block[0] for block in gathered], axis=0)
    value_all = jnp.concatenate([block[1] for block in gathered], axis=0)
    head_mask = (
        jnp.arange(HEADS, dtype=jnp.int32)[:, None, None]
        == (jnp.arange(width_heads, dtype=jnp.int32) // HDIM)[None, None, :]
    )

    def spread(rows):
        return jnp.where(head_mask, rows[None], jnp.zeros((), rows.dtype)).reshape(
            HEADS * tokens, width_heads
        )

    def own_heads(stacked_rows):
        picked = jnp.where(head_mask, stacked_rows.reshape(HEADS, tokens, width_heads), 0.0)
        return jnp.sum(picked, axis=0)

    def contract(lhs, rhs, lhs_dim, rhs_dim):
        return lax.dot_general(
            lhs, rhs, (((lhs_dim,), (rhs_dim,)), ((), ())), preferred_element_type=jnp.float32
        )

    query_spread = spread(query_here)
    scores = contract(query_spread, key_all, 1, 1) * scale_factor
    scores = jnp.where(valid_keys[None, :], scores, -jnp.inf)
    row_max = jnp.max(scores, axis=1, keepdims=True)
    row_total = jnp.sum(jnp.exp(scores - row_max), axis=1, keepdims=True)
    log_total = row_max + jnp.log(row_total)
    weights = jnp.exp(scores - log_total).astype(jnp.bfloat16)
    attended = own_heads(contract(weights, value_all, 1, 0)).astype(jnp.bfloat16)
    hidden = jnp.dot(attended, out_proj, preferred_element_type=jnp.float32)
    masked = jnp.where(valid_rows[:, None], hidden, 0.0).astype(jnp.bfloat16)

    wide_rows = tokens + 2 * halo_width
    padded_m = padded(masked, (("ctx", 0),), 2 * halo_width)
    conv_out = jnp.zeros((wide_rows, channels), jnp.float32)
    for tap_index in range(KW):
        conv_out = conv_out + conv_kernel[tap_index] * padded_m[tap_index : tap_index + wide_rows]
    sigmoid_c = jax.nn.sigmoid(conv_out)
    grad_conv = (
        cot_wide.astype(jnp.float32) * (sigmoid_c + conv_out * sigmoid_c * (1.0 - sigmoid_c))
    ).astype(jnp.bfloat16)
    grad_masked = jnp.zeros((tokens, channels), jnp.float32)
    for tap_index in range(KW):
        start_row = 2 * halo_width - tap_index
        grad_masked = (
            grad_masked + conv_kernel[tap_index] * grad_conv[start_row : start_row + tokens]
        )
    kernel_local = lax.conv_general_dilated(
        padded_m[None, halo_width : halo_width + wide_rows],
        grad_conv[halo_width : halo_width + tokens, None, :],
        window_strides=(1,),
        padding="VALID",
        dimension_numbers=("NWC", "WIO", "NWC"),
        feature_group_count=channels,
        preferred_element_type=jnp.float32,
    )[0]
    grad_hidden = (
        cot_here.astype(jnp.float32) + jnp.where(valid_rows[:, None], grad_masked, 0.0)
    ).astype(jnp.bfloat16)
    proj_local = lax.dot_general(
        attended, grad_hidden, (((0,), (0,)), ((), ())), preferred_element_type=jnp.float32
    )
    ctx_count = lax.axis_size("ctx")
    dp_count = lax.axis_size("dp")
    members = ctx_count * dp_count
    proj_rows = proj_local.shape[0] // members
    kernel_rows = -(-KW // members)
    kernel_padded = jnp.pad(kernel_local, ((0, kernel_rows * members - KW), (0, 0)))
    stacked = jnp.concatenate(
        [
            proj_local.reshape(dp_count, ctx_count, proj_rows, channels),
            kernel_padded.reshape(dp_count, ctx_count, kernel_rows, channels),
        ],
        axis=2,
    )
    summed = halving(halving(stacked, "dp"), "ctx").astype(jnp.bfloat16)
    grad_attended = lax.dot_general(
        grad_hidden, out_proj, (((1,), (1,)), ((), ())), preferred_element_type=jnp.float32
    ).astype(jnp.bfloat16)
    delta_rows = jnp.sum(
        (grad_attended.astype(jnp.float32) * attended.astype(jnp.float32)).reshape(
            tokens, HEADS, HDIM
        ),
        axis=2,
    )
    grad_spread = spread(grad_attended)
    grad_weights = contract(grad_spread, value_all, 1, 1)
    grad_logits = (
        weights.astype(jnp.float32) * (grad_weights - delta_rows.T.reshape(HEADS * tokens, 1))
    ).astype(jnp.bfloat16)
    grad_query = (own_heads(contract(grad_logits, key_all, 1, 0)) * scale_factor).astype(
        jnp.bfloat16
    )
    grad_key_all = contract(grad_logits, query_spread, 0, 0) * scale_factor
    grad_value_all = contract(weights, grad_spread, 0, 0)
    key_blocks = grad_key_all.reshape(span_blocks, tokens, width_heads)
    value_blocks = grad_value_all.reshape(span_blocks, tokens, width_heads)
    def pair_rows(first, last):
        return jnp.stack([key_blocks[first:last], value_blocks[first:last]], axis=1)

    far_down = pair_rows(0, REACH - 1).astype(jnp.bfloat16)
    far_up = pair_rows(REACH + 2, span_blocks).astype(jnp.bfloat16)
    near = pair_rows(REACH - 1, REACH + 2)

    def grad_shift(piece_rows, offset_by):
        return passed_along(piece_rows, "ctx", offset_by)

    gathered = doubling(doubling(summed, "ctx"), "dp")
    proj_sum = gathered[:, :, :proj_rows].reshape(members * proj_rows, channels)
    kernel_sum = (
        gathered[:, :, proj_rows:].astype(jnp.float32).reshape(members * kernel_rows, channels)[:KW]
    )
    own_grads = give_back(near, far_down, far_up, grad_shift)
    grad_key = own_grads[0].astype(jnp.bfloat16)
    grad_value = own_grads[1].astype(jnp.bfloat16)
    return (
        grad_query[None],
        grad_key[None],
        grad_value[None],
        proj_sum,
        kernel_sum,
    )


def solution(mesh):
    return jax.shard_map(
        on_device,
        mesh=mesh,
        in_specs=(
            P(("group", "dp"), "ctx", None),
            P(("group", "dp"), "ctx", None),
            P(("group", "dp"), "ctx", None),
            P(("group", "dp"), "ctx", None),
            P(),
            P(),
            P(("group", "dp")),
        ),
        out_specs=(
            P(("group", "dp"), "ctx", None),
            P(("group", "dp"), "ctx", None),
            P(("group", "dp"), "ctx", None),
            P("group", None),
            P("group", None),
        ),
        check_vma=False,
    )
```

```python
import math

import jax
import jax.numpy as jnp
from jax import lax
from jax.sharding import PartitionSpec as P

HEADS = 8
HDIM = 64
KW = 31
REACH = 3


def passed_along(block, axis, distance):
    devices = range(lax.axis_size(axis))
    route = [(i - distance, i) for i in devices if i - distance in devices]
    return lax.ppermute(block, axis, route)


def padded(cells, sides, width):
    for axis, dim in sides:
        count = lax.axis_size(axis)
        ends = count - 1
        head = lax.slice_in_dim(cells, 0, width, axis=dim)
        tail = lax.slice_in_dim(cells, cells.shape[dim] - width, cells.shape[dim], axis=dim)
        cells = jnp.concatenate(
            [
                lax.ppermute(tail, axis, [(i, (i + 1) % count) for i in range(ends)]),
                cells,
                lax.ppermute(head, axis, [((i + 1) % count, i) for i in range(ends)]),
            ],
            axis=dim,
        )
    return cells


def collect(piece_own, shifter, up_extra, down_extra):
    rows = piece_own.shape[0] * piece_own.shape[1]
    flat = piece_own.reshape(rows, piece_own.shape[2])
    got_below = shifter(jnp.concatenate([flat, up_extra], axis=0), 1)
    got_above = shifter(jnp.concatenate([flat, down_extra], axis=0), -1)
    below_one = got_below[:rows].reshape(piece_own.shape)
    above_one = got_above[:rows].reshape(piece_own.shape)
    below = shifter(jnp.stack([below_one, piece_own], axis=0), 2)
    above = shifter(jnp.stack([piece_own, above_one], axis=0), -2)
    window = [below[0], below[1], below_one, piece_own, above_one, above[0], above[1]]
    return window, got_below[rows:], got_above[rows:]


def give_back(near, narrow, shifter):
    from_below = shifter(narrow[REACH + 2 :], 2).astype(jnp.float32)
    from_above = shifter(narrow[: REACH - 1], -2).astype(jnp.float32)
    upward = (near[2] + from_below[1]).astype(jnp.bfloat16)
    downward = (near[0] + from_above[0]).astype(jnp.bfloat16)
    return (
        near[1]
        + from_below[0]
        + from_above[1]
        + shifter(upward, 1).astype(jnp.float32)
        + shifter(downward, -1).astype(jnp.float32)
    )


def exchange(block, axis, bit):
    count = lax.axis_size(axis)
    return lax.ppermute(block, axis, [(i, i ^ bit) for i in range(count)])


def halving(acc, axis):
    here = lax.axis_index(axis)
    count = lax.axis_size(axis)
    levels = count.bit_length() - 1
    for level in range(levels):
        half = acc.shape[0] // 2
        mine = (here >> level) % 2
        keep = lax.dynamic_slice_in_dim(acc, mine * half, half, 0)
        send = lax.dynamic_slice_in_dim(acc, (1 - mine) * half, half, 0)
        acc = keep + exchange(send.astype(jnp.bfloat16), axis, 1 << level).astype(jnp.float32)
    return acc[0]


def doubling(acc, axis):
    here = lax.axis_index(axis)
    count = lax.axis_size(axis)
    levels = count.bit_length() - 1
    acc = acc[None]
    for level in range(levels - 1, -1, -1):
        theirs = exchange(acc, axis, 1 << level)
        first = (here >> level) % 2 == 0
        acc = jnp.concatenate(
            [jnp.where(first, acc, theirs), jnp.where(first, theirs, acc)], axis=0
        )
    return acc


def on_device(queries, key_rows, values, cotangent, out_proj, conv_kernel, lengths):
    tokens = queries.shape[1]
    width_heads = queries.shape[2]
    channels = out_proj.shape[1]
    span_blocks = 2 * REACH + 1
    scale_factor = 1.0 / math.sqrt(HDIM)
    halo_width = (KW - 1) // 2
    block_index = lax.axis_index("ctx")
    length_here = lengths[0]
    query_here = queries[0]
    key_here = key_rows[0]
    value_here = values[0]
    cot_here = cotangent[0]
    frames = block_index * tokens + jnp.arange(tokens, dtype=jnp.int32)
    valid_rows = frames < length_here
    key_frames = (block_index - REACH) * tokens + jnp.arange(span_blocks * tokens, dtype=jnp.int32)
    valid_keys = (key_frames >= 0) & (key_frames < length_here)

    def kv_shift(piece_rows, offset_by):
        return passed_along(piece_rows, "ctx", offset_by)

    halo_rows = -(-halo_width // 8) * 8

    def edge_rows(rows_here):
        padded_rows = jnp.pad(rows_here, ((0, halo_rows - halo_width), (0, 0)))
        return padded_rows.reshape(-1, width_heads)

    def edge_back(packed):
        return packed.reshape(halo_rows, channels)[:halo_width]

    gathered, cot_low, cot_high = collect(
        jnp.stack([key_here, value_here], axis=0),
        kv_shift,
        edge_rows(cot_here[tokens - halo_width :]),
        edge_rows(cot_here[:halo_width]),
    )
    cot_wide = jnp.concatenate([edge_back(cot_low), cot_here, edge_back(cot_high)], axis=0)
    kv_rows = span_blocks * tokens
    key_all = jnp.concatenate([block[0] for block in gathered], axis=0)
    value_all = jnp.concatenate([block[1] for block in gathered], axis=0)
    head_mask = (
        jnp.arange(HEADS, dtype=jnp.int32)[:, None, None]
        == (jnp.arange(width_heads, dtype=jnp.int32) // HDIM)[None, None, :]
    )

    def spread(rows):
        return jnp.where(head_mask, rows[None], jnp.zeros((), rows.dtype)).reshape(
            HEADS * tokens, width_heads
        )

    def own_heads(stacked_rows):
        picked = jnp.where(head_mask, stacked_rows.reshape(HEADS, tokens, width_heads), 0.0)
        return jnp.sum(picked, axis=0)

    def contract(lhs, rhs, lhs_dim, rhs_dim):
        return lax.dot_general(
            lhs, rhs, (((lhs_dim,), (rhs_dim,)), ((), ())), preferred_element_type=jnp.float32
        )

    query_spread = spread(query_here)
    scores = contract(query_spread, key_all, 1, 1) * scale_factor
    scores = jnp.where(valid_keys[None, :], scores, -jnp.inf)
    row_max = jnp.max(scores, axis=1, keepdims=True)
    row_total = jnp.sum(jnp.exp(scores - row_max), axis=1, keepdims=True)
    log_total = row_max + jnp.log(row_total)
    weights = jnp.exp(scores - log_total).astype(jnp.bfloat16)
    attended = own_heads(contract(weights, value_all, 1, 0)).astype(jnp.bfloat16)
    hidden = jnp.dot(attended, out_proj, preferred_element_type=jnp.float32)
    masked = jnp.where(valid_rows[:, None], hidden, 0.0).astype(jnp.bfloat16)

    wide_rows = tokens + 2 * halo_width
    padded_m = padded(masked, (("ctx", 0),), 2 * halo_width)
    conv_out = jnp.zeros((wide_rows, channels), jnp.float32)
    for tap_index in range(KW):
        conv_out = conv_out + conv_kernel[tap_index] * padded_m[tap_index : tap_index + wide_rows]
    sigmoid_c = jax.nn.sigmoid(conv_out)
    grad_conv = (
        cot_wide.astype(jnp.float32) * (sigmoid_c + conv_out * sigmoid_c * (1.0 - sigmoid_c))
    ).astype(jnp.bfloat16)
    grad_masked = jnp.zeros((tokens, channels), jnp.float32)
    for tap_index in range(KW):
        start_row = 2 * halo_width - tap_index
        grad_masked = (
            grad_masked + conv_kernel[tap_index] * grad_conv[start_row : start_row + tokens]
        )
    kernel_local = lax.conv_general_dilated(
        padded_m[None, halo_width : halo_width + wide_rows],
        grad_conv[halo_width : halo_width + tokens, None, :],
        window_strides=(1,),
        padding="VALID",
        dimension_numbers=("NWC", "WIO", "NWC"),
        feature_group_count=channels,
        preferred_element_type=jnp.float32,
    )[0]
    grad_hidden = (
        cot_here.astype(jnp.float32) + jnp.where(valid_rows[:, None], grad_masked, 0.0)
    ).astype(jnp.bfloat16)
    proj_local = lax.dot_general(
        attended, grad_hidden, (((0,), (0,)), ((), ())), preferred_element_type=jnp.float32
    )
    ctx_count = lax.axis_size("ctx")
    dp_count = lax.axis_size("dp")
    members = ctx_count * dp_count
    proj_rows = proj_local.shape[0] // members
    kernel_rows = -(-KW // (members * 8)) * 8
    kernel_padded = jnp.pad(kernel_local, ((0, kernel_rows * members - KW), (0, 0)))
    stacked = jnp.concatenate(
        [
            proj_local.reshape(dp_count, ctx_count, proj_rows, channels),
            kernel_padded.reshape(dp_count, ctx_count, kernel_rows, channels),
        ],
        axis=2,
    )
    summed = halving(halving(stacked, "dp"), "ctx").astype(jnp.bfloat16)
    grad_attended = lax.dot_general(
        grad_hidden, out_proj, (((1,), (1,)), ((), ())), preferred_element_type=jnp.float32
    ).astype(jnp.bfloat16)
    delta_rows = jnp.sum(
        (grad_attended.astype(jnp.float32) * attended.astype(jnp.float32)).reshape(
            tokens, HEADS, HDIM
        ),
        axis=2,
    )
    grad_spread = spread(grad_attended)
    grad_weights = contract(grad_spread, value_all, 1, 1)
    grad_logits = (
        weights.astype(jnp.float32) * (grad_weights - delta_rows.T.reshape(HEADS * tokens, 1))
    ).astype(jnp.bfloat16)
    grad_query = (own_heads(contract(grad_logits, key_all, 1, 0)) * scale_factor).astype(
        jnp.bfloat16
    )
    grad_key_all = contract(grad_logits, query_spread, 0, 0) * scale_factor
    grad_value_all = contract(weights, grad_spread, 0, 0)
    key_blocks = grad_key_all.reshape(span_blocks, tokens, width_heads)
    value_blocks = grad_value_all.reshape(span_blocks, tokens, width_heads)
    narrow = jnp.stack([key_blocks, value_blocks], axis=1).astype(jnp.bfloat16)
    near = jnp.stack(
        [key_blocks[REACH - 1 : REACH + 2], value_blocks[REACH - 1 : REACH + 2]], axis=1
    )

    def grad_shift(piece_rows, offset_by):
        return passed_along(piece_rows, "ctx", offset_by)

    gathered = doubling(doubling(summed, "ctx"), "dp")
    proj_sum = gathered[:, :, :proj_rows].reshape(members * proj_rows, channels)
    kernel_sum = (
        gathered[:, :, proj_rows:].astype(jnp.float32).reshape(members * kernel_rows, channels)[:KW]
    )
    own_grads = give_back(near, narrow, grad_shift)
    grad_key = own_grads[0].astype(jnp.bfloat16)
    grad_value = own_grads[1].astype(jnp.bfloat16)
    return (
        grad_query[None],
        grad_key[None],
        grad_value[None],
        proj_sum,
        kernel_sum,
    )


def solution(mesh):
    return jax.shard_map(
        on_device,
        mesh=mesh,
        in_specs=(
            P(("group", "dp"), "ctx", None),
            P(("group", "dp"), "ctx", None),
            P(("group", "dp"), "ctx", None),
            P(("group", "dp"), "ctx", None),
            P(),
            P(),
            P(("group", "dp")),
        ),
        out_specs=(
            P(("group", "dp"), "ctx", None),
            P(("group", "dp"), "ctx", None),
            P(("group", "dp"), "ctx", None),
            P("group", None),
            P("group", None),
        ),
        check_vma=False,
    )
```

```python
import math

import jax
import jax.numpy as jnp
from jax import lax
from jax.sharding import PartitionSpec as P

HEADS = 8
HDIM = 64
KW = 31
REACH = 3


def passed_along(block, axis, distance):
    devices = range(lax.axis_size(axis))
    route = [(i - distance, i) for i in devices if i - distance in devices]
    return lax.ppermute(block, axis, route)


def padded(cells, sides, width):
    for axis, dim in sides:
        count = lax.axis_size(axis)
        ends = count - 1
        head = lax.slice_in_dim(cells, 0, width, axis=dim)
        tail = lax.slice_in_dim(cells, cells.shape[dim] - width, cells.shape[dim], axis=dim)
        cells = jnp.concatenate(
            [
                lax.ppermute(tail, axis, [(i, (i + 1) % count) for i in range(ends)]),
                cells,
                lax.ppermute(head, axis, [((i + 1) % count, i) for i in range(ends)]),
            ],
            axis=dim,
        )
    return cells


def collect(piece_own, shifter, up_extra, down_extra):
    rows = piece_own.shape[0] * piece_own.shape[1]
    flat = piece_own.reshape(rows, piece_own.shape[2])
    got_below = shifter(jnp.concatenate([flat, up_extra], axis=0), 1)
    got_above = shifter(jnp.concatenate([flat, down_extra], axis=0), -1)
    below_one = got_below[:rows].reshape(piece_own.shape)
    above_one = got_above[:rows].reshape(piece_own.shape)
    below = shifter(jnp.stack([below_one, piece_own], axis=0), 2)
    above = shifter(jnp.stack([piece_own, above_one], axis=0), -2)
    window = [below[0], below[1], below_one, piece_own, above_one, above[0], above[1]]
    return window, got_below[rows:], got_above[rows:]


def give_back(near, narrow, shifter):
    from_below = shifter(narrow[REACH + 2 :], 2).astype(jnp.float32)
    from_above = shifter(narrow[: REACH - 1], -2).astype(jnp.float32)
    upward = (near[2] + from_below[1]).astype(jnp.bfloat16)
    downward = (near[0] + from_above[0]).astype(jnp.bfloat16)
    return (
        near[1]
        + from_below[0]
        + from_above[1]
        + shifter(upward, 1).astype(jnp.float32)
        + shifter(downward, -1).astype(jnp.float32)
    )


def exchange(block, axis, bit):
    count = lax.axis_size(axis)
    return lax.ppermute(block, axis, [(i, i ^ bit) for i in range(count)])


def halving(acc, axis):
    here = lax.axis_index(axis)
    count = lax.axis_size(axis)
    levels = count.bit_length() - 1
    for level in range(levels):
        half = acc.shape[0] // 2
        mine = (here >> level) % 2
        keep = lax.dynamic_slice_in_dim(acc, mine * half, half, 0)
        send = lax.dynamic_slice_in_dim(acc, (1 - mine) * half, half, 0)
        acc = keep + exchange(send.astype(jnp.bfloat16), axis, 1 << level).astype(jnp.float32)
    return acc[0]


def doubling(acc, axis):
    here = lax.axis_index(axis)
    count = lax.axis_size(axis)
    levels = count.bit_length() - 1
    acc = acc[None]
    for level in range(levels - 1, -1, -1):
        theirs = exchange(acc, axis, 1 << level)
        first = (here >> level) % 2 == 0
        acc = jnp.concatenate(
            [jnp.where(first, acc, theirs), jnp.where(first, theirs, acc)], axis=0
        )
    return acc


def on_device(queries, key_rows, values, cotangent, out_proj, conv_kernel, lengths):
    tokens = queries.shape[1]
    width_heads = queries.shape[2]
    channels = out_proj.shape[1]
    span_blocks = 2 * REACH + 1
    scale_factor = 1.0 / math.sqrt(HDIM)
    halo_width = (KW - 1) // 2
    block_index = lax.axis_index("ctx")
    length_here = lengths[0]
    query_here = queries[0]
    key_here = key_rows[0]
    value_here = values[0]
    cot_here = cotangent[0]
    frames = block_index * tokens + jnp.arange(tokens, dtype=jnp.int32)
    valid_rows = frames < length_here
    key_frames = (block_index - REACH) * tokens + jnp.arange(span_blocks * tokens, dtype=jnp.int32)
    valid_keys = (key_frames >= 0) & (key_frames < length_here)

    def kv_shift(piece_rows, offset_by):
        return passed_along(piece_rows, "ctx", offset_by)

    halo_rows = -(-halo_width // 8) * 8

    def edge_rows(rows_here):
        padded_rows = jnp.pad(rows_here, ((0, halo_rows - halo_width), (0, 0)))
        return padded_rows.reshape(-1, width_heads)

    def edge_back(packed):
        return packed.reshape(halo_rows, channels)[:halo_width]

    gathered, cot_low, cot_high = collect(
        jnp.stack([key_here, value_here], axis=0),
        kv_shift,
        edge_rows(cot_here[tokens - halo_width :]),
        edge_rows(cot_here[:halo_width]),
    )
    cot_wide = jnp.concatenate([edge_back(cot_low), cot_here, edge_back(cot_high)], axis=0)
    kv_rows = span_blocks * tokens
    key_all = jnp.concatenate([block[0] for block in gathered], axis=0)
    value_all = jnp.concatenate([block[1] for block in gathered], axis=0)
    head_mask = (
        jnp.arange(HEADS, dtype=jnp.int32)[:, None, None]
        == (jnp.arange(width_heads, dtype=jnp.int32) // HDIM)[None, None, :]
    )

    def spread(rows):
        return jnp.where(head_mask, rows[None], jnp.zeros((), rows.dtype)).reshape(
            HEADS * tokens, width_heads
        )

    def own_heads(stacked_rows):
        picked = jnp.where(head_mask, stacked_rows.reshape(HEADS, tokens, width_heads), 0.0)
        return jnp.sum(picked, axis=0)

    def contract(lhs, rhs, lhs_dim, rhs_dim):
        return lax.dot_general(
            lhs, rhs, (((lhs_dim,), (rhs_dim,)), ((), ())), preferred_element_type=jnp.float32
        )

    query_spread = spread(query_here)
    scores = contract(query_spread, key_all, 1, 1) * scale_factor
    scores = jnp.where(valid_keys[None, :], scores, -jnp.inf)
    row_max = jnp.max(scores, axis=1, keepdims=True)
    row_total = jnp.sum(jnp.exp(scores - row_max), axis=1, keepdims=True)
    log_total = row_max + jnp.log(row_total)
    weights = jnp.exp(scores - log_total).astype(jnp.bfloat16)
    attended = own_heads(contract(weights, value_all, 1, 0)).astype(jnp.bfloat16)
    hidden = jnp.dot(attended, out_proj, preferred_element_type=jnp.float32)
    masked = jnp.where(valid_rows[:, None], hidden, 0.0).astype(jnp.bfloat16)

    wide_rows = tokens + 2 * halo_width
    edge = -(-2 * halo_width // 8) * 8
    lead = edge - 2 * halo_width
    padded_m = padded(masked, (("ctx", 0),), edge)
    conv_out = jnp.zeros((wide_rows, channels), jnp.float32)
    for tap_index in range(KW):
        conv_out = conv_out + conv_kernel[tap_index] * padded_m[lead + tap_index : lead + tap_index + wide_rows]
    sigmoid_c = jax.nn.sigmoid(conv_out)
    grad_conv = (
        cot_wide.astype(jnp.float32) * (sigmoid_c + conv_out * sigmoid_c * (1.0 - sigmoid_c))
    ).astype(jnp.bfloat16)
    grad_masked = jnp.zeros((tokens, channels), jnp.float32)
    for tap_index in range(KW):
        start_row = 2 * halo_width - tap_index
        grad_masked = (
            grad_masked + conv_kernel[tap_index] * grad_conv[start_row : start_row + tokens]
        )
    kernel_local = lax.conv_general_dilated(
        padded_m[None, lead + halo_width : lead + halo_width + wide_rows],
        grad_conv[halo_width : halo_width + tokens, None, :],
        window_strides=(1,),
        padding="VALID",
        dimension_numbers=("NWC", "WIO", "NWC"),
        feature_group_count=channels,
        preferred_element_type=jnp.float32,
    )[0]
    grad_hidden = (
        cot_here.astype(jnp.float32) + jnp.where(valid_rows[:, None], grad_masked, 0.0)
    ).astype(jnp.bfloat16)
    proj_local = lax.dot_general(
        attended, grad_hidden, (((0,), (0,)), ((), ())), preferred_element_type=jnp.float32
    )
    ctx_count = lax.axis_size("ctx")
    dp_count = lax.axis_size("dp")
    members = ctx_count * dp_count
    proj_rows = proj_local.shape[0] // members
    kernel_rows = -(-KW // (members * 8)) * 8
    kernel_padded = jnp.pad(kernel_local, ((0, kernel_rows * members - KW), (0, 0)))
    stacked = jnp.concatenate(
        [
            proj_local.reshape(dp_count, ctx_count, proj_rows, channels),
            kernel_padded.reshape(dp_count, ctx_count, kernel_rows, channels),
        ],
        axis=2,
    )
    summed = halving(halving(stacked, "dp"), "ctx").astype(jnp.bfloat16)
    grad_attended = lax.dot_general(
        grad_hidden, out_proj, (((1,), (1,)), ((), ())), preferred_element_type=jnp.float32
    ).astype(jnp.bfloat16)
    delta_rows = jnp.sum(
        (grad_attended.astype(jnp.float32) * attended.astype(jnp.float32)).reshape(
            tokens, HEADS, HDIM
        ),
        axis=2,
    )
    grad_spread = spread(grad_attended)
    grad_weights = contract(grad_spread, value_all, 1, 1)
    grad_logits = (
        weights.astype(jnp.float32) * (grad_weights - delta_rows.T.reshape(HEADS * tokens, 1))
    ).astype(jnp.bfloat16)
    grad_query = (own_heads(contract(grad_logits, key_all, 1, 0)) * scale_factor).astype(
        jnp.bfloat16
    )
    grad_key_all = contract(grad_logits, query_spread, 0, 0) * scale_factor
    grad_value_all = contract(weights, grad_spread, 0, 0)
    key_blocks = grad_key_all.reshape(span_blocks, tokens, width_heads)
    value_blocks = grad_value_all.reshape(span_blocks, tokens, width_heads)
    narrow = jnp.stack([key_blocks, value_blocks], axis=1).astype(jnp.bfloat16)
    near = jnp.stack(
        [key_blocks[REACH - 1 : REACH + 2], value_blocks[REACH - 1 : REACH + 2]], axis=1
    )

    def grad_shift(piece_rows, offset_by):
        return passed_along(piece_rows, "ctx", offset_by)

    gathered = doubling(doubling(summed, "ctx"), "dp")
    proj_sum = gathered[:, :, :proj_rows].reshape(members * proj_rows, channels)
    kernel_sum = (
        gathered[:, :, proj_rows:].astype(jnp.float32).reshape(members * kernel_rows, channels)[:KW]
    )
    own_grads = give_back(near, narrow, grad_shift)
    grad_key = own_grads[0].astype(jnp.bfloat16)
    grad_value = own_grads[1].astype(jnp.bfloat16)
    return (
        grad_query[None],
        grad_key[None],
        grad_value[None],
        proj_sum,
        kernel_sum,
    )


def solution(mesh):
    return jax.shard_map(
        on_device,
        mesh=mesh,
        in_specs=(
            P(("group", "dp"), "ctx", None),
            P(("group", "dp"), "ctx", None),
            P(("group", "dp"), "ctx", None),
            P(("group", "dp"), "ctx", None),
            P(),
            P(),
            P(("group", "dp")),
        ),
        out_specs=(
            P(("group", "dp"), "ctx", None),
            P(("group", "dp"), "ctx", None),
            P(("group", "dp"), "ctx", None),
            P("group", None),
            P("group", None),
        ),
        check_vma=False,
    )
```

```python
import math

import jax
import jax.numpy as jnp
from jax import lax
from jax.sharding import PartitionSpec as P

HEADS = 8
HDIM = 64
KW = 31
REACH = 3


def passed_along(block, axis, distance):
    devices = range(lax.axis_size(axis))
    route = [(i - distance, i) for i in devices if i - distance in devices]
    return lax.ppermute(block, axis, route)


def padded(cells, sides, width):
    for axis, dim in sides:
        count = lax.axis_size(axis)
        ends = count - 1
        head = lax.slice_in_dim(cells, 0, width, axis=dim)
        tail = lax.slice_in_dim(cells, cells.shape[dim] - width, cells.shape[dim], axis=dim)
        cells = jnp.concatenate(
            [
                lax.ppermute(tail, axis, [(i, (i + 1) % count) for i in range(ends)]),
                cells,
                lax.ppermute(head, axis, [((i + 1) % count, i) for i in range(ends)]),
            ],
            axis=dim,
        )
    return cells


def collect(piece_own, shifter, up_extra, down_extra):
    rows = piece_own.shape[0] * piece_own.shape[1]
    flat = piece_own.reshape(rows, piece_own.shape[2])
    got_below = shifter(jnp.concatenate([flat, up_extra], axis=0), 1)
    got_above = shifter(jnp.concatenate([flat, down_extra], axis=0), -1)
    below_one = got_below[:rows].reshape(piece_own.shape)
    above_one = got_above[:rows].reshape(piece_own.shape)
    below = shifter(jnp.stack([below_one, piece_own], axis=0), 2)
    above = shifter(jnp.stack([piece_own, above_one], axis=0), -2)
    window = [below[0], below[1], below_one, piece_own, above_one, above[0], above[1]]
    return window, got_below[rows:], got_above[rows:]


def give_back(near, narrow, shifter):
    from_below = shifter(narrow[REACH + 2 :], 2).astype(jnp.float32)
    from_above = shifter(narrow[: REACH - 1], -2).astype(jnp.float32)
    upward = (near[2] + from_below[1]).astype(jnp.bfloat16)
    downward = (near[0] + from_above[0]).astype(jnp.bfloat16)
    return (
        near[1]
        + from_below[0]
        + from_above[1]
        + shifter(upward, 1).astype(jnp.float32)
        + shifter(downward, -1).astype(jnp.float32)
    )


def exchange(block, axis, bit):
    count = lax.axis_size(axis)
    return lax.ppermute(block, axis, [(i, i ^ bit) for i in range(count)])


def halving(acc, axis):
    here = lax.axis_index(axis)
    count = lax.axis_size(axis)
    levels = count.bit_length() - 1
    for level in range(levels):
        half = acc.shape[0] // 2
        mine = (here >> level) % 2
        keep = lax.dynamic_slice_in_dim(acc, mine * half, half, 0)
        send = lax.dynamic_slice_in_dim(acc, (1 - mine) * half, half, 0)
        acc = keep + exchange(send.astype(jnp.bfloat16), axis, 1 << level).astype(jnp.float32)
    return acc[0]


def doubling(acc, axis):
    here = lax.axis_index(axis)
    count = lax.axis_size(axis)
    levels = count.bit_length() - 1
    acc = acc[None]
    for level in range(levels - 1, -1, -1):
        theirs = exchange(acc, axis, 1 << level)
        first = (here >> level) % 2 == 0
        acc = jnp.concatenate(
            [jnp.where(first, acc, theirs), jnp.where(first, theirs, acc)], axis=0
        )
    return acc


def on_device(queries, key_rows, values, cotangent, out_proj, conv_kernel, lengths):
    tokens = queries.shape[1]
    width_heads = queries.shape[2]
    channels = out_proj.shape[1]
    span_blocks = 2 * REACH + 1
    scale_factor = 1.0 / math.sqrt(HDIM)
    halo_width = (KW - 1) // 2
    block_index = lax.axis_index("ctx")
    length_here = lengths[0]
    query_here = queries[0]
    key_here = key_rows[0]
    value_here = values[0]
    cot_here = cotangent[0]
    frames = block_index * tokens + jnp.arange(tokens, dtype=jnp.int32)
    valid_rows = frames < length_here
    key_frames = (block_index - REACH) * tokens + jnp.arange(span_blocks * tokens, dtype=jnp.int32)
    valid_keys = (key_frames >= 0) & (key_frames < length_here)

    def kv_shift(piece_rows, offset_by):
        return passed_along(piece_rows, "ctx", offset_by)

    halo_rows = -(-halo_width // 8) * 8

    def edge_rows(rows_here):
        return rows_here.reshape(-1, width_heads)

    def edge_back(packed):
        return packed.reshape(halo_rows, channels)

    gathered, cot_low, cot_high = collect(
        jnp.stack([key_here, value_here], axis=0),
        kv_shift,
        edge_rows(cot_here[tokens - halo_rows :]),
        edge_rows(cot_here[:halo_rows]),
    )
    cot_wide = jnp.concatenate([edge_back(cot_low), cot_here, edge_back(cot_high)], axis=0)
    kv_rows = span_blocks * tokens
    key_all = jnp.concatenate([block[0] for block in gathered], axis=0)
    value_all = jnp.concatenate([block[1] for block in gathered], axis=0)
    head_mask = (
        jnp.arange(HEADS, dtype=jnp.int32)[:, None, None]
        == (jnp.arange(width_heads, dtype=jnp.int32) // HDIM)[None, None, :]
    )

    def spread(rows):
        return jnp.where(head_mask, rows[None], jnp.zeros((), rows.dtype)).reshape(
            HEADS * tokens, width_heads
        )

    def own_heads(stacked_rows):
        picked = jnp.where(head_mask, stacked_rows.reshape(HEADS, tokens, width_heads), 0.0)
        return jnp.sum(picked, axis=0)

    def contract(lhs, rhs, lhs_dim, rhs_dim):
        return lax.dot_general(
            lhs, rhs, (((lhs_dim,), (rhs_dim,)), ((), ())), preferred_element_type=jnp.float32
        )

    query_spread = spread(query_here)
    scores = contract(query_spread, key_all, 1, 1) * scale_factor
    scores = jnp.where(valid_keys[None, :], scores, -jnp.inf)
    row_max = jnp.max(scores, axis=1, keepdims=True)
    row_total = jnp.sum(jnp.exp(scores - row_max), axis=1, keepdims=True)
    log_total = row_max + jnp.log(row_total)
    weights = jnp.exp(scores - log_total).astype(jnp.bfloat16)
    attended = own_heads(contract(weights, value_all, 1, 0)).astype(jnp.bfloat16)
    hidden = jnp.dot(attended, out_proj, preferred_element_type=jnp.float32)
    masked = jnp.where(valid_rows[:, None], hidden, 0.0).astype(jnp.bfloat16)

    wide_rows = tokens + 2 * halo_rows
    edge = -(-2 * halo_width // 8) * 8
    lead = edge - halo_rows - halo_width
    padded_m = padded(masked, (("ctx", 0),), edge)
    conv_out = jnp.zeros((wide_rows, channels), jnp.float32)
    for tap_index in range(KW):
        conv_out = conv_out + conv_kernel[tap_index] * padded_m[lead + tap_index : lead + tap_index + wide_rows]
    sigmoid_c = jax.nn.sigmoid(conv_out)
    grad_conv = (
        cot_wide.astype(jnp.float32) * (sigmoid_c + conv_out * sigmoid_c * (1.0 - sigmoid_c))
    ).astype(jnp.bfloat16)
    grad_masked = jnp.zeros((tokens, channels), jnp.float32)
    for tap_index in range(KW):
        start_row = halo_rows + halo_width - tap_index
        grad_masked = (
            grad_masked + conv_kernel[tap_index] * grad_conv[start_row : start_row + tokens]
        )
    kernel_local = lax.conv_general_dilated(
        padded_m[None, edge - halo_width : edge + tokens + halo_width],
        grad_conv[halo_rows : halo_rows + tokens, None, :],
        window_strides=(1,),
        padding="VALID",
        dimension_numbers=("NWC", "WIO", "NWC"),
        feature_group_count=channels,
        preferred_element_type=jnp.float32,
    )[0]
    grad_hidden = (
        cot_here.astype(jnp.float32) + jnp.where(valid_rows[:, None], grad_masked, 0.0)
    ).astype(jnp.bfloat16)
    proj_local = lax.dot_general(
        attended, grad_hidden, (((0,), (0,)), ((), ())), preferred_element_type=jnp.float32
    )
    ctx_count = lax.axis_size("ctx")
    dp_count = lax.axis_size("dp")
    members = ctx_count * dp_count
    proj_rows = proj_local.shape[0] // members
    kernel_rows = -(-KW // (members * 8)) * 8
    kernel_padded = jnp.pad(kernel_local, ((0, kernel_rows * members - KW), (0, 0)))
    stacked = jnp.concatenate(
        [
            proj_local.reshape(dp_count, ctx_count, proj_rows, channels),
            kernel_padded.reshape(dp_count, ctx_count, kernel_rows, channels),
        ],
        axis=2,
    )
    summed = halving(halving(stacked, "dp"), "ctx").astype(jnp.bfloat16)
    grad_attended = lax.dot_general(
        grad_hidden, out_proj, (((1,), (1,)), ((), ())), preferred_element_type=jnp.float32
    ).astype(jnp.bfloat16)
    delta_rows = jnp.sum(
        (grad_attended.astype(jnp.float32) * attended.astype(jnp.float32)).reshape(
            tokens, HEADS, HDIM
        ),
        axis=2,
    )
    grad_spread = spread(grad_attended)
    grad_weights = contract(grad_spread, value_all, 1, 1)
    grad_logits = (
        weights.astype(jnp.float32) * (grad_weights - delta_rows.T.reshape(HEADS * tokens, 1))
    ).astype(jnp.bfloat16)
    grad_query = (own_heads(contract(grad_logits, key_all, 1, 0)) * scale_factor).astype(
        jnp.bfloat16
    )
    grad_key_all = contract(grad_logits, query_spread, 0, 0) * scale_factor
    grad_value_all = contract(weights, grad_spread, 0, 0)
    key_blocks = grad_key_all.reshape(span_blocks, tokens, width_heads)
    value_blocks = grad_value_all.reshape(span_blocks, tokens, width_heads)
    narrow = jnp.stack([key_blocks, value_blocks], axis=1).astype(jnp.bfloat16)
    near = jnp.stack(
        [key_blocks[REACH - 1 : REACH + 2], value_blocks[REACH - 1 : REACH + 2]], axis=1
    )

    def grad_shift(piece_rows, offset_by):
        return passed_along(piece_rows, "ctx", offset_by)

    gathered = doubling(doubling(summed, "ctx"), "dp")
    proj_sum = gathered[:, :, :proj_rows].reshape(members * proj_rows, channels)
    kernel_sum = (
        gathered[:, :, proj_rows:].astype(jnp.float32).reshape(members * kernel_rows, channels)[:KW]
    )
    own_grads = give_back(near, narrow, grad_shift)
    grad_key = own_grads[0].astype(jnp.bfloat16)
    grad_value = own_grads[1].astype(jnp.bfloat16)
    return (
        grad_query[None],
        grad_key[None],
        grad_value[None],
        proj_sum,
        kernel_sum,
    )


def solution(mesh):
    return jax.shard_map(
        on_device,
        mesh=mesh,
        in_specs=(
            P(("group", "dp"), "ctx", None),
            P(("group", "dp"), "ctx", None),
            P(("group", "dp"), "ctx", None),
            P(("group", "dp"), "ctx", None),
            P(),
            P(),
            P(("group", "dp")),
        ),
        out_specs=(
            P(("group", "dp"), "ctx", None),
            P(("group", "dp"), "ctx", None),
            P(("group", "dp"), "ctx", None),
            P("group", None),
            P("group", None),
        ),
        check_vma=False,
    )
```

```python
import math

import jax
import jax.numpy as jnp
from jax import lax
from jax.sharding import PartitionSpec as P

HEADS = 8
HDIM = 64
KW = 31
REACH = 3


def passed_along(block, axis, distance):
    devices = range(lax.axis_size(axis))
    route = [(i - distance, i) for i in devices if i - distance in devices]
    return lax.ppermute(block, axis, route)


def padded(cells, sides, width):
    for axis, dim in sides:
        count = lax.axis_size(axis)
        ends = count - 1
        head = lax.slice_in_dim(cells, 0, width, axis=dim)
        tail = lax.slice_in_dim(cells, cells.shape[dim] - width, cells.shape[dim], axis=dim)
        cells = jnp.concatenate(
            [
                lax.ppermute(tail, axis, [(i, (i + 1) % count) for i in range(ends)]),
                cells,
                lax.ppermute(head, axis, [((i + 1) % count, i) for i in range(ends)]),
            ],
            axis=dim,
        )
    return cells


def collect(piece_own, shifter, up_extra, down_extra):
    rows = piece_own.shape[0] * piece_own.shape[1]
    flat = piece_own.reshape(rows, piece_own.shape[2])
    got_below = shifter(jnp.concatenate([flat, up_extra], axis=0), 1)
    got_above = shifter(jnp.concatenate([flat, down_extra], axis=0), -1)
    below_one = got_below[:rows].reshape(piece_own.shape)
    above_one = got_above[:rows].reshape(piece_own.shape)
    below = shifter(jnp.stack([below_one, piece_own], axis=0), 2)
    above = shifter(jnp.stack([piece_own, above_one], axis=0), -2)
    window = [below[0], below[1], below_one, piece_own, above_one, above[0], above[1]]
    return window, got_below[rows:], got_above[rows:]


def give_back(near, narrow, shifter):
    from_below = shifter(narrow[REACH + 2 :], 2).astype(jnp.float32)
    from_above = shifter(narrow[: REACH - 1], -2).astype(jnp.float32)
    upward = (near[2] + from_below[1]).astype(jnp.bfloat16)
    downward = (near[0] + from_above[0]).astype(jnp.bfloat16)
    return (
        near[1]
        + from_below[0]
        + from_above[1]
        + shifter(upward, 1).astype(jnp.float32)
        + shifter(downward, -1).astype(jnp.float32)
    )


def exchange(block, axis, bit):
    count = lax.axis_size(axis)
    return lax.ppermute(block, axis, [(i, i ^ bit) for i in range(count)])


def halving(acc, axis):
    here = lax.axis_index(axis)
    count = lax.axis_size(axis)
    levels = count.bit_length() - 1
    for level in range(levels):
        half = acc.shape[0] // 2
        mine = (here >> level) % 2
        keep = lax.dynamic_slice_in_dim(acc, mine * half, half, 0)
        send = lax.dynamic_slice_in_dim(acc, (1 - mine) * half, half, 0)
        acc = keep + exchange(send.astype(jnp.bfloat16), axis, 1 << level).astype(jnp.float32)
    return acc[0]


def doubling(acc, axis):
    here = lax.axis_index(axis)
    count = lax.axis_size(axis)
    levels = count.bit_length() - 1
    acc = acc[None]
    for level in range(levels - 1, -1, -1):
        theirs = exchange(acc, axis, 1 << level)
        first = (here >> level) % 2 == 0
        acc = jnp.concatenate(
            [jnp.where(first, acc, theirs), jnp.where(first, theirs, acc)], axis=0
        )
    return acc


def on_device(queries, key_rows, values, cotangent, out_proj, conv_kernel, lengths):
    tokens = queries.shape[1]
    width_heads = queries.shape[2]
    channels = out_proj.shape[1]
    span_blocks = 2 * REACH + 1
    scale_factor = 1.0 / math.sqrt(HDIM)
    halo_width = (KW - 1) // 2
    block_index = lax.axis_index("ctx")
    length_here = lengths[0]
    query_here = queries[0]
    key_here = key_rows[0]
    value_here = values[0]
    cot_here = cotangent[0]
    frames = block_index * tokens + jnp.arange(tokens, dtype=jnp.int32)
    valid_rows = frames < length_here
    key_frames = (block_index - REACH) * tokens + jnp.arange(span_blocks * tokens, dtype=jnp.int32)
    valid_keys = (key_frames >= 0) & (key_frames < length_here)

    def kv_shift(piece_rows, offset_by):
        return passed_along(piece_rows, "ctx", offset_by)

    halo_rows = -(-halo_width // 8) * 8

    def edge_rows(rows_here):
        return rows_here.reshape(-1, width_heads)

    def edge_back(packed):
        return packed.reshape(halo_rows, channels)

    gathered, cot_low, cot_high = collect(
        jnp.stack([key_here, value_here], axis=0),
        kv_shift,
        edge_rows(cot_here[tokens - halo_rows :]),
        edge_rows(cot_here[:halo_rows]),
    )
    cot_wide = jnp.concatenate([edge_back(cot_low), cot_here, edge_back(cot_high)], axis=0)
    kv_rows = span_blocks * tokens
    key_all = jnp.concatenate([block[0] for block in gathered], axis=0)
    value_all = jnp.concatenate([block[1] for block in gathered], axis=0)
    head_mask = (
        jnp.arange(HEADS, dtype=jnp.int32)[:, None, None]
        == (jnp.arange(width_heads, dtype=jnp.int32) // HDIM)[None, None, :]
    )

    def spread(rows):
        return jnp.where(head_mask, rows[None], jnp.zeros((), rows.dtype)).reshape(
            HEADS * tokens, width_heads
        )

    def own_heads(stacked_rows):
        picked = jnp.where(head_mask, stacked_rows.reshape(HEADS, tokens, width_heads), 0.0)
        return jnp.sum(picked, axis=0)

    def contract(lhs, rhs, lhs_dim, rhs_dim):
        return lax.dot_general(
            lhs, rhs, (((lhs_dim,), (rhs_dim,)), ((), ())), preferred_element_type=jnp.float32
        )

    query_spread = spread(query_here)
    scores = contract(query_spread, key_all, 1, 1) * scale_factor
    scores = jnp.where(valid_keys[None, :], scores, -jnp.inf)
    row_max = jnp.max(scores, axis=1, keepdims=True)
    row_total = jnp.sum(jnp.exp(scores - row_max), axis=1, keepdims=True)
    log_total = row_max + jnp.log(row_total)
    weights = jnp.exp(scores - log_total).astype(jnp.bfloat16)
    attended = own_heads(contract(weights, value_all, 1, 0)).astype(jnp.bfloat16)
    hidden = jnp.dot(attended, out_proj, preferred_element_type=jnp.float32)
    masked = jnp.where(valid_rows[:, None], hidden, 0.0).astype(jnp.bfloat16)

    wide_rows = tokens + 2 * halo_rows
    edge = -(-2 * halo_width // 8) * 8
    lead = edge - halo_rows - halo_width
    padded_m = padded(masked, (("ctx", 0),), edge)
    conv_out = jnp.zeros((wide_rows, channels), jnp.float32)
    for tap_index in range(KW):
        conv_out = conv_out + conv_kernel[tap_index] * padded_m[lead + tap_index : lead + tap_index + wide_rows]
    sigmoid_c = jax.nn.sigmoid(conv_out)
    grad_conv = (
        cot_wide.astype(jnp.float32) * (sigmoid_c + conv_out * sigmoid_c * (1.0 - sigmoid_c))
    ).astype(jnp.bfloat16)
    grad_masked = jnp.zeros((tokens, channels), jnp.float32)
    for tap_index in range(KW):
        start_row = halo_rows + halo_width - tap_index
        grad_masked = (
            grad_masked + conv_kernel[tap_index] * grad_conv[start_row : start_row + tokens]
        )
    kernel_local = lax.conv_general_dilated(
        padded_m[None, edge - halo_width : edge + tokens + halo_width],
        grad_conv[halo_rows : halo_rows + tokens, None, :],
        window_strides=(1,),
        padding="VALID",
        dimension_numbers=("NWC", "WIO", "NWC"),
        feature_group_count=channels,
        preferred_element_type=jnp.float32,
    )[0]
    grad_hidden = (
        cot_here.astype(jnp.float32) + jnp.where(valid_rows[:, None], grad_masked, 0.0)
    ).astype(jnp.bfloat16)
    proj_local = lax.dot_general(
        attended, grad_hidden, (((0,), (0,)), ((), ())), preferred_element_type=jnp.float32
    )
    ctx_count = lax.axis_size("ctx")
    dp_count = lax.axis_size("dp")
    members = ctx_count * dp_count
    proj_rows = proj_local.shape[0] // members
    kernel_rows = -(-KW // (members * 8)) * 8
    kernel_padded = jnp.pad(kernel_local, ((0, kernel_rows * members - KW), (0, 0)))
    stacked = jnp.concatenate(
        [
            proj_local.reshape(dp_count, ctx_count, proj_rows, channels),
            kernel_padded.reshape(dp_count, ctx_count, kernel_rows, channels),
        ],
        axis=2,
    )
    summed = halving(halving(stacked, "dp"), "ctx").astype(jnp.bfloat16)
    grad_attended = lax.dot_general(
        grad_hidden, out_proj, (((1,), (1,)), ((), ())), preferred_element_type=jnp.float32
    ).astype(jnp.bfloat16)
    delta_rows = jnp.sum(
        (grad_attended.astype(jnp.float32) * attended.astype(jnp.float32)).reshape(
            tokens, HEADS, HDIM
        ),
        axis=2,
    )
    grad_spread = spread(grad_attended)
    grad_weights = contract(grad_spread, value_all, 1, 1)
    grad_logits = (
        weights.astype(jnp.float32) * (grad_weights - delta_rows.T.reshape(HEADS * tokens, 1))
    ).astype(jnp.bfloat16)
    grad_query = (own_heads(contract(grad_logits, key_all, 1, 0)) * scale_factor).astype(
        jnp.bfloat16
    )
    grad_key_all = contract(grad_logits, query_spread, 0, 0) * scale_factor
    grad_value_all = contract(weights, grad_spread, 0, 0)
    key_blocks = grad_key_all.reshape(span_blocks, tokens, width_heads)
    value_blocks = grad_value_all.reshape(span_blocks, tokens, width_heads)
    narrow = jnp.stack([key_blocks, value_blocks], axis=1).astype(jnp.bfloat16)
    near = [jnp.stack([key_blocks[row], value_blocks[row]], axis=0) for row in range(REACH - 1, REACH + 2)]

    def grad_shift(piece_rows, offset_by):
        return passed_along(piece_rows, "ctx", offset_by)

    gathered = doubling(doubling(summed, "ctx"), "dp")
    proj_sum = gathered[:, :, :proj_rows].reshape(members * proj_rows, channels)
    kernel_sum = (
        gathered[:, :, proj_rows:].astype(jnp.float32).reshape(members * kernel_rows, channels)[:KW]
    )
    own_grads = give_back(near, narrow, grad_shift)
    grad_key = own_grads[0].astype(jnp.bfloat16)
    grad_value = own_grads[1].astype(jnp.bfloat16)
    return (
        grad_query[None],
        grad_key[None],
        grad_value[None],
        proj_sum,
        kernel_sum,
    )


def solution(mesh):
    return jax.shard_map(
        on_device,
        mesh=mesh,
        in_specs=(
            P(("group", "dp"), "ctx", None),
            P(("group", "dp"), "ctx", None),
            P(("group", "dp"), "ctx", None),
            P(("group", "dp"), "ctx", None),
            P(),
            P(),
            P(("group", "dp")),
        ),
        out_specs=(
            P(("group", "dp"), "ctx", None),
            P(("group", "dp"), "ctx", None),
            P(("group", "dp"), "ctx", None),
            P("group", None),
            P("group", None),
        ),
        check_vma=False,
    )
```

```python
import math

import jax
import jax.numpy as jnp
from jax import lax
from jax.sharding import PartitionSpec as P

HEADS = 8
HDIM = 64
KW = 31
REACH = 3


def passed_along(block, axis, distance):
    devices = range(lax.axis_size(axis))
    route = [(i - distance, i) for i in devices if i - distance in devices]
    return lax.ppermute(block, axis, route)


def padded(cells, sides, width):
    for axis, dim in sides:
        count = lax.axis_size(axis)
        ends = count - 1
        head = lax.slice_in_dim(cells, 0, width, axis=dim)
        tail = lax.slice_in_dim(cells, cells.shape[dim] - width, cells.shape[dim], axis=dim)
        cells = jnp.concatenate(
            [
                lax.ppermute(tail, axis, [(i, (i + 1) % count) for i in range(ends)]),
                cells,
                lax.ppermute(head, axis, [((i + 1) % count, i) for i in range(ends)]),
            ],
            axis=dim,
        )
    return cells


def collect(piece_own, shifter, up_extra, down_extra):
    rows = piece_own.shape[0] * piece_own.shape[1]
    flat = piece_own.reshape(rows, piece_own.shape[2])
    got_below = shifter(jnp.concatenate([flat, up_extra], axis=0), 1)
    got_above = shifter(jnp.concatenate([flat, down_extra], axis=0), -1)
    below_one = got_below[:rows].reshape(piece_own.shape)
    above_one = got_above[:rows].reshape(piece_own.shape)
    below = shifter(jnp.stack([below_one, piece_own], axis=0), 2)
    above = shifter(jnp.stack([piece_own, above_one], axis=0), -2)
    window = [below[0], below[1], below_one, piece_own, above_one, above[0], above[1]]
    return window, got_below[rows:], got_above[rows:]


def give_back(near, narrow, shifter):
    from_below = shifter(narrow[REACH + 2 :], 2).astype(jnp.float32)
    from_above = shifter(narrow[: REACH - 1], -2).astype(jnp.float32)
    upward = (near[2] + from_below[1]).astype(jnp.bfloat16)
    downward = (near[0] + from_above[0]).astype(jnp.bfloat16)
    return (
        near[1]
        + from_below[0]
        + from_above[1]
        + shifter(upward, 1).astype(jnp.float32)
        + shifter(downward, -1).astype(jnp.float32)
    )


def exchange(block, axis, bit):
    count = lax.axis_size(axis)
    return lax.ppermute(block, axis, [(i, i ^ bit) for i in range(count)])


def halving(acc, axis):
    here = lax.axis_index(axis)
    count = lax.axis_size(axis)
    levels = count.bit_length() - 1
    for level in range(levels):
        half = acc.shape[0] // 2
        mine = (here >> level) % 2
        keep = lax.dynamic_slice_in_dim(acc, mine * half, half, 0)
        send = lax.dynamic_slice_in_dim(acc, (1 - mine) * half, half, 0)
        acc = keep + exchange(send.astype(jnp.bfloat16), axis, 1 << level).astype(jnp.float32)
    return acc[0]


def doubling(acc, axis):
    here = lax.axis_index(axis)
    count = lax.axis_size(axis)
    levels = count.bit_length() - 1
    acc = acc[None]
    for level in range(levels - 1, -1, -1):
        theirs = exchange(acc, axis, 1 << level)
        first = (here >> level) % 2 == 0
        acc = jnp.concatenate(
            [jnp.where(first, acc, theirs), jnp.where(first, theirs, acc)], axis=0
        )
    return acc


def on_device(queries, key_rows, values, cotangent, out_proj, conv_kernel, lengths):
    tokens = queries.shape[1]
    width_heads = queries.shape[2]
    channels = out_proj.shape[1]
    span_blocks = 2 * REACH + 1
    scale_factor = 1.0 / math.sqrt(HDIM)
    halo_width = (KW - 1) // 2
    block_index = lax.axis_index("ctx")
    length_here = lengths[0]
    query_here = queries[0]
    key_here = key_rows[0]
    value_here = values[0]
    cot_here = cotangent[0]
    frames = block_index * tokens + jnp.arange(tokens, dtype=jnp.int32)
    valid_rows = frames < length_here
    key_frames = (block_index - REACH) * tokens + jnp.arange(span_blocks * tokens, dtype=jnp.int32)
    valid_keys = (key_frames >= 0) & (key_frames < length_here)

    def kv_shift(piece_rows, offset_by):
        return passed_along(piece_rows, "ctx", offset_by)

    halo_rows = -(-halo_width // 8) * 8

    def edge_rows(rows_here):
        return rows_here.reshape(-1, width_heads)

    def edge_back(packed):
        return packed.reshape(halo_rows, channels)

    gathered, cot_low, cot_high = collect(
        jnp.stack([key_here, value_here], axis=0),
        kv_shift,
        edge_rows(cot_here[tokens - halo_rows :]),
        edge_rows(cot_here[:halo_rows]),
    )
    cot_wide = jnp.concatenate([edge_back(cot_low), cot_here, edge_back(cot_high)], axis=0)
    kv_rows = span_blocks * tokens
    key_all = jnp.concatenate([block[0] for block in gathered], axis=0)
    value_all = jnp.concatenate([block[1] for block in gathered], axis=0)
    head_mask = (
        jnp.arange(HEADS, dtype=jnp.int32)[:, None, None]
        == (jnp.arange(width_heads, dtype=jnp.int32) // HDIM)[None, None, :]
    )

    def spread(rows):
        return jnp.where(head_mask, rows[None], jnp.zeros((), rows.dtype)).reshape(
            HEADS * tokens, width_heads
        )

    def own_heads(stacked_rows):
        picked = jnp.where(head_mask, stacked_rows.reshape(HEADS, tokens, width_heads), 0.0)
        return jnp.sum(picked, axis=0)

    def contract(lhs, rhs, lhs_dim, rhs_dim):
        return lax.dot_general(
            lhs, rhs, (((lhs_dim,), (rhs_dim,)), ((), ())), preferred_element_type=jnp.float32
        )

    query_spread = spread(query_here)
    scores = contract(query_spread, key_all, 1, 1) * scale_factor
    scores = jnp.where(valid_keys[None, :], scores, -jnp.inf)
    row_max = jnp.max(scores, axis=1, keepdims=True)
    row_total = jnp.sum(jnp.exp(scores - row_max), axis=1, keepdims=True)
    log_total = row_max + jnp.log(row_total)
    weights = jnp.exp(scores - log_total).astype(jnp.bfloat16)
    attended = own_heads(contract(weights, value_all, 1, 0)).astype(jnp.bfloat16)
    hidden = jnp.dot(attended, out_proj, preferred_element_type=jnp.float32)
    masked = jnp.where(valid_rows[:, None], hidden, 0.0).astype(jnp.bfloat16)

    wide_rows = tokens + 2 * halo_rows
    edge = -(-2 * halo_width // 8) * 8
    lead = edge - halo_rows - halo_width
    padded_m = padded(masked, (("ctx", 0),), edge)
    conv_out = jnp.zeros((wide_rows, channels), jnp.float32)
    for tap_index in range(KW):
        conv_out = conv_out + conv_kernel[tap_index] * padded_m[lead + tap_index : lead + tap_index + wide_rows]
    sigmoid_c = jax.nn.sigmoid(conv_out)
    grad_conv = (
        cot_wide.astype(jnp.float32) * (sigmoid_c + conv_out * sigmoid_c * (1.0 - sigmoid_c))
    ).astype(jnp.bfloat16)
    grad_masked = jnp.zeros((tokens, channels), jnp.float32)
    for tap_index in range(KW):
        start_row = halo_rows + halo_width - tap_index
        grad_masked = (
            grad_masked + conv_kernel[tap_index] * grad_conv[start_row : start_row + tokens]
        )
    kernel_local = lax.conv_general_dilated(
        padded_m[None, edge - halo_width : edge + tokens + halo_width],
        grad_conv[halo_rows : halo_rows + tokens, None, :],
        window_strides=(1,),
        padding="VALID",
        dimension_numbers=("NWC", "WIO", "NWC"),
        feature_group_count=channels,
        preferred_element_type=jnp.float32,
    )[0]
    grad_hidden = (
        cot_here.astype(jnp.float32) + jnp.where(valid_rows[:, None], grad_masked, 0.0)
    ).astype(jnp.bfloat16)
    proj_local = lax.dot_general(
        attended, grad_hidden, (((0,), (0,)), ((), ())), preferred_element_type=jnp.float32
    )
    ctx_count = lax.axis_size("ctx")
    dp_count = lax.axis_size("dp")
    members = ctx_count * dp_count
    proj_rows = proj_local.shape[0] // members
    kernel_rows = -(-KW // (members * 16)) * 16
    kernel_padded = jnp.pad(kernel_local, ((0, kernel_rows * members - KW), (0, 0)))
    stacked = jnp.concatenate(
        [
            proj_local.reshape(dp_count, ctx_count, proj_rows, channels),
            kernel_padded.reshape(dp_count, ctx_count, kernel_rows, channels),
        ],
        axis=2,
    )
    summed = halving(halving(stacked, "dp"), "ctx").astype(jnp.bfloat16)
    grad_attended = lax.dot_general(
        grad_hidden, out_proj, (((1,), (1,)), ((), ())), preferred_element_type=jnp.float32
    ).astype(jnp.bfloat16)
    delta_rows = jnp.sum(
        (grad_attended.astype(jnp.float32) * attended.astype(jnp.float32)).reshape(
            tokens, HEADS, HDIM
        ),
        axis=2,
    )
    grad_spread = spread(grad_attended)
    grad_weights = contract(grad_spread, value_all, 1, 1)
    grad_logits = (
        weights.astype(jnp.float32) * (grad_weights - delta_rows.T.reshape(HEADS * tokens, 1))
    ).astype(jnp.bfloat16)
    grad_query = (own_heads(contract(grad_logits, key_all, 1, 0)) * scale_factor).astype(
        jnp.bfloat16
    )
    grad_key_all = contract(grad_logits, query_spread, 0, 0) * scale_factor
    grad_value_all = contract(weights, grad_spread, 0, 0)
    key_blocks = grad_key_all.reshape(span_blocks, tokens, width_heads)
    value_blocks = grad_value_all.reshape(span_blocks, tokens, width_heads)
    narrow = jnp.stack([key_blocks, value_blocks], axis=1).astype(jnp.bfloat16)
    near = jnp.stack(
        [key_blocks[REACH - 1 : REACH + 2], value_blocks[REACH - 1 : REACH + 2]], axis=1
    )

    def grad_shift(piece_rows, offset_by):
        return passed_along(piece_rows, "ctx", offset_by)

    gathered = doubling(doubling(summed, "ctx"), "dp")
    proj_sum = gathered[:, :, :proj_rows].reshape(members * proj_rows, channels)
    kernel_sum = (
        gathered[:, :, proj_rows:].astype(jnp.float32).reshape(members * kernel_rows, channels)[:KW]
    )
    own_grads = give_back(near, narrow, grad_shift)
    grad_key = own_grads[0].astype(jnp.bfloat16)
    grad_value = own_grads[1].astype(jnp.bfloat16)
    return (
        grad_query[None],
        grad_key[None],
        grad_value[None],
        proj_sum,
        kernel_sum,
    )


def solution(mesh):
    return jax.shard_map(
        on_device,
        mesh=mesh,
        in_specs=(
            P(("group", "dp"), "ctx", None),
            P(("group", "dp"), "ctx", None),
            P(("group", "dp"), "ctx", None),
            P(("group", "dp"), "ctx", None),
            P(),
            P(),
            P(("group", "dp")),
        ),
        out_specs=(
            P(("group", "dp"), "ctx", None),
            P(("group", "dp"), "ctx", None),
            P(("group", "dp"), "ctx", None),
            P("group", None),
            P("group", None),
        ),
        check_vma=False,
    )
```

```python
import math

import jax
import jax.numpy as jnp
from jax import lax
from jax.sharding import PartitionSpec as P

HEADS = 8
HDIM = 64
KW = 31
REACH = 3


def passed_along(block, axis, distance):
    devices = range(lax.axis_size(axis))
    route = [(i - distance, i) for i in devices if i - distance in devices]
    return lax.ppermute(block, axis, route)


def padded(cells, sides, width):
    for axis, dim in sides:
        count = lax.axis_size(axis)
        ends = count - 1
        head = lax.slice_in_dim(cells, 0, width, axis=dim)
        tail = lax.slice_in_dim(cells, cells.shape[dim] - width, cells.shape[dim], axis=dim)
        cells = jnp.concatenate(
            [
                lax.ppermute(tail, axis, [(i, (i + 1) % count) for i in range(ends)]),
                cells,
                lax.ppermute(head, axis, [((i + 1) % count, i) for i in range(ends)]),
            ],
            axis=dim,
        )
    return cells


def collect(piece_own, shifter, up_extra, down_extra):
    rows = piece_own.shape[0] * piece_own.shape[1]
    flat = piece_own.reshape(rows, piece_own.shape[2])
    got_below = shifter(jnp.concatenate([flat, up_extra], axis=0), 1)
    got_above = shifter(jnp.concatenate([flat, down_extra], axis=0), -1)
    below_one = got_below[:rows].reshape(piece_own.shape)
    above_one = got_above[:rows].reshape(piece_own.shape)
    below = shifter(jnp.stack([below_one, piece_own], axis=0), 2)
    above = shifter(jnp.stack([piece_own, above_one], axis=0), -2)
    window = [below[0], below[1], below_one, piece_own, above_one, above[0], above[1]]
    return window, got_below[rows:], got_above[rows:]


def give_back(near, narrow, shifter):
    from_below = shifter(narrow[REACH + 2 :], 2).astype(jnp.float32)
    from_above = shifter(narrow[: REACH - 1], -2).astype(jnp.float32)
    upward = (near[2] + from_below[1]).astype(jnp.bfloat16)
    downward = (near[0] + from_above[0]).astype(jnp.bfloat16)
    return (
        near[1]
        + from_below[0]
        + from_above[1]
        + shifter(upward, 1).astype(jnp.float32)
        + shifter(downward, -1).astype(jnp.float32)
    )


def exchange(block, axis, bit):
    count = lax.axis_size(axis)
    return lax.ppermute(block, axis, [(i, i ^ bit) for i in range(count)])


def halving(acc, axis):
    here = lax.axis_index(axis)
    count = lax.axis_size(axis)
    levels = count.bit_length() - 1
    for level in range(levels):
        half = acc.shape[0] // 2
        mine = (here >> level) % 2
        keep = lax.dynamic_slice_in_dim(acc, mine * half, half, 0)
        send = lax.dynamic_slice_in_dim(acc, (1 - mine) * half, half, 0)
        acc = keep + exchange(send.astype(jnp.bfloat16), axis, 1 << level).astype(jnp.float32)
    return acc[0]


def doubling(acc, axis):
    here = lax.axis_index(axis)
    count = lax.axis_size(axis)
    levels = count.bit_length() - 1
    acc = acc[None]
    for level in range(levels - 1, -1, -1):
        theirs = exchange(acc, axis, 1 << level)
        first = (here >> level) % 2 == 0
        acc = jnp.concatenate(
            [jnp.where(first, acc, theirs), jnp.where(first, theirs, acc)], axis=0
        )
    return acc


def on_device(queries, key_rows, values, cotangent, out_proj, conv_kernel, lengths):
    tokens = queries.shape[1]
    width_heads = queries.shape[2]
    channels = out_proj.shape[1]
    span_blocks = 2 * REACH + 1
    scale_factor = 1.0 / math.sqrt(HDIM)
    halo_width = (KW - 1) // 2
    block_index = lax.axis_index("ctx")
    length_here = lengths[0]
    query_here = queries[0]
    key_here = key_rows[0]
    value_here = values[0]
    cot_here = cotangent[0]
    frames = block_index * tokens + jnp.arange(tokens, dtype=jnp.int32)
    valid_rows = frames < length_here
    key_frames = (block_index - REACH) * tokens + jnp.arange(span_blocks * tokens, dtype=jnp.int32)
    valid_keys = (key_frames >= 0) & (key_frames < length_here)

    def kv_shift(piece_rows, offset_by):
        return passed_along(piece_rows, "ctx", offset_by)

    halo_rows = -(-halo_width // 8) * 8

    def edge_rows(rows_here):
        return rows_here.reshape(-1, width_heads)

    def edge_back(packed):
        return packed.reshape(halo_rows, channels)

    gathered, cot_low, cot_high = collect(
        jnp.stack([key_here, value_here], axis=0),
        kv_shift,
        edge_rows(cot_here[tokens - halo_rows :]),
        edge_rows(cot_here[:halo_rows]),
    )
    cot_wide = jnp.concatenate([edge_back(cot_low), cot_here, edge_back(cot_high)], axis=0)
    kv_rows = span_blocks * tokens
    key_all = jnp.concatenate([block[0] for block in gathered], axis=0)
    value_all = jnp.concatenate([block[1] for block in gathered], axis=0)
    head_mask = (
        jnp.arange(HEADS, dtype=jnp.int32)[:, None, None]
        == (jnp.arange(width_heads, dtype=jnp.int32) // HDIM)[None, None, :]
    )

    def spread(rows):
        return jnp.where(head_mask, rows[None], jnp.zeros((), rows.dtype)).reshape(
            HEADS * tokens, width_heads
        )

    def own_heads(stacked_rows):
        picked = jnp.where(head_mask, stacked_rows.reshape(HEADS, tokens, width_heads), 0.0)
        return jnp.sum(picked, axis=0)

    def contract(lhs, rhs, lhs_dim, rhs_dim):
        return lax.dot_general(
            lhs, rhs, (((lhs_dim,), (rhs_dim,)), ((), ())), preferred_element_type=jnp.float32
        )

    query_spread = spread(query_here)
    scores = contract(query_spread, key_all, 1, 1) * scale_factor
    scores = jnp.where(valid_keys[None, :], scores, -jnp.inf)
    row_max = jnp.max(scores, axis=1, keepdims=True)
    row_total = jnp.sum(jnp.exp(scores - row_max), axis=1, keepdims=True)
    log_total = row_max + jnp.log(row_total)
    weights = jnp.exp(scores - log_total).astype(jnp.bfloat16)
    attended = own_heads(contract(weights, value_all, 1, 0)).astype(jnp.bfloat16)
    hidden = jnp.dot(attended, out_proj, preferred_element_type=jnp.float32)
    masked = jnp.where(valid_rows[:, None], hidden, 0.0).astype(jnp.bfloat16)

    wide_rows = tokens + 2 * halo_rows
    edge = -(-2 * halo_width // 8) * 8
    lead = edge - halo_rows - halo_width
    padded_m = padded(masked, (("ctx", 0),), edge)
    conv_out = jnp.zeros((wide_rows, channels), jnp.float32)
    for tap_index in range(KW):
        conv_out = conv_out + conv_kernel[tap_index] * padded_m[lead + tap_index : lead + tap_index + wide_rows]
    sigmoid_c = jax.nn.sigmoid(conv_out)
    grad_conv = (
        cot_wide.astype(jnp.float32) * (sigmoid_c + conv_out * sigmoid_c * (1.0 - sigmoid_c))
    ).astype(jnp.bfloat16)
    grad_masked = jnp.zeros((tokens, channels), jnp.float32)
    for tap_index in range(KW):
        start_row = halo_rows + halo_width - tap_index
        grad_masked = (
            grad_masked + conv_kernel[tap_index] * grad_conv[start_row : start_row + tokens]
        )
    kernel_local = lax.conv_general_dilated(
        padded_m[None, edge - halo_rows : edge + tokens + halo_rows],
        grad_conv[halo_rows : halo_rows + tokens, None, :],
        window_strides=(1,),
        padding="VALID",
        dimension_numbers=("NWC", "WIO", "NWC"),
        feature_group_count=channels,
        preferred_element_type=jnp.float32,
    )[0, halo_rows - halo_width : halo_rows - halo_width + KW]
    grad_hidden = (
        cot_here.astype(jnp.float32) + jnp.where(valid_rows[:, None], grad_masked, 0.0)
    ).astype(jnp.bfloat16)
    proj_local = lax.dot_general(
        attended, grad_hidden, (((0,), (0,)), ((), ())), preferred_element_type=jnp.float32
    )
    ctx_count = lax.axis_size("ctx")
    dp_count = lax.axis_size("dp")
    members = ctx_count * dp_count
    proj_rows = proj_local.shape[0] // members
    kernel_rows = -(-KW // (members * 8)) * 8
    kernel_padded = jnp.pad(kernel_local, ((0, kernel_rows * members - KW), (0, 0)))
    stacked = jnp.concatenate(
        [
            proj_local.reshape(dp_count, ctx_count, proj_rows, channels),
            kernel_padded.reshape(dp_count, ctx_count, kernel_rows, channels),
        ],
        axis=2,
    )
    summed = halving(halving(stacked, "dp"), "ctx").astype(jnp.bfloat16)
    grad_attended = lax.dot_general(
        grad_hidden, out_proj, (((1,), (1,)), ((), ())), preferred_element_type=jnp.float32
    ).astype(jnp.bfloat16)
    delta_rows = jnp.sum(
        (grad_attended.astype(jnp.float32) * attended.astype(jnp.float32)).reshape(
            tokens, HEADS, HDIM
        ),
        axis=2,
    )
    grad_spread = spread(grad_attended)
    grad_weights = contract(grad_spread, value_all, 1, 1)
    grad_logits = (
        weights.astype(jnp.float32) * (grad_weights - delta_rows.T.reshape(HEADS * tokens, 1))
    ).astype(jnp.bfloat16)
    grad_query = (own_heads(contract(grad_logits, key_all, 1, 0)) * scale_factor).astype(
        jnp.bfloat16
    )
    grad_key_all = contract(grad_logits, query_spread, 0, 0) * scale_factor
    grad_value_all = contract(weights, grad_spread, 0, 0)
    key_blocks = grad_key_all.reshape(span_blocks, tokens, width_heads)
    value_blocks = grad_value_all.reshape(span_blocks, tokens, width_heads)
    narrow = jnp.stack([key_blocks, value_blocks], axis=1).astype(jnp.bfloat16)
    near = jnp.stack(
        [key_blocks[REACH - 1 : REACH + 2], value_blocks[REACH - 1 : REACH + 2]], axis=1
    )

    def grad_shift(piece_rows, offset_by):
        return passed_along(piece_rows, "ctx", offset_by)

    gathered = doubling(doubling(summed, "ctx"), "dp")
    proj_sum = gathered[:, :, :proj_rows].reshape(members * proj_rows, channels)
    kernel_sum = (
        gathered[:, :, proj_rows:].astype(jnp.float32).reshape(members * kernel_rows, channels)[:KW]
    )
    own_grads = give_back(near, narrow, grad_shift)
    grad_key = own_grads[0].astype(jnp.bfloat16)
    grad_value = own_grads[1].astype(jnp.bfloat16)
    return (
        grad_query[None],
        grad_key[None],
        grad_value[None],
        proj_sum,
        kernel_sum,
    )


def solution(mesh):
    return jax.shard_map(
        on_device,
        mesh=mesh,
        in_specs=(
            P(("group", "dp"), "ctx", None),
            P(("group", "dp"), "ctx", None),
            P(("group", "dp"), "ctx", None),
            P(("group", "dp"), "ctx", None),
            P(),
            P(),
            P(("group", "dp")),
        ),
        out_specs=(
            P(("group", "dp"), "ctx", None),
            P(("group", "dp"), "ctx", None),
            P(("group", "dp"), "ctx", None),
            P("group", None),
            P("group", None),
        ),
        check_vma=False,
    )
```
